256 devices in a mesh: gx: 64 (over y, x, z_lo, core), gy: 4 (over z_hi).
Axes of the slice: x: 4, y: 4, z: 8 (z_hi: 4, z_lo: 2; z = z_hi * 2 + z_lo), core: 2. Of those that a mesh axis runs over, the one named last changes fastest.
Arguments:
- state: float32 [4, 4, 512, 8192], P(None, None, 'gx', 'gy'), may hold values from -6 to 6
- start: float32 [4, 4, 512, 8192], P(None, None, 'gx', 'gy'), may hold values from -6 to 6
- eddy: float32 [4, 512, 8192], P(None, 'gx', 'gy'), may hold values from 0.05 to 0.5
- solid: int32 [4, 512, 8192], P(None, 'gx', 'gy'), may hold values 0 or 1
- facet_wall: float32 [4, 524288], P(None, ('gx', 'gy')), may hold values from -6 to 6
- facet_dist: float32 [524288], P(('gx', 'gy')), may hold values from 0.1 to 1
- facet_area: float32 [524288], P(('gx', 'gy')), may hold values from 0.1 to 1
- facet_owner: int32 [524288, 1], P(('gx', 'gy')), may hold values from 0 to 63; in each aligned block of 2048 rows (0 to 2047, 2048 to 4095, ...) at most 64 rows name the same one
- facet_cell: int32 [524288], P(('gx', 'gy')), may hold values from 0 to 65535
Outputs:
- new_state: float32 [4, 4, 512, 8192], P(None, None, 'gx', 'gy')
- facet_flux: float32 [4, 524288], P(None, ('gx', 'gy'))
The draws below stay inside these ranges and needn't reach their ends.
Inputs may be any that keep to these rules, and one draw needn't show every extreme that they name: `facet_owner`: among the 2048 facets of one device at most 64 share one owner, and that many do in some devices.
All inputs are finite; a program needn't handle non-finite values. No bound on the sum of `solid` on one device may be relied on, other than what follows from the above.
Results may differ from the reference program's by a relative error of at most 0.0003.
Values sent between devices are 32-bit elements; how exact they have to be, the bound alone decides.
No kernel may reach another device: no remote copies, remote signals or barrier semaphores. Data moves between devices by JAX's collectives and lax.ppermute only.
A program may use at most 64 MiB of HBM per device.

```python
import math
import jax
import jax.numpy as jnp
import numpy as np

CX = 8
CY = 2048
NZ = 4
FAC_DEV = 2048
CAP = 64
NX = 512
NY = 8192
FACETS = 524288
N_GX = 64
N_GY = 4


def touch_ends(values, stream_key, smallest, top_value):
    longest = values.shape.index(max(values.shape))
    spots = []
    for shift in (0, 1):
        where = [jax.random.randint(jax.random.fold_in(stream_key, axis), (), 0, length) for axis, length in enumerate(values.shape)]
        where[longest] = (where[longest] + shift) % values.shape[longest]
        spots.append(tuple(where))
    return values.at[spots[0]].set(smallest).at[spots[1]].set(top_value)


def steps_of(stream_key, dims, pieces, smallest, largest):
    level = 1.0
    for dim, parts in pieces:
        steps = jax.random.uniform(jax.random.fold_in(jax.random.fold_in(stream_key, 6), dim), (parts,), jnp.float32, smallest / len(pieces), largest / len(pieces))
        level = level * jnp.repeat(jnp.exp(steps), dims[dim] // parts).reshape((-1,) + (1,) * (len(dims) - 1 - dim))
    return level


def shared_out(key, own, number, rows, number_of, top, bound, lean):
    sequence = jax.random.permutation(key, number_of)
    packed, common = load_shares(number_of, rows * top, bound, lean, True), load_shares(number_of, rows * top, bound, lean, False)
    places = jnp.arange(number_of)

    def named(sizes, turn):
        used = int((sizes > 0).sum())
        fixed = max(1, used // 4)
        passed = fixed + (places - fixed + turn * (used - fixed)) % max(1, number_of - fixed)
        return jnp.zeros((number_of,), jnp.int32).at[sequence[jnp.where(places < fixed, places, passed)]].set(jnp.asarray(sizes, jnp.int32))

    sizes = jnp.where(number % 4 == 0, named(packed, number // 4), named(common, number - number // 4 - 1))
    mixed = jax.random.permutation(jax.random.fold_in(own, 3), number_of)
    donor, receiver = mixed[0:number_of // 2 * 2:2], mixed[1:number_of // 2 * 2:2]
    margin = jnp.minimum(sizes[donor] - 1, bound - sizes[receiver]) // 2
    margin = jnp.where((donor == sequence[0]) | (receiver == sequence[0]) | (sizes[receiver] == 0), 0, jnp.maximum(margin, 0))
    passed = jax.random.randint(jax.random.fold_in(own, 4), (number_of // 2,), 0, 1 << 20) % (margin + 1)
    sizes = sizes.at[donor].add(-passed).at[receiver].add(passed)
    labels = jnp.searchsorted(jnp.cumsum(sizes), jnp.arange(rows * top), side="right").astype(jnp.int32)
    grid = labels.reshape(top, rows).T
    grid = grid[jax.random.permutation(jax.random.fold_in(own, 1), rows)]
    turn = jax.random.randint(jax.random.fold_in(own, 2), (rows, 1), 0, top)
    return jnp.take_along_axis(grid, (jnp.arange(top)[None, :] + turn) % top, axis=1)


def load_shares(amount, total, limit, lean, full):
    weights = [(1 << 20) // math.isqrt(grade ** lean) + 1 for grade in range(1, amount + 1)]
    largest = limit if full else min(limit, max(-(-total // amount), total * weights[0] // sum(weights)))
    least = 1 if total - largest >= amount - 1 else 0
    given, rest = [largest] + [least] * (amount - 1), total - largest - least * (amount - 1)
    while rest > 0:
        movable = [i for i in range(1, amount) if given[i] < largest] or [i for i in range(1, amount) if given[i] < limit]
        whole, budget = sum([weights[i] for i in movable]), rest
        for i in movable:
            more = min(limit - given[i], max(1, budget * weights[i] // whole), rest)
            given[i] = given[i] + more
            rest = rest - more
    return np.array(given)


def scatter_about(key, dims, deviation, reach, shards=(), kind=jnp.bfloat16):
    entries = deviation * jax.random.normal(key, dims, jnp.float32)
    if shards:
        entries = entries * steps_of(key, dims, shards, -0.22, 0.18)
    return jnp.clip(entries, -reach, reach).astype(kind)


def setup_inputs(seed: int = 0) -> dict:
    keys = jax.random.split(jax.random.key(seed), 10)
    state = scatter_about(keys[0], (4, NZ, NX, NY), 1.0, 6.0, ((2, 64), (3, 4)), jnp.float32)
    start = scatter_about(keys[1], (4, NZ, NX, NY), 1.0, 6.0, ((2, 64), (3, 4)), jnp.float32)
    eddy = jnp.clip(jnp.exp(math.log(0.5) - 2.3025851 * jax.random.uniform(keys[2], (NZ, NX, NY), jnp.float32) ** steps_of(keys[2], (NZ, NX, NY), ((1, 64), (2, 4)), -0.2, 0.2)), 0.05, 0.5)
    solid = touch_ends((jax.random.randint(keys[3], (NZ, NX, NY), 0, 8) < 1).astype(jnp.int32), jax.random.fold_in(keys[3], 1), 0, 1)
    facet_wall = scatter_about(keys[4], (4, FACETS), 1.0, 6.0, ((1, 256),), jnp.float32)
    facet_dist = jnp.clip(jnp.exp(math.log(1.0) - 2.3025851 * jax.random.uniform(keys[5], (FACETS,), jnp.float32) ** steps_of(keys[5], (FACETS,), ((0, 256),), -0.2, 0.2)), 0.1, 1.0)
    facet_area = jnp.clip(jnp.exp(math.log(1.0) - 2.3025851 * jax.random.uniform(keys[6], (FACETS,), jnp.float32) ** steps_of(keys[6], (FACETS,), ((0, 256),), -0.2, 0.2)), 0.1, 1.0)
    facet_owner_keys = jax.random.split(jax.random.fold_in(keys[7], 1), FACETS // FAC_DEV)
    facet_owner_turns = jax.random.permutation(jax.random.fold_in(keys[7], 3), FACETS // FAC_DEV)
    facet_owner = jax.vmap(lambda own, number: shared_out(jax.random.fold_in(keys[7], 2), own, number, FAC_DEV, N_GX, 1, CAP, 2))(facet_owner_keys, facet_owner_turns).reshape((FACETS, 1))
    facet_cell = touch_ends(jax.random.randint(keys[8], (FACETS,), 0, NZ * CX * CY), jax.random.fold_in(keys[8], 1), 0, (NZ * CX * CY) - 1).astype(jnp.int32)
    return {"state": state, "start": start, "eddy": eddy, "solid": solid, "facet_wall": facet_wall, "facet_dist": facet_dist, "facet_area": facet_area, "facet_owner": facet_owner, "facet_cell": facet_cell}


dt_step = 0.2


def upwind_derivative(shifted, velocity):
    forward = (-2.0 * shifted(-3) + 15.0 * shifted(-2) - 60.0 * shifted(-1) + 20.0 * shifted(0) + 30.0 * shifted(1) - 3.0 * shifted(2)) / 60.0
    backward = (3.0 * shifted(-2) - 30.0 * shifted(-1) - 20.0 * shifted(0) + 60.0 * shifted(1) - 15.0 * shifted(2) + 2.0 * shifted(3)) / 60.0
    return jnp.where(velocity > 0, forward, backward)


def vertical_terms(fields, eddy):
    lower = jnp.concatenate([fields[:, :1], fields[:, :-1]], axis=1)
    upper = jnp.concatenate([fields[:, 1:], fields[:, -1:]], axis=1)
    derz = (upper - lower) * 0.5
    face_eddy = 0.5 * (eddy[:-1] + eddy[1:])
    no_face = jnp.zeros_like(eddy[:1])
    eddy_up = jnp.concatenate([face_eddy, no_face], axis=0)
    eddy_down = jnp.concatenate([no_face, face_eddy], axis=0)
    zdiffuse = eddy_up * (upper - fields) - eddy_down * (fields - lower)
    return derz, zdiffuse


def tendency(field_x, field_y, eddy_x, eddy_y, fields, eddy, forcing, solid):
    derx = upwind_derivative(field_x, fields[0])
    dery = upwind_derivative(field_y, fields[1])
    derz, zdiffuse = vertical_terms(fields, eddy)
    advect = fields[0] * derx + fields[1] * dery + fields[2] * derz
    east_eddy = 0.5 * (eddy + eddy_x(1))
    west_eddy = 0.5 * (eddy_x(-1) + eddy)
    north_eddy = 0.5 * (eddy + eddy_y(1))
    south_eddy = 0.5 * (eddy_y(-1) + eddy)
    diff_x = east_eddy * (field_x(1) - fields) - west_eddy * (fields - field_x(-1))
    diff_y = north_eddy * (field_y(1) - fields) - south_eddy * (fields - field_y(-1))
    diffuse = (diff_x + diff_y) + zdiffuse
    return ((diffuse - advect) - forcing) * (1.0 - solid.astype(jnp.float32))


def reference(state, start, eddy, solid, facet_wall, facet_dist, facet_area, facet_owner, facet_cell):
    def field_x(offset):
        return jnp.roll(state, -offset, axis=2)

    def field_y(offset):
        return jnp.roll(state, -offset, axis=3)

    def eddy_x(offset):
        return jnp.roll(eddy, -offset, axis=1)

    def eddy_y(offset):
        return jnp.roll(eddy, -offset, axis=2)

    device_of = jnp.arange(FACETS, dtype=jnp.int32) // FAC_DEV
    row_gy = device_of % N_GY
    owner_gx = facet_owner[:, 0]
    level = facet_cell // (CX * CY)
    local_x = (facet_cell // CY) % CX
    local_y = facet_cell % CY
    flat_cell = (level * NX + owner_gx * CX + local_x) * NY + row_gy * CY + local_y
    cell_values = state.reshape(4, -1)[:, flat_cell]
    facet_flux = facet_area * (cell_values - facet_wall) / facet_dist
    forcing = jnp.zeros((4, NZ * NX * NY), jnp.float32).at[:, flat_cell].add(facet_flux).reshape(state.shape)
    change = tendency(field_x, field_y, eddy_x, eddy_y, state, eddy, forcing, solid)
    new_state = start + dt_step * change
    return new_state, facet_flux
```

```python
import math

import jax
import jax.numpy as jnp
from jax import lax
from jax.experimental import pallas as pl
from jax.experimental.pallas import tpu as pltpu
from jax.sharding import PartitionSpec as P

dt_step = 0.2
exact = lax.Precision.HIGHEST


def padded(shard, sides, width):
    for axis, dim in sides:
        peers, length = (lax.axis_size(axis), shard.shape[dim])
        up = [(i, (i + 1) % peers) for i in range(peers)]
        down = [(j, i) for i, j in up]
        last = lax.slice_in_dim(shard, length - width, length, axis=dim)
        leading = lax.slice_in_dim(shard, 0, width, axis=dim)
        before = lax.ppermute(last, axis, up)
        after = lax.ppermute(leading, axis, down)
        shard = jnp.concatenate([before, shard, after], axis=dim)
    return shard


def upwind_derivative(shifted, velocity):
    forward = (
        -2.0 * shifted(-3)
        + 15.0 * shifted(-2)
        - 60.0 * shifted(-1)
        + 20.0 * shifted(0)
        + 30.0 * shifted(1)
        - 3.0 * shifted(2)
    ) / 60.0
    backward = (
        3.0 * shifted(-2)
        - 30.0 * shifted(-1)
        - 20.0 * shifted(0)
        + 60.0 * shifted(1)
        - 15.0 * shifted(2)
        + 2.0 * shifted(3)
    ) / 60.0
    return jnp.where(velocity > 0, forward, backward)


def vertical_terms(fields, eddy):
    lower = jnp.concatenate([fields[:, :1], fields[:, :-1]], axis=1)
    upper = jnp.concatenate([fields[:, 1:], fields[:, -1:]], axis=1)
    derz = (upper - lower) * 0.5
    face_eddy = 0.5 * (eddy[:-1] + eddy[1:])
    no_face = jnp.zeros_like(eddy[:1])
    eddy_up = jnp.concatenate([face_eddy, no_face], axis=0)
    eddy_down = jnp.concatenate([no_face, face_eddy], axis=0)
    zdiffuse = eddy_up * (upper - fields) - eddy_down * (fields - lower)
    return (derz, zdiffuse)


def tendency(field_x, field_y, eddy_x, eddy_y, fields, eddy, forcing, solid):
    derx = upwind_derivative(field_x, fields[0])
    dery = upwind_derivative(field_y, fields[1])
    derz, zdiffuse = vertical_terms(fields, eddy)
    advect = fields[0] * derx + fields[1] * dery + fields[2] * derz
    east_eddy = 0.5 * (eddy + eddy_x(1))
    west_eddy = 0.5 * (eddy_x(-1) + eddy)
    north_eddy = 0.5 * (eddy + eddy_y(1))
    south_eddy = 0.5 * (eddy_y(-1) + eddy)
    diff_x = east_eddy * (field_x(1) - fields) - west_eddy * (fields - field_x(-1))
    diff_y = north_eddy * (field_y(1) - fields) - south_eddy * (fields - field_y(-1))
    diffuse = diff_x + diff_y + zdiffuse
    return (diffuse - advect - forcing) * (1.0 - solid.astype(jnp.float32))


def _pieces(x, n):
    out = []
    rest = x
    for _ in range(n):
        p = rest.astype(jnp.bfloat16)
        out.append(p)
        rest = rest - p.astype(jnp.float32)
    return out


def owner_kernel(x_ref, cell_ref, wall_ref, area_ref, dist_ref, forcing_ref, flux_ref, pieces_ref):
    rows, cols = x_ref.shape
    fields = wall_ref.shape[0]
    per_field = rows // fields
    block = cell_ref.shape[1]

    @pl.when(pl.program_id(0) == 0)
    def _():
        parts = _pieces(x_ref[...], 3)
        for i, p in enumerate(parts):
            pieces_ref[i * rows:(i + 1) * rows, :] = p
        forcing_ref[...] = jnp.zeros_like(forcing_ref)

    cell = cell_ref[...]
    col = cell % cols
    row = cell // cols
    hot = (lax.broadcasted_iota(jnp.int32, (cols, block), 0) == col).astype(jnp.bfloat16)
    picked = jnp.dot(pieces_ref[...], hot, preferred_element_type=jnp.float32)
    value = (picked[0:rows] + picked[rows:2 * rows]) + picked[2 * rows:3 * rows]
    pick_row = lax.broadcasted_iota(jnp.int32, (per_field, block), 0) == row
    gathered = jnp.concatenate(
        [jnp.sum(jnp.where(pick_row, value[f * per_field:(f + 1) * per_field], 0.0), axis=0, keepdims=True)
         for f in range(fields)], axis=0)
    flux = area_ref[...] * (gathered - wall_ref[...]) / dist_ref[...]
    flux_ref[...] = flux
    spread = jnp.concatenate(
        [jnp.where(pick_row, flux[f:f + 1], 0.0) for f in range(fields)], axis=0)
    w_hi, w_lo = _pieces(spread, 2)
    w = jnp.concatenate([w_hi, w_lo], axis=0)
    added = lax.dot_general(w, hot, (((1,), (1,)), ((), ())), preferred_element_type=jnp.float32)
    forcing_ref[...] += added[0:rows] + added[rows:2 * rows]


def owner_side(x, cell, wall, area, dist, block=256):
    rows, cols = x.shape
    fields, slots = wall.shape
    steps = slots // block
    return pl.pallas_call(
        owner_kernel,
        grid=(steps,),
        in_specs=[
            pl.BlockSpec((rows, cols), lambda j: (0, 0)),
            pl.BlockSpec((1, block), lambda j: (0, j)),
            pl.BlockSpec((fields, block), lambda j: (0, j)),
            pl.BlockSpec((1, block), lambda j: (0, j)),
            pl.BlockSpec((1, block), lambda j: (0, j)),
        ],
        out_specs=[
            pl.BlockSpec((rows, cols), lambda j: (0, 0)),
            pl.BlockSpec((fields, block), lambda j: (0, j)),
        ],
        out_shape=[
            jax.ShapeDtypeStruct((rows, cols), jnp.float32),
            jax.ShapeDtypeStruct((fields, slots), jnp.float32),
        ],
        scratch_shapes=[pltpu.VMEM((3 * rows, cols), jnp.bfloat16)],
        compiler_params=pltpu.CompilerParams(dimension_semantics=("arbitrary",)),
    )(x, cell, wall, area, dist)


def local(state, start, eddy, solid, facet_wall, facet_dist, facet_area, facet_owner, facet_cell):
    levels = state.shape[1]
    cells_x = state.shape[2]
    cells_y = state.shape[3]
    packed = jnp.concatenate([state, eddy[None]], axis=0)
    padded_all = padded(packed, (("gx", 2), ("gy", 3)), 3)
    fields_pad = padded_all[:4]
    eddy_pad = padded_all[4]
    pad_width = 3

    def field_x(offset):
        return fields_pad[:, :, 3 + offset : 3 + offset + cells_x, 3 : 3 + cells_y]

    def field_y(offset):
        return fields_pad[:, :, 3 : 3 + cells_x, 3 + offset : 3 + offset + cells_y]

    def eddy_x(offset):
        return eddy_pad[
            :, pad_width + offset : pad_width + offset + cells_x, pad_width : pad_width + cells_y
        ]

    def eddy_y(offset):
        return eddy_pad[
            :, pad_width : pad_width + cells_x, pad_width + offset : pad_width + offset + cells_y
        ]

    facet_count = facet_cell.shape[0]
    owners_gx = lax.axis_size("gx")
    capacity = 2 * facet_count // owners_gx
    slots = owners_gx * capacity
    owner_gx = facet_owner[:, 0]
    owner_hot = (owner_gx[:, None] == jnp.arange(owners_gx, dtype=jnp.int32)[None, :]).astype(
        jnp.bfloat16
    )
    positions = jnp.arange(facet_count, dtype=jnp.int32)
    earlier = (positions[:, None] > positions[None, :]).astype(jnp.bfloat16)
    before = jnp.dot(earlier, owner_hot, preferred_element_type=jnp.float32)
    owner_float = owner_hot.astype(jnp.float32)
    slot_rank = jnp.sum(before * owner_float, axis=1)
    rank_hot = (slot_rank[:, None] == jnp.arange(capacity, dtype=jnp.float32)[None, :]).astype(
        jnp.float32
    )
    payload = jnp.concatenate(
        [facet_wall, facet_dist[None], facet_area[None], facet_cell[None].astype(jnp.float32)],
        axis=0,
    )
    spread = payload[:, None, :] * owner_float.T[None]
    outgoing = jnp.einsum("cof,fk->cok", spread, rank_hot, precision=exact)
    filled = jnp.dot(owner_float.T, rank_hot, precision=exact)
    unit_dist = (jnp.arange(7, dtype=jnp.int32) == 4).astype(jnp.float32)[:, None, None]
    outgoing = outgoing + unit_dist * (1.0 - filled)[None]
    received = lax.all_to_all(outgoing, "gx", split_axis=1, concat_axis=1, tiled=True).reshape(
        7, slots
    )
    row_count = levels * cells_x
    grid_rows = state.reshape(4 * row_count, cells_y)
    cell_index = (received[6:7] + 0.5).astype(jnp.int32)
    forcing_rows, flux_slots = owner_side(
        grid_rows, cell_index, received[:4], received[5:6], received[4:5]
    )
    forcing = forcing_rows.reshape(state.shape)
    wall_flux = flux_slots.reshape(4, owners_gx, capacity)
    returned = lax.all_to_all(wall_flux, "gx", split_axis=1, concat_axis=1, tiled=True)
    through = jnp.einsum("cok,fk->cof", returned, rank_hot, precision=exact)
    facet_flux = jnp.sum(through * owner_float.T[None], axis=1)
    change = tendency(field_x, field_y, eddy_x, eddy_y, state, eddy, forcing, solid)
    new_state = start + dt_step * change
    return (new_state, facet_flux)


def solution(mesh):
    in_specs = (
        P(None, None, "gx", "gy"),
        P(None, None, "gx", "gy"),
        P(None, "gx", "gy"),
        P(None, "gx", "gy"),
        P(None, ("gx", "gy")),
        P(("gx", "gy")),
        P(("gx", "gy")),
        P(("gx", "gy"), None),
        P(("gx", "gy")),
    )
    out_specs = (P(None, None, "gx", "gy"), P(None, ("gx", "gy")))
    return jax.shard_map(local, mesh=mesh, in_specs=in_specs, out_specs=out_specs, check_vma=False)
```

```python
import math

import jax
import jax.numpy as jnp
from jax import lax
from jax.experimental import pallas as pl
from jax.experimental.pallas import tpu as pltpu
from jax.sharding import PartitionSpec as P

dt_step = 0.2
exact = lax.Precision.HIGHEST


def _upwind(s, c):
    forward = (((((-2.0 * s(-3) + 15.0 * s(-2)) - 60.0 * s(-1)) + 20.0 * s(0)) + 30.0 * s(1)) - 3.0 * s(2))
    backward = (((((3.0 * s(-2) - 30.0 * s(-1)) - 20.0 * s(0)) + 60.0 * s(1)) - 15.0 * s(2)) + 2.0 * s(3))
    return jnp.where(c > 0, forward, backward) / 60.0


def _x_shifter(f, lo, hi):
    rows = f.shape[0]
    row = lax.broadcasted_iota(jnp.int32, f.shape, 0)
    width = lo.shape[0]
    lo_b = [jnp.broadcast_to(lo[i:i + 1], f.shape) for i in range(width)]
    hi_b = [jnp.broadcast_to(hi[i:i + 1], f.shape) for i in range(width)]
    cache = {0: f}

    def s(k):
        if k in cache:
            return cache[k]
        if k > 0:
            r = pltpu.roll(f, rows - k, 0)
            patch = hi_b[k - 1]
            for i in range(k - 2, -1, -1):
                patch = jnp.where(row == rows - k + i, hi_b[i], patch)
            out = jnp.where(row < rows - k, r, patch)
        else:
            m = -k
            r = pltpu.roll(f, m, 0)
            patch = lo_b[width - 1]
            for i in range(m - 1):
                patch = jnp.where(row == i, lo_b[width - m + i], patch)
            out = jnp.where(row >= m, r, patch)
        cache[k] = out
        return out
    return s


def _y_shifter(f, lo, hi):
    cols = f.shape[1]
    edge = lo.shape[1]
    lane = lax.broadcasted_iota(jnp.int32, lo.shape, 1)
    cache = {0: f}

    def s(k):
        if k in cache:
            return cache[k]
        if k > 0:
            r = pltpu.roll(f, cols - k, 1)
            patch = pltpu.roll(hi, edge - k, 1)
            last = jnp.where(lane >= edge - k, patch, r[:, cols - edge:])
            out = jnp.concatenate([r[:, :cols - edge], last], axis=1)
        else:
            m = -k
            r = pltpu.roll(f, m, 1)
            patch = pltpu.roll(lo, m, 1)
            first = jnp.where(lane < m, patch, r[:, :edge])
            out = jnp.concatenate([first, r[:, edge:]], axis=1)
        cache[k] = out
        return out
    return s


def stencil_kernel(sc_ref, sd_ref, su_ref, xl_ref, xh_ref, yl_ref, yh_ref, out_ref):
    level = pl.program_id(0)
    levels = pl.num_programs(0)
    fields = sc_ref.shape[0] - 1
    e = sc_ref[fields, 0]
    ed = sd_ref[fields, 0]
    eu = su_ref[fields, 0]
    up_w = jnp.where(level < levels - 1, 1.0, 0.0)
    down_w = jnp.where(level > 0, 1.0, 0.0)
    eddy_up = (0.5 * (e + eu)) * up_w
    eddy_down = (0.5 * (ed + e)) * down_w
    ex = _x_shifter(e, xl_ref[fields, 0, 2:3], xh_ref[fields, 0, 0:1])
    ey = _y_shifter(e, yl_ref[fields, 0], yh_ref[fields, 0])
    east = 0.5 * (e + ex(1))
    west = 0.5 * (ex(-1) + e)
    north = 0.5 * (e + ey(1))
    south = 0.5 * (ey(-1) + e)
    u = sc_ref[0, 0]
    v = sc_ref[1, 0]
    w = sc_ref[2, 0]
    for f in range(fields):
        fv = sc_ref[f, 0]
        lower = sd_ref[f, 0]
        upper = su_ref[f, 0]
        sx = _x_shifter(fv, xl_ref[f, 0], xh_ref[f, 0])
        sy = _y_shifter(fv, yl_ref[f, 0], yh_ref[f, 0])
        derx = _upwind(sx, u)
        dery = _upwind(sy, v)
        derz = (upper - lower) * 0.5
        zdiffuse = eddy_up * (upper - fv) - eddy_down * (fv - lower)
        advect = (u * derx + v * dery) + w * derz
        diff_x = east * (sx(1) - fv) - west * (fv - sx(-1))
        diff_y = north * (sy(1) - fv) - south * (fv - sy(-1))
        diffuse = (diff_x + diff_y) + zdiffuse
        out_ref[f, 0] = diffuse - advect


def stencil(packed, xl, xh, yl, yh):
    nf, levels, cx, cy = packed.shape
    w = xl.shape[2]
    edge = yl.shape[3]
    fields = nf - 1
    return pl.pallas_call(
        stencil_kernel,
        grid=(levels,),
        in_specs=[
            pl.BlockSpec((nf, 1, cx, cy), lambda l: (0, l, 0, 0)),
            pl.BlockSpec((nf, 1, cx, cy), lambda l: (0, jnp.maximum(l - 1, 0), 0, 0)),
            pl.BlockSpec((nf, 1, cx, cy), lambda l: (0, jnp.minimum(l + 1, levels - 1), 0, 0)),
            pl.BlockSpec((nf, 1, w, cy), lambda l: (0, l, 0, 0)),
            pl.BlockSpec((nf, 1, w, cy), lambda l: (0, l, 0, 0)),
            pl.BlockSpec((nf, 1, cx, edge), lambda l: (0, l, 0, 0)),
            pl.BlockSpec((nf, 1, cx, edge), lambda l: (0, l, 0, 0)),
        ],
        out_specs=pl.BlockSpec((fields, 1, cx, cy), lambda l: (0, l, 0, 0)),
        out_shape=jax.ShapeDtypeStruct((fields, levels, cx, cy), jnp.float32),
        compiler_params=pltpu.CompilerParams(dimension_semantics=("arbitrary",)),
        cost_estimate=pl.CostEstimate(flops=200 * fields * levels * cx * cy, transcendentals=0,
                                      bytes_accessed=4 * (4 * nf + fields) * levels * cx * cy),
    )(packed, packed, packed, xl, xh, yl, yh)


def _pieces(x, n):
    out = []
    rest = x
    for _ in range(n):
        p = rest.astype(jnp.bfloat16)
        out.append(p)
        rest = rest - p.astype(jnp.float32)
    return out


def owner_kernel(x_ref, pay_ref, forcing_ref, flux_ref, pieces_ref, iota_ref):
    rows, cols = x_ref.shape
    fields = 4
    per_field = rows // fields
    block = pay_ref.shape[1]
    sub = 256
    nsub = cols // sub

    @pl.when(pl.program_id(0) == 0)
    def _():
        parts = _pieces(x_ref[...], 3)
        for i, p in enumerate(parts):
            pieces_ref[i * rows:(i + 1) * rows, :] = p
        forcing_ref[...] = jnp.zeros_like(forcing_ref)
        iota_ref[...] = lax.broadcasted_iota(jnp.int32, (sub, block), 0).astype(jnp.bfloat16)

    pay = pay_ref[...]
    cell = (pay[6:7] + 0.5).astype(jnp.int32)
    col = cell % cols
    row = cell // cols
    hi = col // sub
    lo = (col % sub).astype(jnp.float32)
    iota = iota_ref[...]
    hots = []
    for a in range(nsub):
        sel = jnp.where(hi == a, lo, -1.0).astype(jnp.bfloat16)
        hots.append(jnp.where(iota == sel, jnp.bfloat16(1), jnp.bfloat16(0)))
    hot = jnp.concatenate(hots, axis=0)
    picked = jnp.dot(pieces_ref[...], hot, preferred_element_type=jnp.float32)
    value = (picked[0:rows] + picked[rows:2 * rows]) + picked[2 * rows:3 * rows]
    pick_row = lax.broadcasted_iota(jnp.int32, (per_field, block), 0) == row
    gathered = jnp.concatenate(
        [jnp.sum(jnp.where(pick_row, value[f * per_field:(f + 1) * per_field], 0.0), axis=0, keepdims=True)
         for f in range(fields)], axis=0)
    flux = pay[5:6] * (gathered - pay[0:4]) / pay[4:5]
    flux_ref[...] = flux
    spread = jnp.concatenate(
        [jnp.where(pick_row, flux[f:f + 1], 0.0) for f in range(fields)], axis=0)
    w = jnp.concatenate(_pieces(spread, 2), axis=0)
    added = lax.dot_general(w, hot, (((1,), (1,)), ((), ())), preferred_element_type=jnp.float32)
    forcing_ref[...] += added[0:rows] + added[rows:2 * rows]


def owner_side(x, pay, block=1024):
    rows, cols = x.shape
    slots = pay.shape[1]
    steps = slots // block
    return pl.pallas_call(
        owner_kernel,
        grid=(steps,),
        in_specs=[
            pl.BlockSpec((rows, cols), lambda j: (0, 0)),
            pl.BlockSpec((8, block), lambda j: (0, j)),
        ],
        out_specs=[
            pl.BlockSpec((rows, cols), lambda j: (0, 0)),
            pl.BlockSpec((4, block), lambda j: (0, j)),
        ],
        out_shape=[
            jax.ShapeDtypeStruct((rows, cols), jnp.float32),
            jax.ShapeDtypeStruct((4, slots), jnp.float32),
        ],
        scratch_shapes=[pltpu.VMEM((3 * rows, cols), jnp.bfloat16),
                        pltpu.VMEM((256, block), jnp.bfloat16)],
        compiler_params=pltpu.CompilerParams(dimension_semantics=("arbitrary",),
                                             vmem_limit_bytes=48 * 1024 * 1024),
        cost_estimate=pl.CostEstimate(flops=2 * (5 * rows) * cols * slots, transcendentals=0,
                                      bytes_accessed=4 * (2 * rows * cols + 12 * slots)),
    )(x, pay)


def exchange(shard, axis, dim, low, high):
    peers = lax.axis_size(axis)
    length = shard.shape[dim]
    up = [(i, (i + 1) % peers) for i in range(peers)]
    down = [(j, i) for i, j in up]
    last = lax.slice_in_dim(shard, length - low, length, axis=dim)
    leading = lax.slice_in_dim(shard, 0, high, axis=dim)
    before = lax.ppermute(last, axis, up)
    after = lax.ppermute(leading, axis, down)
    return before, after


def local(state, start, eddy, solid, facet_wall, facet_dist, facet_area, facet_owner, facet_cell):
    levels = state.shape[1]
    cells_x = state.shape[2]
    cells_y = state.shape[3]
    packed = jnp.concatenate([state, eddy[None]], axis=0)
    x_low, x_high = exchange(packed, "gx", 2, 3, 3)
    y_low, y_high = exchange(packed, "gy", 3, 128, 128)

    facet_count = facet_cell.shape[0]
    owners_gx = lax.axis_size("gx")
    capacity = 2 * facet_count // owners_gx
    slots = owners_gx * capacity
    owner_gx = facet_owner[:, 0]
    owner_hot = (owner_gx[:, None] == jnp.arange(owners_gx, dtype=jnp.int32)[None, :]).astype(
        jnp.bfloat16
    )
    positions = jnp.arange(facet_count, dtype=jnp.int32)
    earlier = (positions[:, None] > positions[None, :]).astype(jnp.bfloat16)
    before = jnp.dot(earlier, owner_hot, preferred_element_type=jnp.float32)
    owner_float = owner_hot.astype(jnp.float32)
    slot_rank = jnp.sum(before * owner_float, axis=1)
    rank_hot = (slot_rank[:, None] == jnp.arange(capacity, dtype=jnp.float32)[None, :]).astype(
        jnp.float32
    )
    payload = jnp.concatenate(
        [facet_wall, facet_dist[None], facet_area[None], facet_cell[None].astype(jnp.float32)],
        axis=0,
    )
    spread = payload[:, None, :] * owner_float.T[None]
    outgoing = jnp.einsum("cof,fk->cok", spread, rank_hot, precision=exact)
    filled = jnp.dot(owner_float.T, rank_hot, precision=exact)
    unit_dist = (jnp.arange(7, dtype=jnp.int32) == 4).astype(jnp.float32)[:, None, None]
    outgoing = outgoing + unit_dist * (1.0 - filled)[None]
    received = lax.all_to_all(outgoing, "gx", split_axis=1, concat_axis=1, tiled=True).reshape(
        7, slots
    )
    tend = stencil(packed, x_low, x_high, y_low, y_high)
    pay = jnp.concatenate([received, jnp.zeros((1, slots), jnp.float32)], axis=0)
    forcing_rows, flux_slots = owner_side(state.reshape(4 * levels * cells_x, cells_y), pay)
    forcing = forcing_rows.reshape(state.shape)
    wall_flux = flux_slots.reshape(4, owners_gx, capacity)
    returned = lax.all_to_all(wall_flux, "gx", split_axis=1, concat_axis=1, tiled=True)
    through = jnp.einsum("cok,fk->cof", returned, rank_hot, precision=exact)
    facet_flux = jnp.sum(through * owner_float.T[None], axis=1)
    change = (tend - forcing) * (1.0 - solid.astype(jnp.float32))
    new_state = start + dt_step * change
    return (new_state, facet_flux)


def solution(mesh):
    in_specs = (
        P(None, None, "gx", "gy"),
        P(None, None, "gx", "gy"),
        P(None, "gx", "gy"),
        P(None, "gx", "gy"),
        P(None, ("gx", "gy")),
        P(("gx", "gy")),
        P(("gx", "gy")),
        P(("gx", "gy"), None),
        P(("gx", "gy")),
    )
    out_specs = (P(None, None, "gx", "gy"), P(None, ("gx", "gy")))
    return jax.shard_map(local, mesh=mesh, in_specs=in_specs, out_specs=out_specs, check_vma=False)
```

```python
import math

import jax
import jax.numpy as jnp
from jax import lax
from jax.experimental import pallas as pl
from jax.experimental.pallas import tpu as pltpu
from jax.sharding import PartitionSpec as P

dt_step = 0.2
exact = lax.Precision.HIGHEST


def _upwind(s, c):
    forward = (((((-2.0 * s(-3) + 15.0 * s(-2)) - 60.0 * s(-1)) + 20.0 * s(0)) + 30.0 * s(1)) - 3.0 * s(2))
    backward = (((((3.0 * s(-2) - 30.0 * s(-1)) - 20.0 * s(0)) + 60.0 * s(1)) - 15.0 * s(2)) + 2.0 * s(3))
    return jnp.where(c > 0, forward, backward) / 60.0


def _x_shifter(f, lo_rows, hi_rows):
    rows = f.shape[0]
    row = lax.broadcasted_iota(jnp.int32, f.shape, 0)
    width = len(lo_rows)
    lo_b = [jnp.broadcast_to(r, f.shape) for r in lo_rows]
    hi_b = [jnp.broadcast_to(r, f.shape) for r in hi_rows]
    cache = {0: f}

    def s(k):
        if k in cache:
            return cache[k]
        if k > 0:
            r = pltpu.roll(f, rows - k, 0)
            patch = hi_b[k - 1]
            for i in range(k - 2, -1, -1):
                patch = jnp.where(row == rows - k + i, hi_b[i], patch)
            out = jnp.where(row < rows - k, r, patch)
        else:
            m = -k
            r = pltpu.roll(f, m, 0)
            patch = lo_b[width - 1]
            for i in range(m - 1):
                patch = jnp.where(row == i, lo_b[width - m + i], patch)
            out = jnp.where(row >= m, r, patch)
        cache[k] = out
        return out
    return s


def _y_shifter(f, lo, hi):
    cols = f.shape[1]
    edge = lo.shape[1]
    lane = lax.broadcasted_iota(jnp.int32, lo.shape, 1)
    cache = {0: f}

    def s(k):
        if k in cache:
            return cache[k]
        if k > 0:
            r = pltpu.roll(f, cols - k, 1)
            patch = pltpu.roll(hi, edge - k, 1)
            last = jnp.where(lane >= edge - k, patch, r[:, cols - edge:])
            out = jnp.concatenate([r[:, :cols - edge], last], axis=1)
        else:
            m = -k
            r = pltpu.roll(f, m, 1)
            patch = pltpu.roll(lo, m, 1)
            first = jnp.where(lane < m, patch, r[:, :edge])
            out = jnp.concatenate([first, r[:, edge:]], axis=1)
        cache[k] = out
        return out
    return s


def stencil_kernel(sc_ref, sd_ref, su_ref, xl_ref, xh_ref, yl_ref, yh_ref, out_ref):
    level = pl.program_id(0)
    levels = pl.num_programs(0)
    fields = sc_ref.shape[0] - 1
    e = sc_ref[fields, 0]
    ed = sd_ref[fields, 0]
    eu = su_ref[fields, 0]
    up_w = jnp.where(level < levels - 1, 1.0, 0.0)
    down_w = jnp.where(level > 0, 1.0, 0.0)
    eddy_up = (0.5 * (e + eu)) * up_w
    eddy_down = (0.5 * (ed + e)) * down_w
    width = xl_ref.shape[1] // (fields + 1)
    ex = _x_shifter(e, [xl_ref[0, pl.ds(fields * width + width - 1, 1), :]], [xh_ref[0, pl.ds(fields * width, 1), :]])
    ey = _y_shifter(e, yl_ref[fields, 0], yh_ref[fields, 0])
    east = 0.5 * (e + ex(1))
    west = 0.5 * (ex(-1) + e)
    north = 0.5 * (e + ey(1))
    south = 0.5 * (ey(-1) + e)
    u = sc_ref[0, 0]
    v = sc_ref[1, 0]
    w = sc_ref[2, 0]
    for f in range(fields):
        fv = sc_ref[f, 0]
        lower = sd_ref[f, 0]
        upper = su_ref[f, 0]
        sx = _x_shifter(fv, [xl_ref[0, pl.ds(f * width + i, 1), :] for i in range(width)],
                        [xh_ref[0, pl.ds(f * width + i, 1), :] for i in range(width)])
        sy = _y_shifter(fv, yl_ref[f, 0], yh_ref[f, 0])
        derx = _upwind(sx, u)
        dery = _upwind(sy, v)
        derz = (upper - lower) * 0.5
        zdiffuse = eddy_up * (upper - fv) - eddy_down * (fv - lower)
        advect = (u * derx + v * dery) + w * derz
        diff_x = east * (sx(1) - fv) - west * (fv - sx(-1))
        diff_y = north * (sy(1) - fv) - south * (fv - sy(-1))
        diffuse = (diff_x + diff_y) + zdiffuse
        out_ref[f, 0] = diffuse - advect


def stencil(packed, xl, xh, yl, yh):
    nf, levels, cx, cy = packed.shape
    w = xl.shape[1]
    edge = yl.shape[3]
    fields = nf - 1
    return pl.pallas_call(
        stencil_kernel,
        grid=(levels,),
        in_specs=[
            pl.BlockSpec((nf, 1, cx, cy), lambda l: (0, l, 0, 0)),
            pl.BlockSpec((nf, 1, cx, cy), lambda l: (0, jnp.maximum(l - 1, 0), 0, 0)),
            pl.BlockSpec((nf, 1, cx, cy), lambda l: (0, jnp.minimum(l + 1, levels - 1), 0, 0)),
            pl.BlockSpec((1, w, cy), lambda l: (l, 0, 0)),
            pl.BlockSpec((1, w, cy), lambda l: (l, 0, 0)),
            pl.BlockSpec((nf, 1, cx, edge), lambda l: (0, l, 0, 0)),
            pl.BlockSpec((nf, 1, cx, edge), lambda l: (0, l, 0, 0)),
        ],
        out_specs=pl.BlockSpec((fields, 1, cx, cy), lambda l: (0, l, 0, 0)),
        out_shape=jax.ShapeDtypeStruct((fields, levels, cx, cy), jnp.float32),
        compiler_params=pltpu.CompilerParams(dimension_semantics=("arbitrary",)),
        cost_estimate=pl.CostEstimate(flops=200 * fields * levels * cx * cy, transcendentals=0,
                                      bytes_accessed=4 * (4 * nf + fields) * levels * cx * cy),
    )(packed, packed, packed, xl, xh, yl, yh)


def _pieces(x, n):
    out = []
    rest = x
    for _ in range(n):
        p = rest.astype(jnp.bfloat16)
        out.append(p)
        rest = rest - p.astype(jnp.float32)
    return out


def owner_kernel(x_ref, pay_ref, forcing_ref, flux_ref, pieces_ref, iota_ref):
    rows, cols = x_ref.shape
    fields = 4
    per_field = rows // fields
    block = pay_ref.shape[1]
    sub = 256
    nsub = cols // sub

    @pl.when(pl.program_id(0) == 0)
    def _():
        parts = _pieces(x_ref[...], 3)
        for i, p in enumerate(parts):
            pieces_ref[i * rows:(i + 1) * rows, :] = p
        forcing_ref[...] = jnp.zeros_like(forcing_ref)
        iota_ref[...] = lax.broadcasted_iota(jnp.int32, (sub, block), 0).astype(jnp.bfloat16)

    pay = pay_ref[...]
    cell = (pay[6:7] + 0.5).astype(jnp.int32)
    col = cell % cols
    row = cell // cols
    hi = col // sub
    lo = (col % sub).astype(jnp.float32)
    iota = iota_ref[...]
    hots = []
    for a in range(nsub):
        sel = jnp.where(hi == a, lo, -1.0).astype(jnp.bfloat16)
        hots.append(jnp.where(iota == sel, jnp.bfloat16(1), jnp.bfloat16(0)))
    hot = jnp.concatenate(hots, axis=0)
    picked = jnp.dot(pieces_ref[...], hot, preferred_element_type=jnp.float32)
    value = (picked[0:rows] + picked[rows:2 * rows]) + picked[2 * rows:3 * rows]
    pick_row = lax.broadcasted_iota(jnp.int32, (per_field, block), 0) == row
    gathered = jnp.concatenate(
        [jnp.sum(jnp.where(pick_row, value[f * per_field:(f + 1) * per_field], 0.0), axis=0, keepdims=True)
         for f in range(fields)], axis=0)
    flux = pay[5:6] * (gathered - pay[0:4]) / pay[4:5]
    flux_ref[...] = flux
    spread = jnp.concatenate(
        [jnp.where(pick_row, flux[f:f + 1], 0.0) for f in range(fields)], axis=0)
    w = jnp.concatenate(_pieces(spread, 2), axis=0)
    added = lax.dot_general(w, hot, (((1,), (1,)), ((), ())), preferred_element_type=jnp.float32)
    forcing_ref[...] += added[0:rows] + added[rows:2 * rows]


def owner_side(x, pay, block=1024):
    rows, cols = x.shape
    slots = pay.shape[1]
    steps = slots // block
    return pl.pallas_call(
        owner_kernel,
        grid=(steps,),
        in_specs=[
            pl.BlockSpec((rows, cols), lambda j: (0, 0)),
            pl.BlockSpec((8, block), lambda j: (0, j)),
        ],
        out_specs=[
            pl.BlockSpec((rows, cols), lambda j: (0, 0)),
            pl.BlockSpec((4, block), lambda j: (0, j)),
        ],
        out_shape=[
            jax.ShapeDtypeStruct((rows, cols), jnp.float32),
            jax.ShapeDtypeStruct((4, slots), jnp.float32),
        ],
        scratch_shapes=[pltpu.VMEM((3 * rows, cols), jnp.bfloat16),
                        pltpu.VMEM((256, block), jnp.bfloat16)],
        compiler_params=pltpu.CompilerParams(dimension_semantics=("arbitrary",),
                                             vmem_limit_bytes=48 * 1024 * 1024),
        cost_estimate=pl.CostEstimate(flops=2 * (5 * rows) * cols * slots, transcendentals=0,
                                      bytes_accessed=4 * (2 * rows * cols + 12 * slots)),
    )(x, pay)


def shift_pair(last, leading, axis):
    peers = lax.axis_size(axis)
    up = [(i, (i + 1) % peers) for i in range(peers)]
    down = [(j, i) for i, j in up]
    return lax.ppermute(last, axis, up), lax.ppermute(leading, axis, down)


def exchange(shard, axis, dim, low, high):
    peers = lax.axis_size(axis)
    length = shard.shape[dim]
    up = [(i, (i + 1) % peers) for i in range(peers)]
    down = [(j, i) for i, j in up]
    last = lax.slice_in_dim(shard, length - low, length, axis=dim)
    leading = lax.slice_in_dim(shard, 0, high, axis=dim)
    before = lax.ppermute(last, axis, up)
    after = lax.ppermute(leading, axis, down)
    return before, after


def local(state, start, eddy, solid, facet_wall, facet_dist, facet_area, facet_owner, facet_cell):
    levels = state.shape[1]
    cells_x = state.shape[2]
    cells_y = state.shape[3]
    packed = jnp.concatenate([state, eddy[None]], axis=0)
    x_rows = jnp.transpose(packed, (1, 0, 2, 3))
    x_last = x_rows[:, :, cells_x - 3:].reshape(levels, -1, cells_y)
    x_first = x_rows[:, :, :3].reshape(levels, -1, cells_y)
    x_low, x_high = shift_pair(x_last, x_first, "gx")
    y_low, y_high = exchange(packed, "gy", 3, 128, 128)

    facet_count = facet_cell.shape[0]
    owners_gx = lax.axis_size("gx")
    capacity = 2 * facet_count // owners_gx
    slots = owners_gx * capacity
    owner_gx = facet_owner[:, 0]
    owner_hot = (owner_gx[:, None] == jnp.arange(owners_gx, dtype=jnp.int32)[None, :]).astype(
        jnp.bfloat16
    )
    positions = jnp.arange(facet_count, dtype=jnp.int32)
    earlier = (positions[:, None] > positions[None, :]).astype(jnp.bfloat16)
    before = jnp.dot(earlier, owner_hot, preferred_element_type=jnp.float32)
    owner_float = owner_hot.astype(jnp.float32)
    slot_rank = jnp.sum(before * owner_float, axis=1)
    rank_hot = (slot_rank[:, None] == jnp.arange(capacity, dtype=jnp.float32)[None, :]).astype(
        jnp.float32
    )
    payload = jnp.concatenate(
        [facet_wall, facet_dist[None], facet_area[None], facet_cell[None].astype(jnp.float32)],
        axis=0,
    )
    spread = payload[:, None, :] * owner_float.T[None]
    outgoing = jnp.einsum("cof,fk->cok", spread, rank_hot, precision=exact)
    filled = jnp.dot(owner_float.T, rank_hot, precision=exact)
    unit_dist = (jnp.arange(7, dtype=jnp.int32) == 4).astype(jnp.float32)[:, None, None]
    outgoing = outgoing + unit_dist * (1.0 - filled)[None]
    x_low, x_high, y_low, y_high, outgoing = lax.optimization_barrier(
        (x_low, x_high, y_low, y_high, outgoing)
    )
    received = lax.all_to_all(outgoing, "gx", split_axis=1, concat_axis=1, tiled=True).reshape(
        7, slots
    )
    tend = stencil(packed, x_low, x_high, y_low, y_high)
    tend, received = lax.optimization_barrier((tend, received))
    pay = jnp.concatenate([received, jnp.zeros((1, slots), jnp.float32)], axis=0)
    forcing_rows, flux_slots = owner_side(state.reshape(4 * levels * cells_x, cells_y), pay)
    forcing = forcing_rows.reshape(state.shape)
    wall_flux = flux_slots.reshape(4, owners_gx, capacity)
    returned = lax.all_to_all(wall_flux, "gx", split_axis=1, concat_axis=1, tiled=True)
    change = (tend - forcing) * (1.0 - solid.astype(jnp.float32))
    new_state = start + dt_step * change
    new_state, returned = lax.optimization_barrier((new_state, returned))
    through = jnp.einsum("cok,fk->cof", returned, rank_hot, precision=exact)
    facet_flux = jnp.sum(through * owner_float.T[None], axis=1)
    return (new_state, facet_flux)


def solution(mesh):
    in_specs = (
        P(None, None, "gx", "gy"),
        P(None, None, "gx", "gy"),
        P(None, "gx", "gy"),
        P(None, "gx", "gy"),
        P(None, ("gx", "gy")),
        P(("gx", "gy")),
        P(("gx", "gy")),
        P(("gx", "gy"), None),
        P(("gx", "gy")),
    )
    out_specs = (P(None, None, "gx", "gy"), P(None, ("gx", "gy")))
    return jax.shard_map(local, mesh=mesh, in_specs=in_specs, out_specs=out_specs, check_vma=False)
```

```python
import math

import jax
import jax.numpy as jnp
from jax import lax
from jax.experimental import pallas as pl
from jax.experimental.pallas import tpu as pltpu
from jax.sharding import PartitionSpec as P

dt_step = 0.2
exact = lax.Precision.HIGHEST


def _upwind(s, c):
    forward = (((((-2.0 * s(-3) + 15.0 * s(-2)) - 60.0 * s(-1)) + 20.0 * s(0)) + 30.0 * s(1)) - 3.0 * s(2))
    backward = (((((3.0 * s(-2) - 30.0 * s(-1)) - 20.0 * s(0)) + 60.0 * s(1)) - 15.0 * s(2)) + 2.0 * s(3))
    return jnp.where(c > 0, forward, backward) / 60.0


def _x_shifter(f, lo_rows, hi_rows):
    rows = f.shape[0]
    row = lax.broadcasted_iota(jnp.int32, f.shape, 0)
    width = len(lo_rows)
    lo_b = [jnp.broadcast_to(r, f.shape) for r in lo_rows]
    hi_b = [jnp.broadcast_to(r, f.shape) for r in hi_rows]
    cache = {0: f}

    def s(k):
        if k in cache:
            return cache[k]
        if k > 0:
            r = pltpu.roll(f, rows - k, 0)
            patch = hi_b[k - 1]
            for i in range(k - 2, -1, -1):
                patch = jnp.where(row == rows - k + i, hi_b[i], patch)
            out = jnp.where(row < rows - k, r, patch)
        else:
            m = -k
            r = pltpu.roll(f, m, 0)
            patch = lo_b[width - 1]
            for i in range(m - 1):
                patch = jnp.where(row == i, lo_b[width - m + i], patch)
            out = jnp.where(row >= m, r, patch)
        cache[k] = out
        return out
    return s


def _y_shifter(f, lo, hi):
    cols = f.shape[1]
    edge = lo.shape[1]
    lane = lax.broadcasted_iota(jnp.int32, lo.shape, 1)
    cache = {0: f}

    def s(k):
        if k in cache:
            return cache[k]
        if k > 0:
            r = pltpu.roll(f, cols - k, 1)
            patch = pltpu.roll(hi, edge - k, 1)
            last = jnp.where(lane >= edge - k, patch, r[:, cols - edge:])
            out = jnp.concatenate([r[:, :cols - edge], last], axis=1)
        else:
            m = -k
            r = pltpu.roll(f, m, 1)
            patch = pltpu.roll(lo, m, 1)
            first = jnp.where(lane < m, patch, r[:, :edge])
            out = jnp.concatenate([first, r[:, edge:]], axis=1)
        cache[k] = out
        return out
    return s


def stencil_kernel(sc_ref, sd_ref, su_ref, ec_ref, ed_ref, eu_ref, xl_ref, xh_ref, yl_ref, yh_ref, out_ref):
    level = pl.program_id(0)
    levels = pl.num_programs(0)
    fields = sc_ref.shape[0]
    width = (xl_ref.shape[1] - 1) // fields
    e = ec_ref[0]
    ed = ed_ref[0]
    eu = eu_ref[0]
    up_w = jnp.where(level < levels - 1, 1.0, 0.0)
    down_w = jnp.where(level > 0, 1.0, 0.0)
    eddy_up = (0.5 * (e + eu)) * up_w
    eddy_down = (0.5 * (ed + e)) * down_w
    ex = _x_shifter(e, [xl_ref[0, pl.ds(fields * width, 1), :]], [xh_ref[0, pl.ds(fields * width, 1), :]])
    ey = _y_shifter(e, yl_ref[fields, 0], yh_ref[fields, 0])
    east = 0.5 * (e + ex(1))
    west = 0.5 * (ex(-1) + e)
    north = 0.5 * (e + ey(1))
    south = 0.5 * (ey(-1) + e)
    u = sc_ref[0, 0]
    v = sc_ref[1, 0]
    w = sc_ref[2, 0]
    for f in range(fields):
        fv = sc_ref[f, 0]
        lower = sd_ref[f, 0]
        upper = su_ref[f, 0]
        sx = _x_shifter(fv, [xl_ref[0, pl.ds(f * width + i, 1), :] for i in range(width)],
                        [xh_ref[0, pl.ds(f * width + i, 1), :] for i in range(width)])
        sy = _y_shifter(fv, yl_ref[f, 0], yh_ref[f, 0])
        derx = _upwind(sx, u)
        dery = _upwind(sy, v)
        derz = (upper - lower) * 0.5
        zdiffuse = eddy_up * (upper - fv) - eddy_down * (fv - lower)
        advect = (u * derx + v * dery) + w * derz
        diff_x = east * (sx(1) - fv) - west * (fv - sx(-1))
        diff_y = north * (sy(1) - fv) - south * (fv - sy(-1))
        diffuse = (diff_x + diff_y) + zdiffuse
        out_ref[f, 0] = diffuse - advect


def stencil(state, eddy, xl, xh, yl, yh):
    fields, levels, cx, cy = state.shape
    w = xl.shape[1]
    nf = yl.shape[0]
    edge = yl.shape[3]
    below = lambda l: jnp.maximum(l - 1, 0)
    above = lambda l: jnp.minimum(l + 1, levels - 1)
    return pl.pallas_call(
        stencil_kernel,
        grid=(levels,),
        in_specs=[
            pl.BlockSpec((fields, 1, cx, cy), lambda l: (0, l, 0, 0)),
            pl.BlockSpec((fields, 1, cx, cy), lambda l: (0, below(l), 0, 0)),
            pl.BlockSpec((fields, 1, cx, cy), lambda l: (0, above(l), 0, 0)),
            pl.BlockSpec((1, cx, cy), lambda l: (l, 0, 0)),
            pl.BlockSpec((1, cx, cy), lambda l: (below(l), 0, 0)),
            pl.BlockSpec((1, cx, cy), lambda l: (above(l), 0, 0)),
            pl.BlockSpec((1, w, cy), lambda l: (l, 0, 0)),
            pl.BlockSpec((1, w, cy), lambda l: (l, 0, 0)),
            pl.BlockSpec((nf, 1, cx, edge), lambda l: (0, l, 0, 0)),
            pl.BlockSpec((nf, 1, cx, edge), lambda l: (0, l, 0, 0)),
        ],
        out_specs=pl.BlockSpec((fields, 1, cx, cy), lambda l: (0, l, 0, 0)),
        out_shape=jax.ShapeDtypeStruct((fields, levels, cx, cy), jnp.float32),
        compiler_params=pltpu.CompilerParams(dimension_semantics=("arbitrary",)),
        cost_estimate=pl.CostEstimate(flops=200 * fields * levels * cx * cy, transcendentals=0,
                                      bytes_accessed=4 * (4 * nf + fields) * levels * cx * cy),
    )(state, state, state, eddy, eddy, eddy, xl, xh, yl, yh)


def _pieces(x, n):
    out = []
    rest = x
    for _ in range(n):
        p = rest.astype(jnp.bfloat16)
        out.append(p)
        rest = rest - p.astype(jnp.float32)
    return out


def owner_kernel(x_ref, pay_ref, forcing_ref, flux_ref, pieces_ref, iota_ref):
    rows, cols = x_ref.shape
    fields = 4
    per_field = rows // fields
    block = pay_ref.shape[1]
    sub = 256
    nsub = cols // sub

    @pl.when(pl.program_id(0) == 0)
    def _():
        parts = _pieces(x_ref[...], 2)
        for i, p in enumerate(parts):
            pieces_ref[i * rows:(i + 1) * rows, :] = p
        forcing_ref[...] = jnp.zeros_like(forcing_ref)
        iota_ref[...] = lax.broadcasted_iota(jnp.int32, (sub, block), 0).astype(jnp.bfloat16)

    pay = pay_ref[...]
    cell = (pay[6:7] + 0.5).astype(jnp.int32)
    col = cell % cols
    row = cell // cols
    hi = col // sub
    lo = (col % sub).astype(jnp.float32)
    iota = iota_ref[...]
    hots = []
    for a in range(nsub):
        sel = jnp.where(hi == a, lo, -1.0).astype(jnp.bfloat16)
        hots.append(jnp.where(iota == sel, jnp.bfloat16(1), jnp.bfloat16(0)))
    hot = jnp.concatenate(hots, axis=0)
    picked = jnp.dot(pieces_ref[...], hot, preferred_element_type=jnp.float32)
    value = picked[0:rows] + picked[rows:2 * rows]
    pick_row = lax.broadcasted_iota(jnp.int32, (per_field, block), 0) == row
    gathered = jnp.concatenate(
        [jnp.sum(jnp.where(pick_row, value[f * per_field:(f + 1) * per_field], 0.0), axis=0, keepdims=True)
         for f in range(fields)], axis=0)
    flux = pay[5:6] * (gathered - pay[0:4]) / pay[4:5]
    flux_ref[...] = flux
    spread = jnp.concatenate(
        [jnp.where(pick_row, flux[f:f + 1], 0.0) for f in range(fields)], axis=0)
    w = jnp.concatenate(_pieces(spread, 2), axis=0)
    added = lax.dot_general(w, hot, (((1,), (1,)), ((), ())), preferred_element_type=jnp.float32)
    forcing_ref[...] += added[0:rows] + added[rows:2 * rows]


def owner_side(x, pay, block=1024):
    rows, cols = x.shape
    slots = pay.shape[1]
    steps = slots // block
    return pl.pallas_call(
        owner_kernel,
        grid=(steps,),
        in_specs=[
            pl.BlockSpec((rows, cols), lambda j: (0, 0)),
            pl.BlockSpec((8, block), lambda j: (0, j)),
        ],
        out_specs=[
            pl.BlockSpec((rows, cols), lambda j: (0, 0)),
            pl.BlockSpec((4, block), lambda j: (0, j)),
        ],
        out_shape=[
            jax.ShapeDtypeStruct((rows, cols), jnp.float32),
            jax.ShapeDtypeStruct((4, slots), jnp.float32),
        ],
        scratch_shapes=[pltpu.VMEM((2 * rows, cols), jnp.bfloat16),
                        pltpu.VMEM((256, block), jnp.bfloat16)],
        compiler_params=pltpu.CompilerParams(dimension_semantics=("arbitrary",),
                                             vmem_limit_bytes=48 * 1024 * 1024),
        cost_estimate=pl.CostEstimate(flops=2 * (4 * rows) * cols * slots, transcendentals=0,
                                      bytes_accessed=4 * (2 * rows * cols + 12 * slots)),
    )(x, pay)


def shift_pair(last, leading, axis):
    peers = lax.axis_size(axis)
    up = [(i, (i + 1) % peers) for i in range(peers)]
    down = [(j, i) for i, j in up]
    return lax.ppermute(last, axis, up), lax.ppermute(leading, axis, down)


def exchange(shard, axis, dim, low, high):
    peers = lax.axis_size(axis)
    length = shard.shape[dim]
    up = [(i, (i + 1) % peers) for i in range(peers)]
    down = [(j, i) for i, j in up]
    last = lax.slice_in_dim(shard, length - low, length, axis=dim)
    leading = lax.slice_in_dim(shard, 0, high, axis=dim)
    before = lax.ppermute(last, axis, up)
    after = lax.ppermute(leading, axis, down)
    return before, after


def local(state, start, eddy, solid, facet_wall, facet_dist, facet_area, facet_owner, facet_cell):
    levels = state.shape[1]
    cells_x = state.shape[2]
    cells_y = state.shape[3]
    width = 3
    edge = 128

    def x_rows(lo, hi):
        rows = jnp.transpose(state[:, :, lo:hi], (1, 0, 2, 3)).reshape(levels, -1, cells_y)
        return jnp.concatenate([rows, eddy[:, lo:hi][:, -1:] if lo else eddy[:, 0:1]], axis=1)

    x_low, x_high = shift_pair(x_rows(cells_x - width, cells_x), x_rows(0, width), "gx")

    def y_cols(lo, hi):
        return jnp.concatenate([state[..., lo:hi], eddy[None, ..., lo:hi]], axis=0)

    y_low, y_high = shift_pair(y_cols(cells_y - edge, cells_y), y_cols(0, edge), "gy")

    facet_count = facet_cell.shape[0]
    owners_gx = lax.axis_size("gx")
    capacity = 2 * facet_count // owners_gx
    slots = owners_gx * capacity
    owner_gx = facet_owner[:, 0]
    owner_hot = (owner_gx[:, None] == jnp.arange(owners_gx, dtype=jnp.int32)[None, :]).astype(
        jnp.bfloat16
    )
    positions = jnp.arange(facet_count, dtype=jnp.int32)
    earlier = (positions[:, None] > positions[None, :]).astype(jnp.bfloat16)
    before = jnp.dot(earlier, owner_hot, preferred_element_type=jnp.float32)
    owner_float = owner_hot.astype(jnp.float32)
    slot_rank = jnp.sum(before * owner_float, axis=1)
    rank_hot = (slot_rank[:, None] == jnp.arange(capacity, dtype=jnp.float32)[None, :]).astype(
        jnp.float32
    )
    payload = jnp.concatenate(
        [facet_wall, facet_dist[None], facet_area[None], facet_cell[None].astype(jnp.float32)],
        axis=0,
    )
    spread = payload[:, None, :] * owner_float.T[None]
    outgoing = jnp.einsum("cof,fk->cok", spread, rank_hot, precision=exact)
    filled = jnp.dot(owner_float.T, rank_hot, precision=exact)
    unit_dist = (jnp.arange(7, dtype=jnp.int32) == 4).astype(jnp.float32)[:, None, None]
    outgoing = outgoing + unit_dist * (1.0 - filled)[None]
    outgoing = jnp.concatenate([outgoing, jnp.zeros((1, owners_gx, capacity), jnp.float32)], axis=0)
    outgoing = jnp.transpose(outgoing, (1, 0, 2)).reshape(owners_gx, -1)
    x_low, x_high, y_low, y_high, outgoing = lax.optimization_barrier(
        (x_low, x_high, y_low, y_high, outgoing)
    )
    received = lax.all_to_all(outgoing, "gx", 0, 0, tiled=True)
    tend = stencil(state, eddy, x_low, x_high, y_low, y_high)
    tend, received = lax.optimization_barrier((tend, received))
    pay = jnp.transpose(received.reshape(owners_gx, 8, capacity), (1, 0, 2)).reshape(8, slots)
    forcing_rows, flux_slots = owner_side(state.reshape(4 * levels * cells_x, cells_y), pay)
    forcing = forcing_rows.reshape(state.shape)
    wall_flux = jnp.transpose(flux_slots.reshape(4, owners_gx, capacity), (1, 0, 2)).reshape(owners_gx, -1)
    returned = lax.all_to_all(wall_flux, "gx", 0, 0, tiled=True)
    change = (tend - forcing) * (1.0 - solid.astype(jnp.float32))
    new_state = start + dt_step * change
    new_state, returned = lax.optimization_barrier((new_state, returned))
    returned = jnp.transpose(returned.reshape(owners_gx, 4, capacity), (1, 0, 2))
    through = jnp.einsum("cok,fk->cof", returned, rank_hot, precision=exact)
    facet_flux = jnp.sum(through * owner_float.T[None], axis=1)
    return (new_state, facet_flux)


def solution(mesh):
    in_specs = (
        P(None, None, "gx", "gy"),
        P(None, None, "gx", "gy"),
        P(None, "gx", "gy"),
        P(None, "gx", "gy"),
        P(None, ("gx", "gy")),
        P(("gx", "gy")),
        P(("gx", "gy")),
        P(("gx", "gy"), None),
        P(("gx", "gy")),
    )
    out_specs = (P(None, None, "gx", "gy"), P(None, ("gx", "gy")))
    return jax.shard_map(local, mesh=mesh, in_specs=in_specs, out_specs=out_specs, check_vma=False)
```

```python
import math

import jax
import jax.numpy as jnp
from jax import lax
from jax.experimental import pallas as pl
from jax.experimental.pallas import tpu as pltpu
from jax.sharding import PartitionSpec as P

dt_step = 0.2
exact = lax.Precision.HIGHEST


def _upwind(s, c):
    forward = (((((-2.0 * s(-3) + 15.0 * s(-2)) - 60.0 * s(-1)) + 20.0 * s(0)) + 30.0 * s(1)) - 3.0 * s(2))
    backward = (((((3.0 * s(-2) - 30.0 * s(-1)) - 20.0 * s(0)) + 60.0 * s(1)) - 15.0 * s(2)) + 2.0 * s(3))
    return jnp.where(c > 0, forward, backward) / 60.0


def _x_shifter(f, lo_rows, hi_rows):
    rows = f.shape[0]
    row = lax.broadcasted_iota(jnp.int32, f.shape, 0)
    width = len(lo_rows)
    lo_b = [jnp.broadcast_to(r, f.shape) for r in lo_rows]
    hi_b = [jnp.broadcast_to(r, f.shape) for r in hi_rows]
    cache = {0: f}

    def s(k):
        if k in cache:
            return cache[k]
        if k > 0:
            r = pltpu.roll(f, rows - k, 0)
            patch = hi_b[k - 1]
            for i in range(k - 2, -1, -1):
                patch = jnp.where(row == rows - k + i, hi_b[i], patch)
            out = jnp.where(row < rows - k, r, patch)
        else:
            m = -k
            r = pltpu.roll(f, m, 0)
            patch = lo_b[width - 1]
            for i in range(m - 1):
                patch = jnp.where(row == i, lo_b[width - m + i], patch)
            out = jnp.where(row >= m, r, patch)
        cache[k] = out
        return out
    return s


def _y_shifter(f, lo, hi):
    cols = f.shape[1]
    edge = lo.shape[1]
    lane = lax.broadcasted_iota(jnp.int32, lo.shape, 1)
    cache = {0: f}

    def s(k):
        if k in cache:
            return cache[k]
        if k > 0:
            r = pltpu.roll(f, cols - k, 1)
            patch = pltpu.roll(hi, edge - k, 1)
            last = jnp.where(lane >= edge - k, patch, r[:, cols - edge:])
            out = jnp.concatenate([r[:, :cols - edge], last], axis=1)
        else:
            m = -k
            r = pltpu.roll(f, m, 1)
            patch = pltpu.roll(lo, m, 1)
            first = jnp.where(lane < m, patch, r[:, :edge])
            out = jnp.concatenate([first, r[:, edge:]], axis=1)
        cache[k] = out
        return out
    return s


def stencil_kernel(sc_ref, sd_ref, su_ref, ec_ref, ed_ref, eu_ref, xl_ref, xh_ref, yl_ref, yh_ref, out_ref):
    level = pl.program_id(0)
    levels = pl.num_programs(0)
    fields = sc_ref.shape[0]
    width = (xl_ref.shape[1] - 1) // fields
    e = ec_ref[0]
    ed = ed_ref[0]
    eu = eu_ref[0]
    up_w = jnp.where(level < levels - 1, 1.0, 0.0)
    down_w = jnp.where(level > 0, 1.0, 0.0)
    eddy_up = (0.5 * (e + eu)) * up_w
    eddy_down = (0.5 * (ed + e)) * down_w
    ex = _x_shifter(e, [xl_ref[0, pl.ds(fields * width, 1), :]], [xh_ref[0, pl.ds(fields * width, 1), :]])
    ey = _y_shifter(e, yl_ref[fields, 0], yh_ref[fields, 0])
    east = 0.5 * (e + ex(1))
    west = 0.5 * (ex(-1) + e)
    north = 0.5 * (e + ey(1))
    south = 0.5 * (ey(-1) + e)
    u = sc_ref[0, 0]
    v = sc_ref[1, 0]
    w = sc_ref[2, 0]
    for f in range(fields):
        fv = sc_ref[f, 0]
        lower = sd_ref[f, 0]
        upper = su_ref[f, 0]
        sx = _x_shifter(fv, [xl_ref[0, pl.ds(f * width + i, 1), :] for i in range(width)],
                        [xh_ref[0, pl.ds(f * width + i, 1), :] for i in range(width)])
        sy = _y_shifter(fv, yl_ref[f, 0], yh_ref[f, 0])
        derx = _upwind(sx, u)
        dery = _upwind(sy, v)
        derz = (upper - lower) * 0.5
        zdiffuse = eddy_up * (upper - fv) - eddy_down * (fv - lower)
        advect = (u * derx + v * dery) + w * derz
        diff_x = east * (sx(1) - fv) - west * (fv - sx(-1))
        diff_y = north * (sy(1) - fv) - south * (fv - sy(-1))
        diffuse = (diff_x + diff_y) + zdiffuse
        out_ref[f, 0] = diffuse - advect


def stencil(state, eddy, xl, xh, yl, yh):
    fields, levels, cx, cy = state.shape
    w = xl.shape[1]
    nf = yl.shape[0]
    edge = yl.shape[3]
    below = lambda l: jnp.maximum(l - 1, 0)
    above = lambda l: jnp.minimum(l + 1, levels - 1)
    return pl.pallas_call(
        stencil_kernel,
        grid=(levels,),
        in_specs=[
            pl.BlockSpec((fields, 1, cx, cy), lambda l: (0, l, 0, 0)),
            pl.BlockSpec((fields, 1, cx, cy), lambda l: (0, below(l), 0, 0)),
            pl.BlockSpec((fields, 1, cx, cy), lambda l: (0, above(l), 0, 0)),
            pl.BlockSpec((1, cx, cy), lambda l: (l, 0, 0)),
            pl.BlockSpec((1, cx, cy), lambda l: (below(l), 0, 0)),
            pl.BlockSpec((1, cx, cy), lambda l: (above(l), 0, 0)),
            pl.BlockSpec((1, w, cy), lambda l: (l, 0, 0)),
            pl.BlockSpec((1, w, cy), lambda l: (l, 0, 0)),
            pl.BlockSpec((nf, 1, cx, edge), lambda l: (0, l, 0, 0)),
            pl.BlockSpec((nf, 1, cx, edge), lambda l: (0, l, 0, 0)),
        ],
        out_specs=pl.BlockSpec((fields, 1, cx, cy), lambda l: (0, l, 0, 0)),
        out_shape=jax.ShapeDtypeStruct((fields, levels, cx, cy), jnp.float32),
        compiler_params=pltpu.CompilerParams(dimension_semantics=("arbitrary",)),
        cost_estimate=pl.CostEstimate(flops=200 * fields * levels * cx * cy, transcendentals=0,
                                      bytes_accessed=4 * (4 * nf + fields) * levels * cx * cy),
    )(state, state, state, eddy, eddy, eddy, xl, xh, yl, yh)


def _pieces(x, n):
    out = []
    rest = x
    for _ in range(n):
        p = rest.astype(jnp.bfloat16)
        out.append(p)
        rest = rest - p.astype(jnp.float32)
    return out


def owner_kernel(x_ref, pay_ref, forcing_ref, flux_ref, pieces_ref, iota_ref):
    rows, cols = x_ref.shape
    fields = 4
    per_field = rows // fields
    block = pay_ref.shape[1]
    sub = 256
    nsub = cols // sub

    @pl.when(pl.program_id(0) == 0)
    def _():
        parts = _pieces(x_ref[...], 2)
        for i, p in enumerate(parts):
            pieces_ref[i * rows:(i + 1) * rows, :] = p
        forcing_ref[...] = jnp.zeros_like(forcing_ref)
        iota_ref[...] = lax.broadcasted_iota(jnp.int32, (sub, block), 0).astype(jnp.bfloat16)

    pay = pay_ref[...]
    cell = (pay[6:7] + 0.5).astype(jnp.int32)
    col = cell % cols
    row = cell // cols
    hi = col // sub
    lo = (col % sub).astype(jnp.float32)
    iota = iota_ref[...]
    hots = []
    for a in range(nsub):
        sel = jnp.where(hi == a, lo, -1.0).astype(jnp.bfloat16)
        hots.append(jnp.where(iota == sel, jnp.bfloat16(1), jnp.bfloat16(0)))
    hot = jnp.concatenate(hots, axis=0)
    picked = jnp.dot(pieces_ref[...], hot, preferred_element_type=jnp.float32)
    value = picked[0:rows] + picked[rows:2 * rows]
    pick_row = lax.broadcasted_iota(jnp.int32, (per_field, block), 0) == row
    gathered = jnp.concatenate(
        [jnp.sum(jnp.where(pick_row, value[f * per_field:(f + 1) * per_field], 0.0), axis=0, keepdims=True)
         for f in range(fields)], axis=0)
    flux = pay[5:6] * (gathered - pay[0:4]) / pay[4:5]
    flux_ref[...] = flux
    spread = jnp.concatenate(
        [jnp.where(pick_row, flux[f:f + 1], 0.0) for f in range(fields)], axis=0)
    w = jnp.concatenate(_pieces(spread, 2), axis=0)
    added = lax.dot_general(w, hot, (((1,), (1,)), ((), ())), preferred_element_type=jnp.float32)
    forcing_ref[...] += added[0:rows] + added[rows:2 * rows]


def owner_side(x, pay, block=1024):
    rows, cols = x.shape
    slots = pay.shape[1]
    steps = slots // block
    return pl.pallas_call(
        owner_kernel,
        grid=(steps,),
        in_specs=[
            pl.BlockSpec((rows, cols), lambda j: (0, 0)),
            pl.BlockSpec((8, block), lambda j: (0, j)),
        ],
        out_specs=[
            pl.BlockSpec((rows, cols), lambda j: (0, 0)),
            pl.BlockSpec((4, block), lambda j: (0, j)),
        ],
        out_shape=[
            jax.ShapeDtypeStruct((rows, cols), jnp.float32),
            jax.ShapeDtypeStruct((4, slots), jnp.float32),
        ],
        scratch_shapes=[pltpu.VMEM((2 * rows, cols), jnp.bfloat16),
                        pltpu.VMEM((256, block), jnp.bfloat16)],
        compiler_params=pltpu.CompilerParams(dimension_semantics=("arbitrary",),
                                             vmem_limit_bytes=48 * 1024 * 1024),
        cost_estimate=pl.CostEstimate(flops=2 * (4 * rows) * cols * slots, transcendentals=0,
                                      bytes_accessed=4 * (2 * rows * cols + 12 * slots)),
    )(x, pay)


def two_stage_all_to_all(x):
    outer = lax.axis_size("ga")
    inner = lax.axis_size("gb")
    rest = x.shape[1:]
    y = x.reshape((outer, inner) + rest)
    y = lax.all_to_all(y, "gb", 1, 1, tiled=True)
    y = lax.all_to_all(y, "ga", 0, 0, tiled=True)
    return y.reshape((outer * inner,) + rest)


def shift_pair(last, leading, axis):
    peers = lax.axis_size(axis)
    up = [(i, (i + 1) % peers) for i in range(peers)]
    down = [(j, i) for i, j in up]
    return lax.ppermute(last, axis, up), lax.ppermute(leading, axis, down)


def exchange(shard, axis, dim, low, high):
    peers = lax.axis_size(axis)
    length = shard.shape[dim]
    up = [(i, (i + 1) % peers) for i in range(peers)]
    down = [(j, i) for i, j in up]
    last = lax.slice_in_dim(shard, length - low, length, axis=dim)
    leading = lax.slice_in_dim(shard, 0, high, axis=dim)
    before = lax.ppermute(last, axis, up)
    after = lax.ppermute(leading, axis, down)
    return before, after


def local(state, start, eddy, solid, facet_wall, facet_dist, facet_area, facet_owner, facet_cell):
    levels = state.shape[1]
    cells_x = state.shape[2]
    cells_y = state.shape[3]
    width = 3
    edge = 128

    def x_rows(lo, hi):
        rows = jnp.transpose(state[:, :, lo:hi], (1, 0, 2, 3)).reshape(levels, -1, cells_y)
        return jnp.concatenate([rows, eddy[:, lo:hi][:, -1:] if lo else eddy[:, 0:1]], axis=1)

    x_low, x_high = shift_pair(x_rows(cells_x - width, cells_x), x_rows(0, width), ("ga", "gb"))

    def y_cols(lo, hi):
        return jnp.concatenate([state[..., lo:hi], eddy[None, ..., lo:hi]], axis=0)

    y_low, y_high = shift_pair(y_cols(cells_y - edge, cells_y), y_cols(0, edge), "gy")

    facet_count = facet_cell.shape[0]
    owners_gx = lax.axis_size(("ga", "gb"))
    capacity = 2 * facet_count // owners_gx
    slots = owners_gx * capacity
    owner_gx = facet_owner[:, 0]
    owner_hot = (owner_gx[:, None] == jnp.arange(owners_gx, dtype=jnp.int32)[None, :]).astype(
        jnp.bfloat16
    )
    positions = jnp.arange(facet_count, dtype=jnp.int32)
    earlier = (positions[:, None] > positions[None, :]).astype(jnp.bfloat16)
    before = jnp.dot(earlier, owner_hot, preferred_element_type=jnp.float32)
    owner_float = owner_hot.astype(jnp.float32)
    slot_rank = jnp.sum(before * owner_float, axis=1)
    rank_hot = (slot_rank[:, None] == jnp.arange(capacity, dtype=jnp.float32)[None, :]).astype(
        jnp.float32
    )
    payload = jnp.concatenate(
        [facet_wall, facet_dist[None], facet_area[None], facet_cell[None].astype(jnp.float32)],
        axis=0,
    )
    spread = payload[:, None, :] * owner_float.T[None]
    outgoing = jnp.einsum("cof,fk->cok", spread, rank_hot, precision=exact)
    filled = jnp.dot(owner_float.T, rank_hot, precision=exact)
    unit_dist = (jnp.arange(7, dtype=jnp.int32) == 4).astype(jnp.float32)[:, None, None]
    outgoing = outgoing + unit_dist * (1.0 - filled)[None]
    outgoing = jnp.concatenate([outgoing, jnp.zeros((1, owners_gx, capacity), jnp.float32)], axis=0)
    outgoing = jnp.transpose(outgoing, (1, 0, 2)).reshape(owners_gx, -1)
    x_low, x_high, y_low, y_high, outgoing = lax.optimization_barrier(
        (x_low, x_high, y_low, y_high, outgoing)
    )
    received = two_stage_all_to_all(outgoing)
    tend = stencil(state, eddy, x_low, x_high, y_low, y_high)
    tend, received = lax.optimization_barrier((tend, received))
    pay = jnp.transpose(received.reshape(owners_gx, 8, capacity), (1, 0, 2)).reshape(8, slots)
    forcing_rows, flux_slots = owner_side(state.reshape(4 * levels * cells_x, cells_y), pay)
    forcing = forcing_rows.reshape(state.shape)
    wall_flux = jnp.transpose(flux_slots.reshape(4, owners_gx, capacity), (1, 0, 2)).reshape(owners_gx, -1)
    returned = two_stage_all_to_all(wall_flux)
    change = (tend - forcing) * (1.0 - solid.astype(jnp.float32))
    new_state = start + dt_step * change
    new_state, returned = lax.optimization_barrier((new_state, returned))
    returned = jnp.transpose(returned.reshape(owners_gx, 4, capacity), (1, 0, 2))
    through = jnp.einsum("cok,fk->cof", returned, rank_hot, precision=exact)
    facet_flux = jnp.sum(through * owner_float.T[None], axis=1)
    return (new_state, facet_flux)


def solution(mesh):
    devices = mesh.devices
    groups = 8
    split = jax.sharding.Mesh(
        devices.reshape(groups, devices.shape[0] // groups, devices.shape[1]), ("ga", "gb", "gy")
    )
    gx = ("ga", "gb")
    in_specs = (
        P(None, None, gx, "gy"),
        P(None, None, gx, "gy"),
        P(None, gx, "gy"),
        P(None, gx, "gy"),
        P(None, (*gx, "gy")),
        P((*gx, "gy")),
        P((*gx, "gy")),
        P((*gx, "gy"), None),
        P((*gx, "gy")),
    )
    out_specs = (P(None, None, gx, "gy"), P(None, (*gx, "gy")))
    return jax.shard_map(local, mesh=split, in_specs=in_specs, out_specs=out_specs, check_vma=False)
```

```python
import math

import jax
import jax.numpy as jnp
from jax import lax
from jax.experimental import pallas as pl
from jax.experimental.pallas import tpu as pltpu
from jax.sharding import PartitionSpec as P

dt_step = 0.2
exact = lax.Precision.HIGHEST


def _upwind(s, c):
    forward = (((((-2.0 * s(-3) + 15.0 * s(-2)) - 60.0 * s(-1)) + 20.0 * s(0)) + 30.0 * s(1)) - 3.0 * s(2))
    backward = (((((3.0 * s(-2) - 30.0 * s(-1)) - 20.0 * s(0)) + 60.0 * s(1)) - 15.0 * s(2)) + 2.0 * s(3))
    return jnp.where(c > 0, forward, backward) / 60.0


def _x_shifter(f, lo_rows, hi_rows):
    rows = f.shape[0]
    row = lax.broadcasted_iota(jnp.int32, f.shape, 0)
    width = len(lo_rows)
    lo_b = [jnp.broadcast_to(r, f.shape) for r in lo_rows]
    hi_b = [jnp.broadcast_to(r, f.shape) for r in hi_rows]
    cache = {0: f}

    def s(k):
        if k in cache:
            return cache[k]
        if k > 0:
            r = pltpu.roll(f, rows - k, 0)
            patch = hi_b[k - 1]
            for i in range(k - 2, -1, -1):
                patch = jnp.where(row == rows - k + i, hi_b[i], patch)
            out = jnp.where(row < rows - k, r, patch)
        else:
            m = -k
            r = pltpu.roll(f, m, 0)
            patch = lo_b[width - 1]
            for i in range(m - 1):
                patch = jnp.where(row == i, lo_b[width - m + i], patch)
            out = jnp.where(row >= m, r, patch)
        cache[k] = out
        return out
    return s


def _y_shifter(f, lo, hi):
    cols = f.shape[1]
    edge = lo.shape[1]
    lane = lax.broadcasted_iota(jnp.int32, lo.shape, 1)
    cache = {0: f}

    def s(k):
        if k in cache:
            return cache[k]
        if k > 0:
            r = pltpu.roll(f, cols - k, 1)
            patch = pltpu.roll(hi, edge - k, 1)
            last = jnp.where(lane >= edge - k, patch, r[:, cols - edge:])
            out = jnp.concatenate([r[:, :cols - edge], last], axis=1)
        else:
            m = -k
            r = pltpu.roll(f, m, 1)
            patch = pltpu.roll(lo, m, 1)
            first = jnp.where(lane < m, patch, r[:, :edge])
            out = jnp.concatenate([first, r[:, edge:]], axis=1)
        cache[k] = out
        return out
    return s


def stencil_kernel(sc_ref, sd_ref, su_ref, ec_ref, ed_ref, eu_ref, xl_ref, xh_ref, yl_ref, yh_ref, out_ref):
    level = pl.program_id(0)
    levels = pl.num_programs(0)
    fields = sc_ref.shape[0]
    width = (xl_ref.shape[1] - 1) // fields
    e = ec_ref[0]
    ed = ed_ref[0]
    eu = eu_ref[0]
    up_w = jnp.where(level < levels - 1, 1.0, 0.0)
    down_w = jnp.where(level > 0, 1.0, 0.0)
    eddy_up = (0.5 * (e + eu)) * up_w
    eddy_down = (0.5 * (ed + e)) * down_w
    ex = _x_shifter(e, [xl_ref[0, pl.ds(fields * width, 1), :]], [xh_ref[0, pl.ds(fields * width, 1), :]])
    ey = _y_shifter(e, yl_ref[fields, 0], yh_ref[fields, 0])
    east = 0.5 * (e + ex(1))
    west = 0.5 * (ex(-1) + e)
    north = 0.5 * (e + ey(1))
    south = 0.5 * (ey(-1) + e)
    u = sc_ref[0, 0]
    v = sc_ref[1, 0]
    w = sc_ref[2, 0]
    for f in range(fields):
        fv = sc_ref[f, 0]
        lower = sd_ref[f, 0]
        upper = su_ref[f, 0]
        sx = _x_shifter(fv, [xl_ref[0, pl.ds(f * width + i, 1), :] for i in range(width)],
                        [xh_ref[0, pl.ds(f * width + i, 1), :] for i in range(width)])
        sy = _y_shifter(fv, yl_ref[f, 0], yh_ref[f, 0])
        derx = _upwind(sx, u)
        dery = _upwind(sy, v)
        derz = (upper - lower) * 0.5
        zdiffuse = eddy_up * (upper - fv) - eddy_down * (fv - lower)
        advect = (u * derx + v * dery) + w * derz
        diff_x = east * (sx(1) - fv) - west * (fv - sx(-1))
        diff_y = north * (sy(1) - fv) - south * (fv - sy(-1))
        diffuse = (diff_x + diff_y) + zdiffuse
        out_ref[f, 0] = diffuse - advect


def stencil(state, eddy, xl, xh, yl, yh):
    fields, levels, cx, cy = state.shape
    w = xl.shape[1]
    nf = yl.shape[0]
    edge = yl.shape[3]
    below = lambda l: jnp.maximum(l - 1, 0)
    above = lambda l: jnp.minimum(l + 1, levels - 1)
    return pl.pallas_call(
        stencil_kernel,
        grid=(levels,),
        in_specs=[
            pl.BlockSpec((fields, 1, cx, cy), lambda l: (0, l, 0, 0)),
            pl.BlockSpec((fields, 1, cx, cy), lambda l: (0, below(l), 0, 0)),
            pl.BlockSpec((fields, 1, cx, cy), lambda l: (0, above(l), 0, 0)),
            pl.BlockSpec((1, cx, cy), lambda l: (l, 0, 0)),
            pl.BlockSpec((1, cx, cy), lambda l: (below(l), 0, 0)),
            pl.BlockSpec((1, cx, cy), lambda l: (above(l), 0, 0)),
            pl.BlockSpec((1, w, cy), lambda l: (l, 0, 0)),
            pl.BlockSpec((1, w, cy), lambda l: (l, 0, 0)),
            pl.BlockSpec((nf, 1, cx, edge), lambda l: (0, l, 0, 0)),
            pl.BlockSpec((nf, 1, cx, edge), lambda l: (0, l, 0, 0)),
        ],
        out_specs=pl.BlockSpec((fields, 1, cx, cy), lambda l: (0, l, 0, 0)),
        out_shape=jax.ShapeDtypeStruct((fields, levels, cx, cy), jnp.float32),
        compiler_params=pltpu.CompilerParams(dimension_semantics=("arbitrary",)),
        cost_estimate=pl.CostEstimate(flops=200 * fields * levels * cx * cy, transcendentals=0,
                                      bytes_accessed=4 * (4 * nf + fields) * levels * cx * cy),
    )(state, state, state, eddy, eddy, eddy, xl, xh, yl, yh)


def _pieces(x, n):
    out = []
    rest = x
    for _ in range(n):
        p = rest.astype(jnp.bfloat16)
        out.append(p)
        rest = rest - p.astype(jnp.float32)
    return out


def _one_hot(cell, cols, iota):
    sub = iota.shape[0]
    col = cell % cols
    hi = col // sub
    lo = (col % sub).astype(jnp.float32)
    hots = []
    for a in range(cols // sub):
        sel = jnp.where(hi == a, lo, -1.0).astype(jnp.bfloat16)
        hots.append(jnp.where(iota == sel, jnp.bfloat16(1), jnp.bfloat16(0)))
    return jnp.concatenate(hots, axis=0)


def gather_kernel(x_ref, pay_ref, flux_ref, pieces_ref, iota_ref):
    rows, cols = x_ref.shape
    fields = 4
    per_field = rows // fields
    block = pay_ref.shape[1]

    @pl.when(pl.program_id(0) == 0)
    def _():
        parts = _pieces(x_ref[...], 2)
        for i, p in enumerate(parts):
            pieces_ref[i * rows:(i + 1) * rows, :] = p
        iota_ref[...] = lax.broadcasted_iota(jnp.int32, iota_ref.shape, 0).astype(jnp.bfloat16)

    pay = pay_ref[...]
    cell = (pay[6:7] + 0.5).astype(jnp.int32)
    row = cell // cols
    hot = _one_hot(cell, cols, iota_ref[...])
    picked = jnp.dot(pieces_ref[...], hot, preferred_element_type=jnp.float32)
    value = picked[0:rows] + picked[rows:2 * rows]
    pick_row = lax.broadcasted_iota(jnp.int32, (per_field, block), 0) == row
    gathered = jnp.concatenate(
        [jnp.sum(jnp.where(pick_row, value[f * per_field:(f + 1) * per_field], 0.0), axis=0, keepdims=True)
         for f in range(fields)], axis=0)
    flux_ref[...] = pay[5:6] * (gathered - pay[0:4]) / pay[4:5]


def scatter_kernel(pay_ref, flux_ref, forcing_ref, iota_ref):
    rows, cols = forcing_ref.shape
    fields = 4
    per_field = rows // fields
    block = pay_ref.shape[1]

    @pl.when(pl.program_id(0) == 0)
    def _():
        forcing_ref[...] = jnp.zeros_like(forcing_ref)
        iota_ref[...] = lax.broadcasted_iota(jnp.int32, iota_ref.shape, 0).astype(jnp.bfloat16)

    pay = pay_ref[...]
    cell = (pay[6:7] + 0.5).astype(jnp.int32)
    row = cell // cols
    hot = _one_hot(cell, cols, iota_ref[...])
    flux = flux_ref[...]
    pick_row = lax.broadcasted_iota(jnp.int32, (per_field, block), 0) == row
    spread = jnp.concatenate(
        [jnp.where(pick_row, flux[f:f + 1], 0.0) for f in range(fields)], axis=0)
    w = jnp.concatenate(_pieces(spread, 2), axis=0)
    added = lax.dot_general(w, hot, (((1,), (1,)), ((), ())), preferred_element_type=jnp.float32)
    forcing_ref[...] += added[0:rows] + added[rows:2 * rows]


def owner_gather(x, pay, block=1024):
    rows, cols = x.shape
    slots = pay.shape[1]
    return pl.pallas_call(
        gather_kernel,
        grid=(slots // block,),
        in_specs=[
            pl.BlockSpec((rows, cols), lambda j: (0, 0)),
            pl.BlockSpec((8, block), lambda j: (0, j)),
        ],
        out_specs=pl.BlockSpec((4, block), lambda j: (0, j)),
        out_shape=jax.ShapeDtypeStruct((4, slots), jnp.float32),
        scratch_shapes=[pltpu.VMEM((2 * rows, cols), jnp.bfloat16),
                        pltpu.VMEM((256, block), jnp.bfloat16)],
        compiler_params=pltpu.CompilerParams(dimension_semantics=("arbitrary",),
                                             vmem_limit_bytes=48 * 1024 * 1024),
        cost_estimate=pl.CostEstimate(flops=2 * (2 * rows) * cols * slots, transcendentals=0,
                                      bytes_accessed=4 * (rows * cols + 12 * slots)),
    )(x, pay)


def owner_scatter(pay, flux, rows, cols, block=1024):
    slots = pay.shape[1]
    return pl.pallas_call(
        scatter_kernel,
        grid=(slots // block,),
        in_specs=[
            pl.BlockSpec((8, block), lambda j: (0, j)),
            pl.BlockSpec((4, block), lambda j: (0, j)),
        ],
        out_specs=pl.BlockSpec((rows, cols), lambda j: (0, 0)),
        out_shape=jax.ShapeDtypeStruct((rows, cols), jnp.float32),
        scratch_shapes=[pltpu.VMEM((256, block), jnp.bfloat16)],
        compiler_params=pltpu.CompilerParams(dimension_semantics=("arbitrary",),
                                             vmem_limit_bytes=48 * 1024 * 1024),
        cost_estimate=pl.CostEstimate(flops=rows * cols, transcendentals=0, bytes_accessed=4 * rows * cols),
    )(pay, flux)


def shift_pair(last, leading, axis):
    peers = lax.axis_size(axis)
    up = [(i, (i + 1) % peers) for i in range(peers)]
    down = [(j, i) for i, j in up]
    return lax.ppermute(last, axis, up), lax.ppermute(leading, axis, down)


def exchange(shard, axis, dim, low, high):
    peers = lax.axis_size(axis)
    length = shard.shape[dim]
    up = [(i, (i + 1) % peers) for i in range(peers)]
    down = [(j, i) for i, j in up]
    last = lax.slice_in_dim(shard, length - low, length, axis=dim)
    leading = lax.slice_in_dim(shard, 0, high, axis=dim)
    before = lax.ppermute(last, axis, up)
    after = lax.ppermute(leading, axis, down)
    return before, after


def local(state, start, eddy, solid, facet_wall, facet_dist, facet_area, facet_owner, facet_cell):
    levels = state.shape[1]
    cells_x = state.shape[2]
    cells_y = state.shape[3]
    width = 3
    edge = 128

    def x_rows(lo, hi):
        rows = jnp.transpose(state[:, :, lo:hi], (1, 0, 2, 3)).reshape(levels, -1, cells_y)
        return jnp.concatenate([rows, eddy[:, lo:hi][:, -1:] if lo else eddy[:, 0:1]], axis=1)

    x_last, x_first = x_rows(cells_x - width, cells_x), x_rows(0, width)
    x_low, x_high = shift_pair(x_last, x_first, "gx")

    def y_cols(lo, hi):
        return jnp.concatenate([state[..., lo:hi], eddy[None, ..., lo:hi]], axis=0)

    y_low, y_high = shift_pair(y_cols(cells_y - edge, cells_y), y_cols(0, edge), "gy")

    facet_count = facet_cell.shape[0]
    owners_gx = lax.axis_size("gx")
    capacity = 2 * facet_count // owners_gx
    slots = owners_gx * capacity
    owner_gx = facet_owner[:, 0]
    owner_hot = (owner_gx[:, None] == jnp.arange(owners_gx, dtype=jnp.int32)[None, :]).astype(
        jnp.bfloat16
    )
    positions = jnp.arange(facet_count, dtype=jnp.int32)
    earlier = (positions[:, None] > positions[None, :]).astype(jnp.bfloat16)
    before = jnp.dot(earlier, owner_hot, preferred_element_type=jnp.float32)
    owner_float = owner_hot.astype(jnp.float32)
    slot_rank = jnp.sum(before * owner_float, axis=1)
    rank_hot = (slot_rank[:, None] == jnp.arange(capacity, dtype=jnp.float32)[None, :]).astype(
        jnp.float32
    )
    payload = jnp.concatenate(
        [facet_wall, facet_dist[None], facet_area[None], facet_cell[None].astype(jnp.float32)],
        axis=0,
    )
    spread = payload[:, None, :] * owner_float.T[None]
    outgoing = jnp.einsum("cof,fk->cok", spread, rank_hot, precision=exact)
    filled = jnp.dot(owner_float.T, rank_hot, precision=exact)
    unit_dist = (jnp.arange(7, dtype=jnp.int32) == 4).astype(jnp.float32)[:, None, None]
    outgoing = outgoing + unit_dist * (1.0 - filled)[None]
    outgoing = jnp.concatenate([outgoing, jnp.zeros((1, owners_gx, capacity), jnp.float32)], axis=0)
    outgoing = jnp.transpose(outgoing, (1, 0, 2)).reshape(owners_gx, -1)
    x_low, x_high, y_low, y_high, outgoing = lax.optimization_barrier(
        (x_low, x_high, y_low, y_high, outgoing)
    )
    received = lax.all_to_all(outgoing, "gx", 0, 0, tiled=True)
    tend = stencil(state, eddy, x_low, x_high, y_low, y_high)
    tend, received = lax.optimization_barrier((tend, received))
    pay = jnp.transpose(received.reshape(owners_gx, 8, capacity), (1, 0, 2)).reshape(8, slots)
    flux_slots = owner_gather(state.reshape(4 * levels * cells_x, cells_y), pay)
    wall_flux = jnp.transpose(flux_slots.reshape(4, owners_gx, capacity), (1, 0, 2)).reshape(owners_gx, -1)
    wall_flux, pay, flux_slots = lax.optimization_barrier((wall_flux, pay, flux_slots))
    forcing = owner_scatter(pay, flux_slots, 4 * levels * cells_x, cells_y).reshape(state.shape)
    returned = lax.all_to_all(wall_flux, "gx", 0, 0, tiled=True)
    change = (tend - forcing) * (1.0 - solid.astype(jnp.float32))
    new_state = start + dt_step * change
    new_state, returned = lax.optimization_barrier((new_state, returned))
    returned = jnp.transpose(returned.reshape(owners_gx, 4, capacity), (1, 0, 2))
    through = jnp.einsum("cok,fk->cof", returned, rank_hot, precision=exact)
    facet_flux = jnp.sum(through * owner_float.T[None], axis=1)
    return (new_state, facet_flux)


def solution(mesh):
    in_specs = (
        P(None, None, "gx", "gy"),
        P(None, None, "gx", "gy"),
        P(None, "gx", "gy"),
        P(None, "gx", "gy"),
        P(None, ("gx", "gy")),
        P(("gx", "gy")),
        P(("gx", "gy")),
        P(("gx", "gy"), None),
        P(("gx", "gy")),
    )
    out_specs = (P(None, None, "gx", "gy"), P(None, ("gx", "gy")))
    return jax.shard_map(local, mesh=mesh, in_specs=in_specs, out_specs=out_specs, check_vma=False)
```

```python
import math

import jax
import jax.numpy as jnp
from jax import lax
from jax.experimental import pallas as pl
from jax.experimental.pallas import tpu as pltpu
from jax.sharding import PartitionSpec as P

dt_step = 0.2
exact = lax.Precision.HIGHEST


def _upwind(s, c):
    forward = (((((-2.0 * s(-3) + 15.0 * s(-2)) - 60.0 * s(-1)) + 20.0 * s(0)) + 30.0 * s(1)) - 3.0 * s(2))
    backward = (((((3.0 * s(-2) - 30.0 * s(-1)) - 20.0 * s(0)) + 60.0 * s(1)) - 15.0 * s(2)) + 2.0 * s(3))
    return jnp.where(c > 0, forward, backward) / 60.0


def _x_shifter(f, lo_rows, hi_rows):
    rows = f.shape[0]
    row = lax.broadcasted_iota(jnp.int32, f.shape, 0)
    width = len(lo_rows)
    lo_b = [jnp.broadcast_to(r, f.shape) for r in lo_rows]
    hi_b = [jnp.broadcast_to(r, f.shape) for r in hi_rows]
    cache = {0: f}

    def s(k):
        if k in cache:
            return cache[k]
        if k > 0:
            r = pltpu.roll(f, rows - k, 0)
            patch = hi_b[k - 1]
            for i in range(k - 2, -1, -1):
                patch = jnp.where(row == rows - k + i, hi_b[i], patch)
            out = jnp.where(row < rows - k, r, patch)
        else:
            m = -k
            r = pltpu.roll(f, m, 0)
            patch = lo_b[width - 1]
            for i in range(m - 1):
                patch = jnp.where(row == i, lo_b[width - m + i], patch)
            out = jnp.where(row >= m, r, patch)
        cache[k] = out
        return out
    return s


def _y_shifter(f, lo, hi):
    cols = f.shape[1]
    edge = lo.shape[1]
    lane = lax.broadcasted_iota(jnp.int32, lo.shape, 1)
    cache = {0: f}

    def s(k):
        if k in cache:
            return cache[k]
        if k > 0:
            r = pltpu.roll(f, cols - k, 1)
            patch = pltpu.roll(hi, edge - k, 1)
            last = jnp.where(lane >= edge - k, patch, r[:, cols - edge:])
            out = jnp.concatenate([r[:, :cols - edge], last], axis=1)
        else:
            m = -k
            r = pltpu.roll(f, m, 1)
            patch = pltpu.roll(lo, m, 1)
            first = jnp.where(lane < m, patch, r[:, :edge])
            out = jnp.concatenate([first, r[:, edge:]], axis=1)
        cache[k] = out
        return out
    return s


def stencil_kernel(sc_ref, sd_ref, su_ref, ec_ref, ed_ref, eu_ref, xl_ref, xh_ref, yl_ref, yh_ref, out_ref):
    level = pl.program_id(0)
    levels = pl.num_programs(0)
    fields = sc_ref.shape[0]
    width = (xl_ref.shape[1] - 1) // fields
    e = ec_ref[0]
    ed = ed_ref[0]
    eu = eu_ref[0]
    up_w = jnp.where(level < levels - 1, 1.0, 0.0)
    down_w = jnp.where(level > 0, 1.0, 0.0)
    eddy_up = (0.5 * (e + eu)) * up_w
    eddy_down = (0.5 * (ed + e)) * down_w
    ex = _x_shifter(e, [xl_ref[0, pl.ds(fields * width, 1), :]], [xh_ref[0, pl.ds(fields * width, 1), :]])
    ey = _y_shifter(e, yl_ref[fields, 0], yh_ref[fields, 0])
    east = 0.5 * (e + ex(1))
    west = 0.5 * (ex(-1) + e)
    north = 0.5 * (e + ey(1))
    south = 0.5 * (ey(-1) + e)
    u = sc_ref[0, 0]
    v = sc_ref[1, 0]
    w = sc_ref[2, 0]
    for f in range(fields):
        fv = sc_ref[f, 0]
        lower = sd_ref[f, 0]
        upper = su_ref[f, 0]
        sx = _x_shifter(fv, [xl_ref[0, pl.ds(f * width + i, 1), :] for i in range(width)],
                        [xh_ref[0, pl.ds(f * width + i, 1), :] for i in range(width)])
        sy = _y_shifter(fv, yl_ref[f, 0], yh_ref[f, 0])
        derx = _upwind(sx, u)
        dery = _upwind(sy, v)
        derz = (upper - lower) * 0.5
        zdiffuse = eddy_up * (upper - fv) - eddy_down * (fv - lower)
        advect = (u * derx + v * dery) + w * derz
        diff_x = east * (sx(1) - fv) - west * (fv - sx(-1))
        diff_y = north * (sy(1) - fv) - south * (fv - sy(-1))
        diffuse = (diff_x + diff_y) + zdiffuse
        out_ref[f, 0] = diffuse - advect


def stencil(state, eddy, xl, xh, yl, yh):
    fields, levels, cx, cy = state.shape
    w = xl.shape[1]
    nf = yl.shape[0]
    edge = yl.shape[3]
    below = lambda l: jnp.maximum(l - 1, 0)
    above = lambda l: jnp.minimum(l + 1, levels - 1)
    return pl.pallas_call(
        stencil_kernel,
        grid=(levels,),
        in_specs=[
            pl.BlockSpec((fields, 1, cx, cy), lambda l: (0, l, 0, 0)),
            pl.BlockSpec((fields, 1, cx, cy), lambda l: (0, below(l), 0, 0)),
            pl.BlockSpec((fields, 1, cx, cy), lambda l: (0, above(l), 0, 0)),
            pl.BlockSpec((1, cx, cy), lambda l: (l, 0, 0)),
            pl.BlockSpec((1, cx, cy), lambda l: (below(l), 0, 0)),
            pl.BlockSpec((1, cx, cy), lambda l: (above(l), 0, 0)),
            pl.BlockSpec((1, w, cy), lambda l: (l, 0, 0)),
            pl.BlockSpec((1, w, cy), lambda l: (l, 0, 0)),
            pl.BlockSpec((nf, 1, cx, edge), lambda l: (0, l, 0, 0)),
            pl.BlockSpec((nf, 1, cx, edge), lambda l: (0, l, 0, 0)),
        ],
        out_specs=pl.BlockSpec((fields, 1, cx, cy), lambda l: (0, l, 0, 0)),
        out_shape=jax.ShapeDtypeStruct((fields, levels, cx, cy), jnp.float32),
        compiler_params=pltpu.CompilerParams(dimension_semantics=("arbitrary",)),
        cost_estimate=pl.CostEstimate(flops=200 * fields * levels * cx * cy, transcendentals=0,
                                      bytes_accessed=4 * (4 * nf + fields) * levels * cx * cy),
    )(state, state, state, eddy, eddy, eddy, xl, xh, yl, yh)


def _pieces(x, n):
    out = []
    rest = x
    for _ in range(n):
        p = rest.astype(jnp.bfloat16)
        out.append(p)
        rest = rest - p.astype(jnp.float32)
    return out


def _one_hot(cell, cols, iota):
    sub = iota.shape[0]
    col = cell % cols
    hi = col // sub
    lo = (col % sub).astype(jnp.float32)
    hots = []
    for a in range(cols // sub):
        sel = jnp.where(hi == a, lo, -1.0).astype(jnp.bfloat16)
        hots.append(jnp.where(iota == sel, jnp.bfloat16(1), jnp.bfloat16(0)))
    return jnp.concatenate(hots, axis=0)


def gather_kernel(x_ref, pay_ref, flux_ref, pieces_ref, iota_ref):
    rows, cols = x_ref.shape
    fields = 4
    per_field = rows // fields
    block = pay_ref.shape[1]

    @pl.when(pl.program_id(0) == 0)
    def _():
        parts = _pieces(x_ref[...], 2)
        for i, p in enumerate(parts):
            pieces_ref[i * rows:(i + 1) * rows, :] = p
        iota_ref[...] = lax.broadcasted_iota(jnp.int32, iota_ref.shape, 0).astype(jnp.bfloat16)

    pay = pay_ref[...]
    cell = (pay[6:7] + 0.5).astype(jnp.int32)
    row = cell // cols
    hot = _one_hot(cell, cols, iota_ref[...])
    picked = jnp.dot(pieces_ref[...], hot, preferred_element_type=jnp.float32)
    value = picked[0:rows] + picked[rows:2 * rows]
    pick_row = lax.broadcasted_iota(jnp.int32, (per_field, block), 0) == row
    gathered = jnp.concatenate(
        [jnp.sum(jnp.where(pick_row, value[f * per_field:(f + 1) * per_field], 0.0), axis=0, keepdims=True)
         for f in range(fields)], axis=0)
    flux_ref[...] = pay[5:6] * (gathered - pay[0:4]) / pay[4:5]


def scatter_kernel(pay_ref, flux_ref, forcing_ref, iota_ref):
    rows, cols = forcing_ref.shape
    fields = 4
    per_field = rows // fields
    block = pay_ref.shape[1]

    @pl.when(pl.program_id(0) == 0)
    def _():
        forcing_ref[...] = jnp.zeros_like(forcing_ref)
        iota_ref[...] = lax.broadcasted_iota(jnp.int32, iota_ref.shape, 0).astype(jnp.bfloat16)

    pay = pay_ref[...]
    cell = (pay[6:7] + 0.5).astype(jnp.int32)
    row = cell // cols
    hot = _one_hot(cell, cols, iota_ref[...])
    flux = flux_ref[...]
    pick_row = lax.broadcasted_iota(jnp.int32, (per_field, block), 0) == row
    spread = jnp.concatenate(
        [jnp.where(pick_row, flux[f:f + 1], 0.0) for f in range(fields)], axis=0)
    w = jnp.concatenate(_pieces(spread, 2), axis=0)
    added = lax.dot_general(w, hot, (((1,), (1,)), ((), ())), preferred_element_type=jnp.float32)
    forcing_ref[...] += added[0:rows] + added[rows:2 * rows]


def owner_gather(x, pay, block=1024):
    rows, cols = x.shape
    slots = pay.shape[1]
    return pl.pallas_call(
        gather_kernel,
        grid=(slots // block,),
        in_specs=[
            pl.BlockSpec((rows, cols), lambda j: (0, 0)),
            pl.BlockSpec((8, block), lambda j: (0, j)),
        ],
        out_specs=pl.BlockSpec((4, block), lambda j: (0, j)),
        out_shape=jax.ShapeDtypeStruct((4, slots), jnp.float32),
        scratch_shapes=[pltpu.VMEM((2 * rows, cols), jnp.bfloat16),
                        pltpu.VMEM((256, block), jnp.bfloat16)],
        compiler_params=pltpu.CompilerParams(dimension_semantics=("arbitrary",),
                                             vmem_limit_bytes=48 * 1024 * 1024),
        cost_estimate=pl.CostEstimate(flops=2 * (2 * rows) * cols * slots, transcendentals=0,
                                      bytes_accessed=4 * (rows * cols + 12 * slots)),
    )(x, pay)


def owner_scatter(pay, flux, rows, cols, block=1024):
    slots = pay.shape[1]
    return pl.pallas_call(
        scatter_kernel,
        grid=(slots // block,),
        in_specs=[
            pl.BlockSpec((8, block), lambda j: (0, j)),
            pl.BlockSpec((4, block), lambda j: (0, j)),
        ],
        out_specs=pl.BlockSpec((rows, cols), lambda j: (0, 0)),
        out_shape=jax.ShapeDtypeStruct((rows, cols), jnp.float32),
        scratch_shapes=[pltpu.VMEM((256, block), jnp.bfloat16)],
        compiler_params=pltpu.CompilerParams(dimension_semantics=("arbitrary",),
                                             vmem_limit_bytes=48 * 1024 * 1024),
        cost_estimate=pl.CostEstimate(flops=rows * cols, transcendentals=0, bytes_accessed=4 * rows * cols),
    )(pay, flux)


def shift_pair(last, leading, axis):
    peers = lax.axis_size(axis)
    up = [(i, (i + 1) % peers) for i in range(peers)]
    down = [(j, i) for i, j in up]
    return lax.ppermute(last, axis, up), lax.ppermute(leading, axis, down)


def exchange(shard, axis, dim, low, high):
    peers = lax.axis_size(axis)
    length = shard.shape[dim]
    up = [(i, (i + 1) % peers) for i in range(peers)]
    down = [(j, i) for i, j in up]
    last = lax.slice_in_dim(shard, length - low, length, axis=dim)
    leading = lax.slice_in_dim(shard, 0, high, axis=dim)
    before = lax.ppermute(last, axis, up)
    after = lax.ppermute(leading, axis, down)
    return before, after


def local(state, start, eddy, solid, facet_wall, facet_dist, facet_area, facet_owner, facet_cell):
    levels = state.shape[1]
    cells_x = state.shape[2]
    cells_y = state.shape[3]
    width = 3
    edge = 128

    def x_rows(lo, hi):
        rows = jnp.transpose(state[:, :, lo:hi], (1, 0, 2, 3)).reshape(levels, -1, cells_y)
        return jnp.concatenate([rows, eddy[:, lo:hi][:, -1:] if lo else eddy[:, 0:1]], axis=1)

    x_last, x_first = x_rows(cells_x - width, cells_x), x_rows(0, width)
    x_low, x_high = shift_pair(x_last, x_first, "gx")

    facet_count = facet_cell.shape[0]
    owners_gx = lax.axis_size("gx")
    capacity = 2 * facet_count // owners_gx
    slots = owners_gx * capacity
    owner_gx = facet_owner[:, 0]
    owner_hot = (owner_gx[:, None] == jnp.arange(owners_gx, dtype=jnp.int32)[None, :]).astype(
        jnp.bfloat16
    )
    positions = jnp.arange(facet_count, dtype=jnp.int32)
    earlier = (positions[:, None] > positions[None, :]).astype(jnp.bfloat16)
    before = jnp.dot(earlier, owner_hot, preferred_element_type=jnp.float32)
    owner_float = owner_hot.astype(jnp.float32)
    slot_rank = jnp.sum(before * owner_float, axis=1)
    rank_hot = (slot_rank[:, None] == jnp.arange(capacity, dtype=jnp.float32)[None, :]).astype(
        jnp.float32
    )
    payload = jnp.concatenate(
        [facet_wall, facet_dist[None], facet_area[None], facet_cell[None].astype(jnp.float32)],
        axis=0,
    )
    spread = payload[:, None, :] * owner_float.T[None]
    outgoing = jnp.einsum("cof,fk->cok", spread, rank_hot, precision=exact)
    filled = jnp.dot(owner_float.T, rank_hot, precision=exact)
    unit_dist = (jnp.arange(7, dtype=jnp.int32) == 4).astype(jnp.float32)[:, None, None]
    outgoing = outgoing + unit_dist * (1.0 - filled)[None]
    outgoing = jnp.concatenate([outgoing, jnp.zeros((1, owners_gx, capacity), jnp.float32)], axis=0)
    outgoing = jnp.transpose(outgoing, (1, 0, 2)).reshape(owners_gx, -1)
    outgoing, y_state, y_eddy = lax.optimization_barrier((outgoing, state, eddy))

    def y_cols(lo, hi):
        return jnp.concatenate([y_state[..., lo:hi], y_eddy[None, ..., lo:hi]], axis=0)

    y_low, y_high = shift_pair(y_cols(cells_y - edge, cells_y), y_cols(0, edge), "gy")
    x_low, x_high, y_low, y_high, outgoing = lax.optimization_barrier(
        (x_low, x_high, y_low, y_high, outgoing)
    )
    received = lax.all_to_all(outgoing, "gx", 0, 0, tiled=True)
    tend = stencil(state, eddy, x_low, x_high, y_low, y_high)
    tend, received = lax.optimization_barrier((tend, received))
    pay = jnp.transpose(received.reshape(owners_gx, 8, capacity), (1, 0, 2)).reshape(8, slots)
    flux_slots = owner_gather(state.reshape(4 * levels * cells_x, cells_y), pay)
    wall_flux = jnp.transpose(flux_slots.reshape(4, owners_gx, capacity), (1, 0, 2)).reshape(owners_gx, -1)
    wall_flux, pay, flux_slots = lax.optimization_barrier((wall_flux, pay, flux_slots))
    forcing = owner_scatter(pay, flux_slots, 4 * levels * cells_x, cells_y).reshape(state.shape)
    returned = lax.all_to_all(wall_flux, "gx", 0, 0, tiled=True)
    change = (tend - forcing) * (1.0 - solid.astype(jnp.float32))
    new_state = start + dt_step * change
    new_state, returned = lax.optimization_barrier((new_state, returned))
    returned = jnp.transpose(returned.reshape(owners_gx, 4, capacity), (1, 0, 2))
    through = jnp.einsum("cok,fk->cof", returned, rank_hot, precision=exact)
    facet_flux = jnp.sum(through * owner_float.T[None], axis=1)
    return (new_state, facet_flux)


def solution(mesh):
    in_specs = (
        P(None, None, "gx", "gy"),
        P(None, None, "gx", "gy"),
        P(None, "gx", "gy"),
        P(None, "gx", "gy"),
        P(None, ("gx", "gy")),
        P(("gx", "gy")),
        P(("gx", "gy")),
        P(("gx", "gy"), None),
        P(("gx", "gy")),
    )
    out_specs = (P(None, None, "gx", "gy"), P(None, ("gx", "gy")))
    return jax.shard_map(local, mesh=mesh, in_specs=in_specs, out_specs=out_specs, check_vma=False)
```

```python
import math

import jax
import jax.numpy as jnp
from jax import lax
from jax.experimental import pallas as pl
from jax.experimental.pallas import tpu as pltpu
from jax.sharding import PartitionSpec as P

dt_step = 0.2
exact = lax.Precision.HIGHEST


def _upwind(s, c):
    forward = (((((-2.0 * s(-3) + 15.0 * s(-2)) - 60.0 * s(-1)) + 20.0 * s(0)) + 30.0 * s(1)) - 3.0 * s(2))
    backward = (((((3.0 * s(-2) - 30.0 * s(-1)) - 20.0 * s(0)) + 60.0 * s(1)) - 15.0 * s(2)) + 2.0 * s(3))
    return jnp.where(c > 0, forward, backward) / 60.0


def _x_shifter(f, lo_rows, hi_rows):
    rows = f.shape[0]
    row = lax.broadcasted_iota(jnp.int32, f.shape, 0)
    width = len(lo_rows)
    lo_b = [jnp.broadcast_to(r, f.shape) for r in lo_rows]
    hi_b = [jnp.broadcast_to(r, f.shape) for r in hi_rows]
    cache = {0: f}

    def s(k):
        if k in cache:
            return cache[k]
        if k > 0:
            r = pltpu.roll(f, rows - k, 0)
            patch = hi_b[k - 1]
            for i in range(k - 2, -1, -1):
                patch = jnp.where(row == rows - k + i, hi_b[i], patch)
            out = jnp.where(row < rows - k, r, patch)
        else:
            m = -k
            r = pltpu.roll(f, m, 0)
            patch = lo_b[width - 1]
            for i in range(m - 1):
                patch = jnp.where(row == i, lo_b[width - m + i], patch)
            out = jnp.where(row >= m, r, patch)
        cache[k] = out
        return out
    return s


def _y_shifter(f, lo, hi):
    cols = f.shape[1]
    edge = lo.shape[1]
    lane = lax.broadcasted_iota(jnp.int32, lo.shape, 1)
    cache = {0: f}

    def s(k):
        if k in cache:
            return cache[k]
        if k > 0:
            r = pltpu.roll(f, cols - k, 1)
            patch = pltpu.roll(hi, edge - k, 1)
            last = jnp.where(lane >= edge - k, patch, r[:, cols - edge:])
            out = jnp.concatenate([r[:, :cols - edge], last], axis=1)
        else:
            m = -k
            r = pltpu.roll(f, m, 1)
            patch = pltpu.roll(lo, m, 1)
            first = jnp.where(lane < m, patch, r[:, :edge])
            out = jnp.concatenate([first, r[:, edge:]], axis=1)
        cache[k] = out
        return out
    return s


def stencil_kernel(sc_ref, sd_ref, su_ref, ec_ref, ed_ref, eu_ref, xl_ref, xh_ref, yl_ref, yh_ref, out_ref):
    level = pl.program_id(0)
    levels = pl.num_programs(0)
    fields = sc_ref.shape[0]
    width = (xl_ref.shape[1] - 1) // fields
    e = ec_ref[0]
    ed = ed_ref[0]
    eu = eu_ref[0]
    up_w = jnp.where(level < levels - 1, 1.0, 0.0)
    down_w = jnp.where(level > 0, 1.0, 0.0)
    eddy_up = (0.5 * (e + eu)) * up_w
    eddy_down = (0.5 * (ed + e)) * down_w
    ex = _x_shifter(e, [xl_ref[0, pl.ds(fields * width, 1), :]], [xh_ref[0, pl.ds(fields * width, 1), :]])
    ey = _y_shifter(e, yl_ref[fields, 0], yh_ref[fields, 0])
    east = 0.5 * (e + ex(1))
    west = 0.5 * (ex(-1) + e)
    north = 0.5 * (e + ey(1))
    south = 0.5 * (ey(-1) + e)
    u = sc_ref[0, 0]
    v = sc_ref[1, 0]
    w = sc_ref[2, 0]
    for f in range(fields):
        fv = sc_ref[f, 0]
        lower = sd_ref[f, 0]
        upper = su_ref[f, 0]
        sx = _x_shifter(fv, [xl_ref[0, pl.ds(f * width + i, 1), :] for i in range(width)],
                        [xh_ref[0, pl.ds(f * width + i, 1), :] for i in range(width)])
        sy = _y_shifter(fv, yl_ref[f, 0], yh_ref[f, 0])
        derx = _upwind(sx, u)
        dery = _upwind(sy, v)
        derz = (upper - lower) * 0.5
        zdiffuse = eddy_up * (upper - fv) - eddy_down * (fv - lower)
        advect = (u * derx + v * dery) + w * derz
        diff_x = east * (sx(1) - fv) - west * (fv - sx(-1))
        diff_y = north * (sy(1) - fv) - south * (fv - sy(-1))
        diffuse = (diff_x + diff_y) + zdiffuse
        out_ref[f, 0] = diffuse - advect


def stencil(state, eddy, xl, xh, yl, yh):
    fields, levels, cx, cy = state.shape
    w = xl.shape[1]
    nf = yl.shape[0]
    edge = yl.shape[3]
    below = lambda l: jnp.maximum(l - 1, 0)
    above = lambda l: jnp.minimum(l + 1, levels - 1)
    return pl.pallas_call(
        stencil_kernel,
        grid=(levels,),
        in_specs=[
            pl.BlockSpec((fields, 1, cx, cy), lambda l: (0, l, 0, 0)),
            pl.BlockSpec((fields, 1, cx, cy), lambda l: (0, below(l), 0, 0)),
            pl.BlockSpec((fields, 1, cx, cy), lambda l: (0, above(l), 0, 0)),
            pl.BlockSpec((1, cx, cy), lambda l: (l, 0, 0)),
            pl.BlockSpec((1, cx, cy), lambda l: (below(l), 0, 0)),
            pl.BlockSpec((1, cx, cy), lambda l: (above(l), 0, 0)),
            pl.BlockSpec((1, w, cy), lambda l: (l, 0, 0)),
            pl.BlockSpec((1, w, cy), lambda l: (l, 0, 0)),
            pl.BlockSpec((nf, 1, cx, edge), lambda l: (0, l, 0, 0)),
            pl.BlockSpec((nf, 1, cx, edge), lambda l: (0, l, 0, 0)),
        ],
        out_specs=pl.BlockSpec((fields, 1, cx, cy), lambda l: (0, l, 0, 0)),
        out_shape=jax.ShapeDtypeStruct((fields, levels, cx, cy), jnp.float32),
        compiler_params=pltpu.CompilerParams(dimension_semantics=("arbitrary",)),
        cost_estimate=pl.CostEstimate(flops=200 * fields * levels * cx * cy, transcendentals=0,
                                      bytes_accessed=4 * (4 * nf + fields) * levels * cx * cy),
    )(state, state, state, eddy, eddy, eddy, xl, xh, yl, yh)


def _pieces(x, n):
    out = []
    rest = x
    for _ in range(n):
        p = rest.astype(jnp.bfloat16)
        out.append(p)
        rest = rest - p.astype(jnp.float32)
    return out


def _one_hot(cell, cols, iota):
    sub = iota.shape[0]
    col = cell % cols
    hi = col // sub
    lo = (col % sub).astype(jnp.float32)
    hots = []
    for a in range(cols // sub):
        sel = jnp.where(hi == a, lo, -1.0).astype(jnp.bfloat16)
        hots.append(jnp.where(iota == sel, jnp.bfloat16(1), jnp.bfloat16(0)))
    return jnp.concatenate(hots, axis=0)


def gather_kernel(x_ref, pay_ref, flux_ref, pieces_ref, iota_ref):
    rows, cols = x_ref.shape
    fields = 4
    per_field = rows // fields
    block = pay_ref.shape[1]

    @pl.when(pl.program_id(0) == 0)
    def _():
        parts = _pieces(x_ref[...], 2)
        for i, p in enumerate(parts):
            pieces_ref[i * rows:(i + 1) * rows, :] = p
        iota_ref[...] = lax.broadcasted_iota(jnp.int32, iota_ref.shape, 0).astype(jnp.bfloat16)

    pay = pay_ref[...]
    cell = (pay[6:7] + 0.5).astype(jnp.int32)
    row = cell // cols
    hot = _one_hot(cell, cols, iota_ref[...])
    picked = jnp.dot(pieces_ref[...], hot, preferred_element_type=jnp.float32)
    value = picked[0:rows] + picked[rows:2 * rows]
    pick_row = lax.broadcasted_iota(jnp.int32, (per_field, block), 0) == row
    gathered = jnp.concatenate(
        [jnp.sum(jnp.where(pick_row, value[f * per_field:(f + 1) * per_field], 0.0), axis=0, keepdims=True)
         for f in range(fields)], axis=0)
    flux_ref[...] = pay[5:6] * (gathered - pay[0:4]) / pay[4:5]


def scatter_kernel(pay_ref, flux_ref, forcing_ref, iota_ref):
    rows, cols = forcing_ref.shape
    fields = 4
    per_field = rows // fields
    block = pay_ref.shape[1]

    @pl.when(pl.program_id(0) == 0)
    def _():
        forcing_ref[...] = jnp.zeros_like(forcing_ref)
        iota_ref[...] = lax.broadcasted_iota(jnp.int32, iota_ref.shape, 0).astype(jnp.bfloat16)

    pay = pay_ref[...]
    cell = (pay[6:7] + 0.5).astype(jnp.int32)
    row = cell // cols
    hot = _one_hot(cell, cols, iota_ref[...])
    flux = flux_ref[...]
    pick_row = lax.broadcasted_iota(jnp.int32, (per_field, block), 0) == row
    spread = jnp.concatenate(
        [jnp.where(pick_row, flux[f:f + 1], 0.0) for f in range(fields)], axis=0)
    w = jnp.concatenate(_pieces(spread, 2), axis=0)
    added = lax.dot_general(w, hot, (((1,), (1,)), ((), ())), preferred_element_type=jnp.float32)
    forcing_ref[...] += added[0:rows] + added[rows:2 * rows]


def owner_gather(x, pay, block=1024):
    rows, cols = x.shape
    slots = pay.shape[1]
    return pl.pallas_call(
        gather_kernel,
        grid=(slots // block,),
        in_specs=[
            pl.BlockSpec((rows, cols), lambda j: (0, 0)),
            pl.BlockSpec((8, block), lambda j: (0, j)),
        ],
        out_specs=pl.BlockSpec((4, block), lambda j: (0, j)),
        out_shape=jax.ShapeDtypeStruct((4, slots), jnp.float32),
        scratch_shapes=[pltpu.VMEM((2 * rows, cols), jnp.bfloat16),
                        pltpu.VMEM((256, block), jnp.bfloat16)],
        compiler_params=pltpu.CompilerParams(dimension_semantics=("arbitrary",),
                                             vmem_limit_bytes=48 * 1024 * 1024),
        cost_estimate=pl.CostEstimate(flops=2 * (2 * rows) * cols * slots, transcendentals=0,
                                      bytes_accessed=4 * (rows * cols + 12 * slots)),
    )(x, pay)


def owner_scatter(pay, flux, rows, cols, block=1024):
    slots = pay.shape[1]
    return pl.pallas_call(
        scatter_kernel,
        grid=(slots // block,),
        in_specs=[
            pl.BlockSpec((8, block), lambda j: (0, j)),
            pl.BlockSpec((4, block), lambda j: (0, j)),
        ],
        out_specs=pl.BlockSpec((rows, cols), lambda j: (0, 0)),
        out_shape=jax.ShapeDtypeStruct((rows, cols), jnp.float32),
        scratch_shapes=[pltpu.VMEM((256, block), jnp.bfloat16)],
        compiler_params=pltpu.CompilerParams(dimension_semantics=("arbitrary",),
                                             vmem_limit_bytes=48 * 1024 * 1024),
        cost_estimate=pl.CostEstimate(flops=rows * cols, transcendentals=0, bytes_accessed=4 * rows * cols),
    )(pay, flux)


def shift_pair(last, leading, axis):
    peers = lax.axis_size(axis)
    up = [(i, (i + 1) % peers) for i in range(peers)]
    down = [(j, i) for i, j in up]
    return lax.ppermute(last, axis, up), lax.ppermute(leading, axis, down)


def exchange(shard, axis, dim, low, high):
    peers = lax.axis_size(axis)
    length = shard.shape[dim]
    up = [(i, (i + 1) % peers) for i in range(peers)]
    down = [(j, i) for i, j in up]
    last = lax.slice_in_dim(shard, length - low, length, axis=dim)
    leading = lax.slice_in_dim(shard, 0, high, axis=dim)
    before = lax.ppermute(last, axis, up)
    after = lax.ppermute(leading, axis, down)
    return before, after


def local(state, start, eddy, solid, facet_wall, facet_dist, facet_area, facet_owner, facet_cell):
    levels = state.shape[1]
    cells_x = state.shape[2]
    cells_y = state.shape[3]
    width = 3
    edge = 128

    def x_rows(lo, hi):
        rows = jnp.transpose(state[:, :, lo:hi], (1, 0, 2, 3)).reshape(levels, -1, cells_y)
        return jnp.concatenate([rows, eddy[:, lo:hi][:, -1:] if lo else eddy[:, 0:1]], axis=1)

    x_last, x_first = x_rows(cells_x - width, cells_x), x_rows(0, width)
    x_low, x_high = shift_pair(x_last, x_first, "gx")

    facet_count = facet_cell.shape[0]
    owners_gx = lax.axis_size("gx")
    capacity = 2 * facet_count // owners_gx
    slots = owners_gx * capacity
    owner_gx = facet_owner[:, 0]
    owner_hot = (owner_gx[:, None] == jnp.arange(owners_gx, dtype=jnp.int32)[None, :]).astype(
        jnp.bfloat16
    )
    positions = jnp.arange(facet_count, dtype=jnp.int32)
    earlier = (positions[:, None] > positions[None, :]).astype(jnp.bfloat16)
    before = jnp.dot(earlier, owner_hot, preferred_element_type=jnp.float32)
    owner_float = owner_hot.astype(jnp.float32)
    slot_rank = jnp.sum(before * owner_float, axis=1)
    rank_hot = (slot_rank[:, None] == jnp.arange(capacity, dtype=jnp.float32)[None, :]).astype(
        jnp.float32
    )
    payload = jnp.concatenate(
        [facet_wall, facet_dist[None], facet_area[None], facet_cell[None].astype(jnp.float32)],
        axis=0,
    )
    spread = payload[:, None, :] * owner_float.T[None]
    outgoing = jnp.einsum("cof,fk->cok", spread, rank_hot, precision=exact)
    filled = jnp.dot(owner_float.T, rank_hot, precision=exact)
    unit_dist = (jnp.arange(7, dtype=jnp.int32) == 4).astype(jnp.float32)[:, None, None]
    outgoing = outgoing + unit_dist * (1.0 - filled)[None]
    outgoing = jnp.concatenate([outgoing, jnp.zeros((1, owners_gx, capacity), jnp.float32)], axis=0)
    outgoing = jnp.transpose(outgoing, (1, 0, 2)).reshape(owners_gx, -1)
    outgoing, y_state, y_eddy = lax.optimization_barrier((outgoing, state, eddy))

    def y_cols(lo, hi, one):
        return jnp.concatenate([y_state[..., lo:hi].reshape(-1), y_eddy[..., one:one + 1].reshape(-1)])

    def y_tile(flat, lanes, one):
        fields_part = flat[: 4 * levels * cells_x * width].reshape(4, levels, cells_x, width)
        eddy_part = flat[4 * levels * cells_x * width:].reshape(1, levels, cells_x, 1)
        pad_f = ((0, 0), (0, 0), (0, 0), (lanes, edge - width - lanes))
        pad_e = ((0, 0), (0, 0), (0, 0), (one, edge - 1 - one))
        return jnp.concatenate([jnp.pad(fields_part, pad_f), jnp.pad(eddy_part, pad_e)], axis=0)

    y_low, y_high = shift_pair(
        y_cols(cells_y - width, cells_y, cells_y - 1), y_cols(0, width, 0), "gy"
    )
    y_low = y_tile(y_low, edge - width, edge - 1)
    y_high = y_tile(y_high, 0, 0)
    x_low, x_high, y_low, y_high, outgoing = lax.optimization_barrier(
        (x_low, x_high, y_low, y_high, outgoing)
    )
    received = lax.all_to_all(outgoing, "gx", 0, 0, tiled=True)
    tend = stencil(state, eddy, x_low, x_high, y_low, y_high)
    tend, received = lax.optimization_barrier((tend, received))
    pay = jnp.transpose(received.reshape(owners_gx, 8, capacity), (1, 0, 2)).reshape(8, slots)
    flux_slots = owner_gather(state.reshape(4 * levels * cells_x, cells_y), pay)
    wall_flux = jnp.transpose(flux_slots.reshape(4, owners_gx, capacity), (1, 0, 2)).reshape(owners_gx, -1)
    wall_flux, pay, flux_slots = lax.optimization_barrier((wall_flux, pay, flux_slots))
    forcing = owner_scatter(pay, flux_slots, 4 * levels * cells_x, cells_y).reshape(state.shape)
    returned = lax.all_to_all(wall_flux, "gx", 0, 0, tiled=True)
    change = (tend - forcing) * (1.0 - solid.astype(jnp.float32))
    new_state = start + dt_step * change
    new_state, returned = lax.optimization_barrier((new_state, returned))
    returned = jnp.transpose(returned.reshape(owners_gx, 4, capacity), (1, 0, 2))
    through = jnp.einsum("cok,fk->cof", returned, rank_hot, precision=exact)
    facet_flux = jnp.sum(through * owner_float.T[None], axis=1)
    return (new_state, facet_flux)


def solution(mesh):
    in_specs = (
        P(None, None, "gx", "gy"),
        P(None, None, "gx", "gy"),
        P(None, "gx", "gy"),
        P(None, "gx", "gy"),
        P(None, ("gx", "gy")),
        P(("gx", "gy")),
        P(("gx", "gy")),
        P(("gx", "gy"), None),
        P(("gx", "gy")),
    )
    out_specs = (P(None, None, "gx", "gy"), P(None, ("gx", "gy")))
    return jax.shard_map(local, mesh=mesh, in_specs=in_specs, out_specs=out_specs, check_vma=False)
```

```python
import math

import jax
import jax.numpy as jnp
from jax import lax
from jax.experimental import pallas as pl
from jax.experimental.pallas import tpu as pltpu
from jax.sharding import PartitionSpec as P

dt_step = 0.2
exact = lax.Precision.HIGHEST


def _upwind(s, c):
    forward = (((((-2.0 * s(-3) + 15.0 * s(-2)) - 60.0 * s(-1)) + 20.0 * s(0)) + 30.0 * s(1)) - 3.0 * s(2))
    backward = (((((3.0 * s(-2) - 30.0 * s(-1)) - 20.0 * s(0)) + 60.0 * s(1)) - 15.0 * s(2)) + 2.0 * s(3))
    return jnp.where(c > 0, forward, backward) / 60.0


def _x_shifter(f, lo_rows, hi_rows):
    rows = f.shape[0]
    row = lax.broadcasted_iota(jnp.int32, f.shape, 0)
    width = len(lo_rows)
    lo_b = [jnp.broadcast_to(r, f.shape) for r in lo_rows]
    hi_b = [jnp.broadcast_to(r, f.shape) for r in hi_rows]
    cache = {0: f}

    def s(k):
        if k in cache:
            return cache[k]
        if k > 0:
            r = pltpu.roll(f, rows - k, 0)
            patch = hi_b[k - 1]
            for i in range(k - 2, -1, -1):
                patch = jnp.where(row == rows - k + i, hi_b[i], patch)
            out = jnp.where(row < rows - k, r, patch)
        else:
            m = -k
            r = pltpu.roll(f, m, 0)
            patch = lo_b[width - 1]
            for i in range(m - 1):
                patch = jnp.where(row == i, lo_b[width - m + i], patch)
            out = jnp.where(row >= m, r, patch)
        cache[k] = out
        return out
    return s


def _y_shifter(f, lo, hi):
    cols = f.shape[1]
    edge = lo.shape[1]
    lane = lax.broadcasted_iota(jnp.int32, lo.shape, 1)
    cache = {0: f}

    def s(k):
        if k in cache:
            return cache[k]
        if k > 0:
            r = pltpu.roll(f, cols - k, 1)
            patch = pltpu.roll(hi, edge - k, 1)
            last = jnp.where(lane >= edge - k, patch, r[:, cols - edge:])
            out = jnp.concatenate([r[:, :cols - edge], last], axis=1)
        else:
            m = -k
            r = pltpu.roll(f, m, 1)
            patch = pltpu.roll(lo, m, 1)
            first = jnp.where(lane < m, patch, r[:, :edge])
            out = jnp.concatenate([first, r[:, edge:]], axis=1)
        cache[k] = out
        return out
    return s


def stencil_kernel(sc_ref, sd_ref, su_ref, ec_ref, ed_ref, eu_ref, xl_ref, xh_ref, yl_ref, yh_ref, out_ref):
    level = pl.program_id(0)
    levels = pl.num_programs(0)
    fields = sc_ref.shape[0]
    width = (xl_ref.shape[1] - 1) // fields
    e = ec_ref[0]
    ed = ed_ref[0]
    eu = eu_ref[0]
    up_w = jnp.where(level < levels - 1, 1.0, 0.0)
    down_w = jnp.where(level > 0, 1.0, 0.0)
    eddy_up = (0.5 * (e + eu)) * up_w
    eddy_down = (0.5 * (ed + e)) * down_w
    ex = _x_shifter(e, [xl_ref[0, pl.ds(fields * width, 1), :]], [xh_ref[0, pl.ds(fields * width, 1), :]])
    ey = _y_shifter(e, yl_ref[fields, 0], yh_ref[fields, 0])
    east = 0.5 * (e + ex(1))
    west = 0.5 * (ex(-1) + e)
    north = 0.5 * (e + ey(1))
    south = 0.5 * (ey(-1) + e)
    u = sc_ref[0, 0]
    v = sc_ref[1, 0]
    w = sc_ref[2, 0]
    for f in range(fields):
        fv = sc_ref[f, 0]
        lower = sd_ref[f, 0]
        upper = su_ref[f, 0]
        sx = _x_shifter(fv, [xl_ref[0, pl.ds(f * width + i, 1), :] for i in range(width)],
                        [xh_ref[0, pl.ds(f * width + i, 1), :] for i in range(width)])
        sy = _y_shifter(fv, yl_ref[f, 0], yh_ref[f, 0])
        derx = _upwind(sx, u)
        dery = _upwind(sy, v)
        derz = (upper - lower) * 0.5
        zdiffuse = eddy_up * (upper - fv) - eddy_down * (fv - lower)
        advect = (u * derx + v * dery) + w * derz
        diff_x = east * (sx(1) - fv) - west * (fv - sx(-1))
        diff_y = north * (sy(1) - fv) - south * (fv - sy(-1))
        diffuse = (diff_x + diff_y) + zdiffuse
        out_ref[f, 0] = diffuse - advect


def stencil(state, eddy, xl, xh, yl, yh):
    fields, levels, cx, cy = state.shape
    w = xl.shape[1]
    nf = yl.shape[0]
    edge = yl.shape[3]
    below = lambda l: jnp.maximum(l - 1, 0)
    above = lambda l: jnp.minimum(l + 1, levels - 1)
    return pl.pallas_call(
        stencil_kernel,
        grid=(levels,),
        in_specs=[
            pl.BlockSpec((fields, 1, cx, cy), lambda l: (0, l, 0, 0)),
            pl.BlockSpec((fields, 1, cx, cy), lambda l: (0, below(l), 0, 0)),
            pl.BlockSpec((fields, 1, cx, cy), lambda l: (0, above(l), 0, 0)),
            pl.BlockSpec((1, cx, cy), lambda l: (l, 0, 0)),
            pl.BlockSpec((1, cx, cy), lambda l: (below(l), 0, 0)),
            pl.BlockSpec((1, cx, cy), lambda l: (above(l), 0, 0)),
            pl.BlockSpec((1, w, cy), lambda l: (l, 0, 0)),
            pl.BlockSpec((1, w, cy), lambda l: (l, 0, 0)),
            pl.BlockSpec((nf, 1, cx, edge), lambda l: (0, l, 0, 0)),
            pl.BlockSpec((nf, 1, cx, edge), lambda l: (0, l, 0, 0)),
        ],
        out_specs=pl.BlockSpec((fields, 1, cx, cy), lambda l: (0, l, 0, 0)),
        out_shape=jax.ShapeDtypeStruct((fields, levels, cx, cy), jnp.float32),
        compiler_params=pltpu.CompilerParams(dimension_semantics=("arbitrary",)),
        cost_estimate=pl.CostEstimate(flops=200 * fields * levels * cx * cy, transcendentals=0,
                                      bytes_accessed=4 * (4 * nf + fields) * levels * cx * cy),
    )(state, state, state, eddy, eddy, eddy, xl, xh, yl, yh)


def _pieces(x, n):
    out = []
    rest = x
    for _ in range(n):
        p = rest.astype(jnp.bfloat16)
        out.append(p)
        rest = rest - p.astype(jnp.float32)
    return out


def _one_hot(cell, cols, iota):
    sub = iota.shape[0]
    col = cell % cols
    hi = col // sub
    lo = (col % sub).astype(jnp.float32)
    hots = []
    for a in range(cols // sub):
        sel = jnp.where(hi == a, lo, -1.0).astype(jnp.bfloat16)
        hots.append(jnp.where(iota == sel, jnp.bfloat16(1), jnp.bfloat16(0)))
    return jnp.concatenate(hots, axis=0)


def gather_kernel(x_ref, pay_ref, flux_ref, pieces_ref, iota_ref):
    rows, cols = x_ref.shape
    fields = 4
    per_field = rows // fields
    block = pay_ref.shape[1]

    @pl.when(pl.program_id(0) == 0)
    def _():
        parts = _pieces(x_ref[...], 2)
        for i, p in enumerate(parts):
            pieces_ref[i * rows:(i + 1) * rows, :] = p
        iota_ref[...] = lax.broadcasted_iota(jnp.int32, iota_ref.shape, 0).astype(jnp.bfloat16)

    pay = pay_ref[...]
    cell = (pay[6:7] + 0.5).astype(jnp.int32)
    row = cell // cols
    hot = _one_hot(cell, cols, iota_ref[...])
    picked = jnp.dot(pieces_ref[...], hot, preferred_element_type=jnp.float32)
    value = picked[0:rows] + picked[rows:2 * rows]
    pick_row = lax.broadcasted_iota(jnp.int32, (per_field, block), 0) == row
    gathered = jnp.concatenate(
        [jnp.sum(jnp.where(pick_row, value[f * per_field:(f + 1) * per_field], 0.0), axis=0, keepdims=True)
         for f in range(fields)], axis=0)
    flux_ref[...] = pay[5:6] * (gathered - pay[0:4]) / pay[4:5]


def scatter_kernel(pay_ref, flux_ref, forcing_ref, iota_ref):
    rows, cols = forcing_ref.shape
    fields = 4
    per_field = rows // fields
    block = pay_ref.shape[1]

    @pl.when(pl.program_id(0) == 0)
    def _():
        forcing_ref[...] = jnp.zeros_like(forcing_ref)
        iota_ref[...] = lax.broadcasted_iota(jnp.int32, iota_ref.shape, 0).astype(jnp.bfloat16)

    pay = pay_ref[...]
    cell = (pay[6:7] + 0.5).astype(jnp.int32)
    row = cell // cols
    hot = _one_hot(cell, cols, iota_ref[...])
    flux = flux_ref[...]
    pick_row = lax.broadcasted_iota(jnp.int32, (per_field, block), 0) == row
    spread = jnp.concatenate(
        [jnp.where(pick_row, flux[f:f + 1], 0.0) for f in range(fields)], axis=0)
    w = jnp.concatenate(_pieces(spread, 2), axis=0)
    added = lax.dot_general(w, hot, (((1,), (1,)), ((), ())), preferred_element_type=jnp.float32)
    forcing_ref[...] += added[0:rows] + added[rows:2 * rows]


def owner_gather(x, pay, block=1024):
    rows, cols = x.shape
    slots = pay.shape[1]
    return pl.pallas_call(
        gather_kernel,
        grid=(slots // block,),
        in_specs=[
            pl.BlockSpec((rows, cols), lambda j: (0, 0)),
            pl.BlockSpec((8, block), lambda j: (0, j)),
        ],
        out_specs=pl.BlockSpec((4, block), lambda j: (0, j)),
        out_shape=jax.ShapeDtypeStruct((4, slots), jnp.float32),
        scratch_shapes=[pltpu.VMEM((2 * rows, cols), jnp.bfloat16),
                        pltpu.VMEM((256, block), jnp.bfloat16)],
        compiler_params=pltpu.CompilerParams(dimension_semantics=("arbitrary",),
                                             vmem_limit_bytes=48 * 1024 * 1024),
        cost_estimate=pl.CostEstimate(flops=2 * (2 * rows) * cols * slots, transcendentals=0,
                                      bytes_accessed=4 * (rows * cols + 12 * slots)),
    )(x, pay)


def owner_scatter(pay, flux, rows, cols, block=1024):
    slots = pay.shape[1]
    return pl.pallas_call(
        scatter_kernel,
        grid=(slots // block,),
        in_specs=[
            pl.BlockSpec((8, block), lambda j: (0, j)),
            pl.BlockSpec((4, block), lambda j: (0, j)),
        ],
        out_specs=pl.BlockSpec((rows, cols), lambda j: (0, 0)),
        out_shape=jax.ShapeDtypeStruct((rows, cols), jnp.float32),
        scratch_shapes=[pltpu.VMEM((256, block), jnp.bfloat16)],
        compiler_params=pltpu.CompilerParams(dimension_semantics=("arbitrary",),
                                             vmem_limit_bytes=48 * 1024 * 1024),
        cost_estimate=pl.CostEstimate(flops=rows * cols, transcendentals=0, bytes_accessed=4 * rows * cols),
    )(pay, flux)


def shift_pair(last, leading, axis):
    peers = lax.axis_size(axis)
    up = [(i, (i + 1) % peers) for i in range(peers)]
    down = [(j, i) for i, j in up]
    return lax.ppermute(last, axis, up), lax.ppermute(leading, axis, down)


def exchange(shard, axis, dim, low, high):
    peers = lax.axis_size(axis)
    length = shard.shape[dim]
    up = [(i, (i + 1) % peers) for i in range(peers)]
    down = [(j, i) for i, j in up]
    last = lax.slice_in_dim(shard, length - low, length, axis=dim)
    leading = lax.slice_in_dim(shard, 0, high, axis=dim)
    before = lax.ppermute(last, axis, up)
    after = lax.ppermute(leading, axis, down)
    return before, after


def local(state, start, eddy, solid, facet_wall, facet_dist, facet_area, facet_owner, facet_cell):
    levels = state.shape[1]
    cells_x = state.shape[2]
    cells_y = state.shape[3]
    width = 3
    edge = 128

    def x_rows(lo, hi):
        rows = jnp.transpose(state[:, :, lo:hi], (1, 0, 2, 3)).reshape(levels, -1, cells_y)
        return jnp.concatenate([rows, eddy[:, lo:hi][:, -1:] if lo else eddy[:, 0:1]], axis=1)

    x_last, x_first = x_rows(cells_x - width, cells_x), x_rows(0, width)
    x_low, x_high = shift_pair(x_last, x_first, "gx")

    facet_count = facet_cell.shape[0]
    owners_gx = lax.axis_size("gx")
    capacity = 2 * facet_count // owners_gx
    slots = owners_gx * capacity
    owner_gx = facet_owner[:, 0]
    owner_hot = (owner_gx[:, None] == jnp.arange(owners_gx, dtype=jnp.int32)[None, :]).astype(
        jnp.bfloat16
    )
    positions = jnp.arange(facet_count, dtype=jnp.int32)
    earlier = (positions[:, None] > positions[None, :]).astype(jnp.bfloat16)
    before = jnp.dot(earlier, owner_hot, preferred_element_type=jnp.float32)
    owner_float = owner_hot.astype(jnp.float32)
    slot_rank = jnp.sum(before * owner_float, axis=1)
    rank_hot = (slot_rank[:, None] == jnp.arange(capacity, dtype=jnp.float32)[None, :]).astype(
        jnp.float32
    )
    payload = jnp.concatenate(
        [facet_wall, facet_dist[None], facet_area[None], facet_cell[None].astype(jnp.float32)],
        axis=0,
    )
    spread = payload[:, None, :] * owner_float.T[None]
    outgoing = jnp.einsum("cof,fk->cok", spread, rank_hot, precision=exact)
    filled = jnp.dot(owner_float.T, rank_hot, precision=exact)
    unit_dist = (jnp.arange(7, dtype=jnp.int32) == 4).astype(jnp.float32)[:, None, None]
    outgoing = outgoing + unit_dist * (1.0 - filled)[None]
    outgoing = jnp.concatenate([outgoing, jnp.zeros((1, owners_gx, capacity), jnp.float32)], axis=0)
    outgoing = jnp.transpose(outgoing, (1, 0, 2)).reshape(owners_gx, -1)
    outgoing, y_state, y_eddy = lax.optimization_barrier((outgoing, state, eddy))

    def y_cols(lo, hi, one):
        return jnp.concatenate([y_state[..., lo:hi].reshape(-1), y_eddy[..., one:one + 1].reshape(-1)])

    def y_tile(flat, lanes, one):
        fields_part = flat[: 4 * levels * cells_x * width].reshape(4, levels, cells_x, width)
        eddy_part = flat[4 * levels * cells_x * width:].reshape(1, levels, cells_x, 1)
        pad_f = ((0, 0), (0, 0), (0, 0), (lanes, edge - width - lanes))
        pad_e = ((0, 0), (0, 0), (0, 0), (one, edge - 1 - one))
        return jnp.concatenate([jnp.pad(fields_part, pad_f), jnp.pad(eddy_part, pad_e)], axis=0)

    y_low, y_high = shift_pair(
        y_cols(cells_y - width, cells_y, cells_y - 1), y_cols(0, width, 0), "gy"
    )
    y_low = y_tile(y_low, edge - width, edge - 1)
    y_high = y_tile(y_high, 0, 0)
    received = lax.all_to_all(outgoing, "gx", 0, 0, tiled=True)
    tend = stencil(state, eddy, x_low, x_high, y_low, y_high)
    tend, received = lax.optimization_barrier((tend, received))
    pay = jnp.transpose(received.reshape(owners_gx, 8, capacity), (1, 0, 2)).reshape(8, slots)
    flux_slots = owner_gather(state.reshape(4 * levels * cells_x, cells_y), pay)
    wall_flux = jnp.transpose(flux_slots.reshape(4, owners_gx, capacity), (1, 0, 2)).reshape(owners_gx, -1)
    wall_flux, pay, flux_slots = lax.optimization_barrier((wall_flux, pay, flux_slots))
    forcing = owner_scatter(pay, flux_slots, 4 * levels * cells_x, cells_y).reshape(state.shape)
    returned = lax.all_to_all(wall_flux, "gx", 0, 0, tiled=True)
    change = (tend - forcing) * (1.0 - solid.astype(jnp.float32))
    new_state = start + dt_step * change
    new_state, returned = lax.optimization_barrier((new_state, returned))
    returned = jnp.transpose(returned.reshape(owners_gx, 4, capacity), (1, 0, 2))
    through = jnp.einsum("cok,fk->cof", returned, rank_hot, precision=exact)
    facet_flux = jnp.sum(through * owner_float.T[None], axis=1)
    return (new_state, facet_flux)


def solution(mesh):
    in_specs = (
        P(None, None, "gx", "gy"),
        P(None, None, "gx", "gy"),
        P(None, "gx", "gy"),
        P(None, "gx", "gy"),
        P(None, ("gx", "gy")),
        P(("gx", "gy")),
        P(("gx", "gy")),
        P(("gx", "gy"), None),
        P(("gx", "gy")),
    )
    out_specs = (P(None, None, "gx", "gy"), P(None, ("gx", "gy")))
    return jax.shard_map(local, mesh=mesh, in_specs=in_specs, out_specs=out_specs, check_vma=False)
```

```python
import math

import jax
import jax.numpy as jnp
from jax import lax
from jax.experimental import pallas as pl
from jax.experimental.pallas import tpu as pltpu
from jax.sharding import PartitionSpec as P

dt_step = 0.2
exact = lax.Precision.HIGHEST


def _upwind(s, c):
    forward = (((((-2.0 * s(-3) + 15.0 * s(-2)) - 60.0 * s(-1)) + 20.0 * s(0)) + 30.0 * s(1)) - 3.0 * s(2))
    backward = (((((3.0 * s(-2) - 30.0 * s(-1)) - 20.0 * s(0)) + 60.0 * s(1)) - 15.0 * s(2)) + 2.0 * s(3))
    return jnp.where(c > 0, forward, backward) / 60.0


def _x_shifter(f, lo_rows, hi_rows):
    rows = f.shape[0]
    row = lax.broadcasted_iota(jnp.int32, f.shape, 0)
    width = len(lo_rows)
    lo_b = [jnp.broadcast_to(r, f.shape) for r in lo_rows]
    hi_b = [jnp.broadcast_to(r, f.shape) for r in hi_rows]
    cache = {0: f}

    def s(k):
        if k in cache:
            return cache[k]
        if k > 0:
            r = pltpu.roll(f, rows - k, 0)
            patch = hi_b[k - 1]
            for i in range(k - 2, -1, -1):
                patch = jnp.where(row == rows - k + i, hi_b[i], patch)
            out = jnp.where(row < rows - k, r, patch)
        else:
            m = -k
            r = pltpu.roll(f, m, 0)
            patch = lo_b[width - 1]
            for i in range(m - 1):
                patch = jnp.where(row == i, lo_b[width - m + i], patch)
            out = jnp.where(row >= m, r, patch)
        cache[k] = out
        return out
    return s


def _y_shifter(f, lo, hi):
    cols = f.shape[1]
    edge = lo.shape[1]
    lane = lax.broadcasted_iota(jnp.int32, lo.shape, 1)
    cache = {0: f}

    def s(k):
        if k in cache:
            return cache[k]
        if k > 0:
            r = pltpu.roll(f, cols - k, 1)
            patch = pltpu.roll(hi, edge - k, 1)
            last = jnp.where(lane >= edge - k, patch, r[:, cols - edge:])
            out = jnp.concatenate([r[:, :cols - edge], last], axis=1)
        else:
            m = -k
            r = pltpu.roll(f, m, 1)
            patch = pltpu.roll(lo, m, 1)
            first = jnp.where(lane < m, patch, r[:, :edge])
            out = jnp.concatenate([first, r[:, edge:]], axis=1)
        cache[k] = out
        return out
    return s


def stencil_kernel(sc_ref, sd_ref, su_ref, ec_ref, ed_ref, eu_ref, xl_ref, xh_ref, yl_ref, yh_ref, out_ref):
    level = pl.program_id(0)
    levels = pl.num_programs(0)
    fields = sc_ref.shape[0]
    width = (xl_ref.shape[1] - 1) // fields
    e = ec_ref[0]
    ed = ed_ref[0]
    eu = eu_ref[0]
    up_w = jnp.where(level < levels - 1, 1.0, 0.0)
    down_w = jnp.where(level > 0, 1.0, 0.0)
    eddy_up = (0.5 * (e + eu)) * up_w
    eddy_down = (0.5 * (ed + e)) * down_w
    ex = _x_shifter(e, [xl_ref[0, pl.ds(fields * width, 1), :]], [xh_ref[0, pl.ds(fields * width, 1), :]])
    ey = _y_shifter(e, yl_ref[fields, 0], yh_ref[fields, 0])
    east = 0.5 * (e + ex(1))
    west = 0.5 * (ex(-1) + e)
    north = 0.5 * (e + ey(1))
    south = 0.5 * (ey(-1) + e)
    u = sc_ref[0, 0]
    v = sc_ref[1, 0]
    w = sc_ref[2, 0]
    for f in range(fields):
        fv = sc_ref[f, 0]
        lower = sd_ref[f, 0]
        upper = su_ref[f, 0]
        sx = _x_shifter(fv, [xl_ref[0, pl.ds(f * width + i, 1), :] for i in range(width)],
                        [xh_ref[0, pl.ds(f * width + i, 1), :] for i in range(width)])
        sy = _y_shifter(fv, yl_ref[f, 0], yh_ref[f, 0])
        derx = _upwind(sx, u)
        dery = _upwind(sy, v)
        derz = (upper - lower) * 0.5
        zdiffuse = eddy_up * (upper - fv) - eddy_down * (fv - lower)
        advect = (u * derx + v * dery) + w * derz
        diff_x = east * (sx(1) - fv) - west * (fv - sx(-1))
        diff_y = north * (sy(1) - fv) - south * (fv - sy(-1))
        diffuse = (diff_x + diff_y) + zdiffuse
        out_ref[f, 0] = diffuse - advect


def stencil(state, eddy, xl, xh, yl, yh):
    fields, levels, cx, cy = state.shape
    w = xl.shape[1]
    nf = yl.shape[0]
    edge = yl.shape[3]
    below = lambda l: jnp.maximum(l - 1, 0)
    above = lambda l: jnp.minimum(l + 1, levels - 1)
    return pl.pallas_call(
        stencil_kernel,
        grid=(levels,),
        in_specs=[
            pl.BlockSpec((fields, 1, cx, cy), lambda l: (0, l, 0, 0)),
            pl.BlockSpec((fields, 1, cx, cy), lambda l: (0, below(l), 0, 0)),
            pl.BlockSpec((fields, 1, cx, cy), lambda l: (0, above(l), 0, 0)),
            pl.BlockSpec((1, cx, cy), lambda l: (l, 0, 0)),
            pl.BlockSpec((1, cx, cy), lambda l: (below(l), 0, 0)),
            pl.BlockSpec((1, cx, cy), lambda l: (above(l), 0, 0)),
            pl.BlockSpec((1, w, cy), lambda l: (l, 0, 0)),
            pl.BlockSpec((1, w, cy), lambda l: (l, 0, 0)),
            pl.BlockSpec((nf, 1, cx, edge), lambda l: (0, l, 0, 0)),
            pl.BlockSpec((nf, 1, cx, edge), lambda l: (0, l, 0, 0)),
        ],
        out_specs=pl.BlockSpec((fields, 1, cx, cy), lambda l: (0, l, 0, 0)),
        out_shape=jax.ShapeDtypeStruct((fields, levels, cx, cy), jnp.float32),
        compiler_params=pltpu.CompilerParams(dimension_semantics=("arbitrary",)),
        cost_estimate=pl.CostEstimate(flops=200 * fields * levels * cx * cy, transcendentals=0,
                                      bytes_accessed=4 * (4 * nf + fields) * levels * cx * cy),
    )(state, state, state, eddy, eddy, eddy, xl, xh, yl, yh)


def _pieces(x, n):
    out = []
    rest = x
    for _ in range(n):
        p = rest.astype(jnp.bfloat16)
        out.append(p)
        rest = rest - p.astype(jnp.float32)
    return out


def _one_hot(cell, cols, iota):
    sub = iota.shape[0]
    col = cell % cols
    hi = col // sub
    lo = (col % sub).astype(jnp.float32)
    hots = []
    for a in range(cols // sub):
        sel = jnp.where(hi == a, lo, -1.0).astype(jnp.bfloat16)
        hots.append(jnp.where(iota == sel, jnp.bfloat16(1), jnp.bfloat16(0)))
    return jnp.concatenate(hots, axis=0)


def gather_kernel(x_ref, pay_ref, flux_ref, pieces_ref, iota_ref):
    rows, cols = x_ref.shape
    fields = 4
    per_field = rows // fields
    block = pay_ref.shape[1]

    @pl.when(pl.program_id(0) == 0)
    def _():
        parts = _pieces(x_ref[...], 2)
        for i, p in enumerate(parts):
            pieces_ref[i * rows:(i + 1) * rows, :] = p
        iota_ref[...] = lax.broadcasted_iota(jnp.int32, iota_ref.shape, 0).astype(jnp.bfloat16)

    pay = pay_ref[...]
    cell = (pay[6:7] + 0.5).astype(jnp.int32)
    row = cell // cols
    hot = _one_hot(cell, cols, iota_ref[...])
    picked = jnp.dot(pieces_ref[...], hot, preferred_element_type=jnp.float32)
    value = picked[0:rows] + picked[rows:2 * rows]
    pick_row = lax.broadcasted_iota(jnp.int32, (per_field, block), 0) == row
    gathered = jnp.concatenate(
        [jnp.sum(jnp.where(pick_row, value[f * per_field:(f + 1) * per_field], 0.0), axis=0, keepdims=True)
         for f in range(fields)], axis=0)
    flux_ref[...] = pay[5:6] * (gathered - pay[0:4]) / pay[4:5]


def scatter_kernel(pay_ref, flux_ref, forcing_ref, iota_ref):
    rows, cols = forcing_ref.shape
    fields = 4
    per_field = rows // fields
    block = pay_ref.shape[1]

    @pl.when(pl.program_id(0) == 0)
    def _():
        forcing_ref[...] = jnp.zeros_like(forcing_ref)
        iota_ref[...] = lax.broadcasted_iota(jnp.int32, iota_ref.shape, 0).astype(jnp.bfloat16)

    pay = pay_ref[...]
    cell = (pay[6:7] + 0.5).astype(jnp.int32)
    row = cell // cols
    hot = _one_hot(cell, cols, iota_ref[...])
    flux = flux_ref[...]
    pick_row = lax.broadcasted_iota(jnp.int32, (per_field, block), 0) == row
    spread = jnp.concatenate(
        [jnp.where(pick_row, flux[f:f + 1], 0.0) for f in range(fields)], axis=0)
    w = jnp.concatenate(_pieces(spread, 2), axis=0)
    added = lax.dot_general(w, hot, (((1,), (1,)), ((), ())), preferred_element_type=jnp.float32)
    forcing_ref[...] += added[0:rows] + added[rows:2 * rows]


def owner_gather(x, pay, block=1024):
    rows, cols = x.shape
    slots = pay.shape[1]
    return pl.pallas_call(
        gather_kernel,
        grid=(slots // block,),
        in_specs=[
            pl.BlockSpec((rows, cols), lambda j: (0, 0)),
            pl.BlockSpec((8, block), lambda j: (0, j)),
        ],
        out_specs=pl.BlockSpec((4, block), lambda j: (0, j)),
        out_shape=jax.ShapeDtypeStruct((4, slots), jnp.float32),
        scratch_shapes=[pltpu.VMEM((2 * rows, cols), jnp.bfloat16),
                        pltpu.VMEM((256, block), jnp.bfloat16)],
        compiler_params=pltpu.CompilerParams(dimension_semantics=("arbitrary",),
                                             vmem_limit_bytes=48 * 1024 * 1024),
        cost_estimate=pl.CostEstimate(flops=2 * (2 * rows) * cols * slots, transcendentals=0,
                                      bytes_accessed=4 * (rows * cols + 12 * slots)),
    )(x, pay)


def owner_scatter(pay, flux, rows, cols, block=1024):
    slots = pay.shape[1]
    return pl.pallas_call(
        scatter_kernel,
        grid=(slots // block,),
        in_specs=[
            pl.BlockSpec((8, block), lambda j: (0, j)),
            pl.BlockSpec((4, block), lambda j: (0, j)),
        ],
        out_specs=pl.BlockSpec((rows, cols), lambda j: (0, 0)),
        out_shape=jax.ShapeDtypeStruct((rows, cols), jnp.float32),
        scratch_shapes=[pltpu.VMEM((256, block), jnp.bfloat16)],
        compiler_params=pltpu.CompilerParams(dimension_semantics=("arbitrary",),
                                             vmem_limit_bytes=48 * 1024 * 1024),
        cost_estimate=pl.CostEstimate(flops=rows * cols, transcendentals=0, bytes_accessed=4 * rows * cols),
    )(pay, flux)


def shift_pair(last, leading, axis):
    peers = lax.axis_size(axis)
    up = [(i, (i + 1) % peers) for i in range(peers)]
    down = [(j, i) for i, j in up]
    return lax.ppermute(last, axis, up), lax.ppermute(leading, axis, down)


def exchange(shard, axis, dim, low, high):
    peers = lax.axis_size(axis)
    length = shard.shape[dim]
    up = [(i, (i + 1) % peers) for i in range(peers)]
    down = [(j, i) for i, j in up]
    last = lax.slice_in_dim(shard, length - low, length, axis=dim)
    leading = lax.slice_in_dim(shard, 0, high, axis=dim)
    before = lax.ppermute(last, axis, up)
    after = lax.ppermute(leading, axis, down)
    return before, after


def local(state, start, eddy, solid, facet_wall, facet_dist, facet_area, facet_owner, facet_cell):
    levels = state.shape[1]
    cells_x = state.shape[2]
    cells_y = state.shape[3]
    width = 3
    edge = 128

    def x_rows(lo, hi):
        rows = jnp.transpose(state[:, :, lo:hi], (1, 0, 2, 3)).reshape(levels, -1, cells_y)
        return jnp.concatenate([rows, eddy[:, lo:hi][:, -1:] if lo else eddy[:, 0:1]], axis=1)

    x_last, x_first = x_rows(cells_x - width, cells_x), x_rows(0, width)
    x_last, x_first, y_state, y_eddy = lax.optimization_barrier((x_last, x_first, state, eddy))
    x_low, x_high = shift_pair(x_last, x_first, "gx")

    def y_cols(lo, hi, one):
        return jnp.concatenate([y_state[..., lo:hi].reshape(-1), y_eddy[..., one:one + 1].reshape(-1)])

    def y_tile(flat, lanes, one):
        fields_part = flat[: 4 * levels * cells_x * width].reshape(4, levels, cells_x, width)
        eddy_part = flat[4 * levels * cells_x * width:].reshape(1, levels, cells_x, 1)
        pad_f = ((0, 0), (0, 0), (0, 0), (lanes, edge - width - lanes))
        pad_e = ((0, 0), (0, 0), (0, 0), (one, edge - 1 - one))
        return jnp.concatenate([jnp.pad(fields_part, pad_f), jnp.pad(eddy_part, pad_e)], axis=0)

    y_last, y_first = y_cols(cells_y - width, cells_y, cells_y - 1), y_cols(0, width, 0)
    y_last, y_first, facet_wall, facet_dist, facet_area, facet_owner, facet_cell = lax.optimization_barrier(
        (y_last, y_first, facet_wall, facet_dist, facet_area, facet_owner, facet_cell)
    )
    y_low, y_high = shift_pair(y_last, y_first, "gy")
    y_low = y_tile(y_low, edge - width, edge - 1)
    y_high = y_tile(y_high, 0, 0)

    facet_count = facet_cell.shape[0]
    owners_gx = lax.axis_size("gx")
    capacity = 2 * facet_count // owners_gx
    slots = owners_gx * capacity
    owner_gx = facet_owner[:, 0]
    owner_hot = (owner_gx[:, None] == jnp.arange(owners_gx, dtype=jnp.int32)[None, :]).astype(
        jnp.bfloat16
    )
    positions = jnp.arange(facet_count, dtype=jnp.int32)
    earlier = (positions[:, None] > positions[None, :]).astype(jnp.bfloat16)
    before = jnp.dot(earlier, owner_hot, preferred_element_type=jnp.float32)
    owner_float = owner_hot.astype(jnp.float32)
    slot_rank = jnp.sum(before * owner_float, axis=1)
    rank_hot = (slot_rank[:, None] == jnp.arange(capacity, dtype=jnp.float32)[None, :]).astype(
        jnp.float32
    )
    payload = jnp.concatenate(
        [facet_wall, facet_dist[None], facet_area[None], facet_cell[None].astype(jnp.float32)],
        axis=0,
    )
    spread = payload[:, None, :] * owner_float.T[None]
    outgoing = jnp.einsum("cof,fk->cok", spread, rank_hot, precision=exact)
    filled = jnp.dot(owner_float.T, rank_hot, precision=exact)
    unit_dist = (jnp.arange(7, dtype=jnp.int32) == 4).astype(jnp.float32)[:, None, None]
    outgoing = outgoing + unit_dist * (1.0 - filled)[None]
    outgoing = jnp.concatenate([outgoing, jnp.zeros((1, owners_gx, capacity), jnp.float32)], axis=0)
    outgoing = jnp.transpose(outgoing, (1, 0, 2)).reshape(owners_gx, -1)
    x_low, x_high, y_low, y_high, outgoing = lax.optimization_barrier(
        (x_low, x_high, y_low, y_high, outgoing)
    )
    received = lax.all_to_all(outgoing, "gx", 0, 0, tiled=True)
    tend = stencil(state, eddy, x_low, x_high, y_low, y_high)
    tend, received = lax.optimization_barrier((tend, received))
    pay = jnp.transpose(received.reshape(owners_gx, 8, capacity), (1, 0, 2)).reshape(8, slots)
    flux_slots = owner_gather(state.reshape(4 * levels * cells_x, cells_y), pay)
    wall_flux = jnp.transpose(flux_slots.reshape(4, owners_gx, capacity), (1, 0, 2)).reshape(owners_gx, -1)
    wall_flux, pay, flux_slots = lax.optimization_barrier((wall_flux, pay, flux_slots))
    forcing = owner_scatter(pay, flux_slots, 4 * levels * cells_x, cells_y).reshape(state.shape)
    returned = lax.all_to_all(wall_flux, "gx", 0, 0, tiled=True)
    change = (tend - forcing) * (1.0 - solid.astype(jnp.float32))
    new_state = start + dt_step * change
    new_state, returned = lax.optimization_barrier((new_state, returned))
    returned = jnp.transpose(returned.reshape(owners_gx, 4, capacity), (1, 0, 2))
    through = jnp.einsum("cok,fk->cof", returned, rank_hot, precision=exact)
    facet_flux = jnp.sum(through * owner_float.T[None], axis=1)
    return (new_state, facet_flux)


def solution(mesh):
    in_specs = (
        P(None, None, "gx", "gy"),
        P(None, None, "gx", "gy"),
        P(None, "gx", "gy"),
        P(None, "gx", "gy"),
        P(None, ("gx", "gy")),
        P(("gx", "gy")),
        P(("gx", "gy")),
        P(("gx", "gy"), None),
        P(("gx", "gy")),
    )
    out_specs = (P(None, None, "gx", "gy"), P(None, ("gx", "gy")))
    return jax.shard_map(local, mesh=mesh, in_specs=in_specs, out_specs=out_specs, check_vma=False)
```

```python
import math

import jax
import jax.numpy as jnp
from jax import lax
from jax.experimental import pallas as pl
from jax.experimental.pallas import tpu as pltpu
from jax.sharding import PartitionSpec as P

dt_step = 0.2
exact = lax.Precision.HIGHEST


def _upwind(s, c):
    forward = (((((-2.0 * s(-3) + 15.0 * s(-2)) - 60.0 * s(-1)) + 20.0 * s(0)) + 30.0 * s(1)) - 3.0 * s(2))
    backward = (((((3.0 * s(-2) - 30.0 * s(-1)) - 20.0 * s(0)) + 60.0 * s(1)) - 15.0 * s(2)) + 2.0 * s(3))
    return jnp.where(c > 0, forward, backward) / 60.0


def _x_shifter(f, lo_rows, hi_rows):
    rows = f.shape[0]
    row = lax.broadcasted_iota(jnp.int32, f.shape, 0)
    width = len(lo_rows)
    lo_b = [jnp.broadcast_to(r, f.shape) for r in lo_rows]
    hi_b = [jnp.broadcast_to(r, f.shape) for r in hi_rows]
    cache = {0: f}

    def s(k):
        if k in cache:
            return cache[k]
        if k > 0:
            r = pltpu.roll(f, rows - k, 0)
            patch = hi_b[k - 1]
            for i in range(k - 2, -1, -1):
                patch = jnp.where(row == rows - k + i, hi_b[i], patch)
            out = jnp.where(row < rows - k, r, patch)
        else:
            m = -k
            r = pltpu.roll(f, m, 0)
            patch = lo_b[width - 1]
            for i in range(m - 1):
                patch = jnp.where(row == i, lo_b[width - m + i], patch)
            out = jnp.where(row >= m, r, patch)
        cache[k] = out
        return out
    return s


def _y_shifter(f, lo, hi):
    cols = f.shape[1]
    edge = lo.shape[1]
    lane = lax.broadcasted_iota(jnp.int32, lo.shape, 1)
    cache = {0: f}

    def s(k):
        if k in cache:
            return cache[k]
        if k > 0:
            r = pltpu.roll(f, cols - k, 1)
            patch = pltpu.roll(hi, edge - k, 1)
            last = jnp.where(lane >= edge - k, patch, r[:, cols - edge:])
            out = jnp.concatenate([r[:, :cols - edge], last], axis=1)
        else:
            m = -k
            r = pltpu.roll(f, m, 1)
            patch = pltpu.roll(lo, m, 1)
            first = jnp.where(lane < m, patch, r[:, :edge])
            out = jnp.concatenate([first, r[:, edge:]], axis=1)
        cache[k] = out
        return out
    return s


def stencil_kernel(sc_ref, sd_ref, su_ref, ec_ref, ed_ref, eu_ref, xl_ref, xh_ref, yl_ref, yh_ref, out_ref):
    level = pl.program_id(0)
    levels = pl.num_programs(0)
    fields = sc_ref.shape[0]
    width = (xl_ref.shape[1] - 1) // fields
    e = ec_ref[0]
    ed = ed_ref[0]
    eu = eu_ref[0]
    up_w = jnp.where(level < levels - 1, 1.0, 0.0)
    down_w = jnp.where(level > 0, 1.0, 0.0)
    eddy_up = (0.5 * (e + eu)) * up_w
    eddy_down = (0.5 * (ed + e)) * down_w
    ex = _x_shifter(e, [xl_ref[0, pl.ds(fields * width, 1), :]], [xh_ref[0, pl.ds(fields * width, 1), :]])
    ey = _y_shifter(e, yl_ref[fields, 0], yh_ref[fields, 0])
    east = 0.5 * (e + ex(1))
    west = 0.5 * (ex(-1) + e)
    north = 0.5 * (e + ey(1))
    south = 0.5 * (ey(-1) + e)
    u = sc_ref[0, 0]
    v = sc_ref[1, 0]
    w = sc_ref[2, 0]
    for f in range(fields):
        fv = sc_ref[f, 0]
        lower = sd_ref[f, 0]
        upper = su_ref[f, 0]
        sx = _x_shifter(fv, [xl_ref[0, pl.ds(f * width + i, 1), :] for i in range(width)],
                        [xh_ref[0, pl.ds(f * width + i, 1), :] for i in range(width)])
        sy = _y_shifter(fv, yl_ref[f, 0], yh_ref[f, 0])
        derx = _upwind(sx, u)
        dery = _upwind(sy, v)
        derz = (upper - lower) * 0.5
        zdiffuse = eddy_up * (upper - fv) - eddy_down * (fv - lower)
        advect = (u * derx + v * dery) + w * derz
        diff_x = east * (sx(1) - fv) - west * (fv - sx(-1))
        diff_y = north * (sy(1) - fv) - south * (fv - sy(-1))
        diffuse = (diff_x + diff_y) + zdiffuse
        out_ref[f, 0] = diffuse - advect


def stencil(state, eddy, xl, xh, yl, yh):
    fields, levels, cx, cy = state.shape
    w = xl.shape[1]
    nf = yl.shape[0]
    edge = yl.shape[3]
    below = lambda l: jnp.maximum(l - 1, 0)
    above = lambda l: jnp.minimum(l + 1, levels - 1)
    return pl.pallas_call(
        stencil_kernel,
        grid=(levels,),
        in_specs=[
            pl.BlockSpec((fields, 1, cx, cy), lambda l: (0, l, 0, 0)),
            pl.BlockSpec((fields, 1, cx, cy), lambda l: (0, below(l), 0, 0)),
            pl.BlockSpec((fields, 1, cx, cy), lambda l: (0, above(l), 0, 0)),
            pl.BlockSpec((1, cx, cy), lambda l: (l, 0, 0)),
            pl.BlockSpec((1, cx, cy), lambda l: (below(l), 0, 0)),
            pl.BlockSpec((1, cx, cy), lambda l: (above(l), 0, 0)),
            pl.BlockSpec((1, w, cy), lambda l: (l, 0, 0)),
            pl.BlockSpec((1, w, cy), lambda l: (l, 0, 0)),
            pl.BlockSpec((nf, 1, cx, edge), lambda l: (0, l, 0, 0)),
            pl.BlockSpec((nf, 1, cx, edge), lambda l: (0, l, 0, 0)),
        ],
        out_specs=pl.BlockSpec((fields, 1, cx, cy), lambda l: (0, l, 0, 0)),
        out_shape=jax.ShapeDtypeStruct((fields, levels, cx, cy), jnp.float32),
        compiler_params=pltpu.CompilerParams(dimension_semantics=("arbitrary",)),
        cost_estimate=pl.CostEstimate(flops=200 * fields * levels * cx * cy, transcendentals=0,
                                      bytes_accessed=4 * (4 * nf + fields) * levels * cx * cy),
    )(state, state, state, eddy, eddy, eddy, xl, xh, yl, yh)


def _pieces(x, n):
    out = []
    rest = x
    for _ in range(n):
        p = rest.astype(jnp.bfloat16)
        out.append(p)
        rest = rest - p.astype(jnp.float32)
    return out


def _one_hot(cell, cols, iota):
    sub = iota.shape[0]
    col = cell % cols
    hi = col // sub
    lo = (col % sub).astype(jnp.float32)
    hots = []
    for a in range(cols // sub):
        sel = jnp.where(hi == a, lo, -1.0).astype(jnp.bfloat16)
        hots.append(jnp.where(iota == sel, jnp.bfloat16(1), jnp.bfloat16(0)))
    return jnp.concatenate(hots, axis=0)


def gather_kernel(x_ref, pay_ref, flux_ref, pieces_ref, iota_ref):
    rows, cols = x_ref.shape
    fields = 4
    per_field = rows // fields
    block = pay_ref.shape[1]

    @pl.when(pl.program_id(0) == 0)
    def _():
        parts = _pieces(x_ref[...], 2)
        for i, p in enumerate(parts):
            pieces_ref[i * rows:(i + 1) * rows, :] = p
        iota_ref[...] = lax.broadcasted_iota(jnp.int32, iota_ref.shape, 0).astype(jnp.bfloat16)

    pay = pay_ref[...]
    cell = (pay[6:7] + 0.5).astype(jnp.int32)
    row = cell // cols
    hot = _one_hot(cell, cols, iota_ref[...])
    picked = jnp.dot(pieces_ref[...], hot, preferred_element_type=jnp.float32)
    value = picked[0:rows] + picked[rows:2 * rows]
    pick_row = lax.broadcasted_iota(jnp.int32, (per_field, block), 0) == row
    gathered = jnp.concatenate(
        [jnp.sum(jnp.where(pick_row, value[f * per_field:(f + 1) * per_field], 0.0), axis=0, keepdims=True)
         for f in range(fields)], axis=0)
    flux_ref[...] = pay[5:6] * (gathered - pay[0:4]) / pay[4:5]


def scatter_kernel(pay_ref, flux_ref, forcing_ref, iota_ref):
    rows, cols = forcing_ref.shape
    fields = 4
    per_field = rows // fields
    block = pay_ref.shape[1]

    @pl.when(pl.program_id(0) == 0)
    def _():
        forcing_ref[...] = jnp.zeros_like(forcing_ref)
        iota_ref[...] = lax.broadcasted_iota(jnp.int32, iota_ref.shape, 0).astype(jnp.bfloat16)

    pay = pay_ref[...]
    cell = (pay[6:7] + 0.5).astype(jnp.int32)
    row = cell // cols
    hot = _one_hot(cell, cols, iota_ref[...])
    flux = flux_ref[...]
    pick_row = lax.broadcasted_iota(jnp.int32, (per_field, block), 0) == row
    spread = jnp.concatenate(
        [jnp.where(pick_row, flux[f:f + 1], 0.0) for f in range(fields)], axis=0)
    w = jnp.concatenate(_pieces(spread, 2), axis=0)
    added = lax.dot_general(w, hot, (((1,), (1,)), ((), ())), preferred_element_type=jnp.float32)
    forcing_ref[...] += added[0:rows] + added[rows:2 * rows]


def owner_gather(x, pay, block=1024):
    rows, cols = x.shape
    slots = pay.shape[1]
    return pl.pallas_call(
        gather_kernel,
        grid=(slots // block,),
        in_specs=[
            pl.BlockSpec((rows, cols), lambda j: (0, 0)),
            pl.BlockSpec((8, block), lambda j: (0, j)),
        ],
        out_specs=pl.BlockSpec((4, block), lambda j: (0, j)),
        out_shape=jax.ShapeDtypeStruct((4, slots), jnp.float32),
        scratch_shapes=[pltpu.VMEM((2 * rows, cols), jnp.bfloat16),
                        pltpu.VMEM((256, block), jnp.bfloat16)],
        compiler_params=pltpu.CompilerParams(dimension_semantics=("arbitrary",),
                                             vmem_limit_bytes=48 * 1024 * 1024),
        cost_estimate=pl.CostEstimate(flops=2 * (2 * rows) * cols * slots, transcendentals=0,
                                      bytes_accessed=4 * (rows * cols + 12 * slots)),
    )(x, pay)


def owner_scatter(pay, flux, rows, cols, block=1024):
    slots = pay.shape[1]
    return pl.pallas_call(
        scatter_kernel,
        grid=(slots // block,),
        in_specs=[
            pl.BlockSpec((8, block), lambda j: (0, j)),
            pl.BlockSpec((4, block), lambda j: (0, j)),
        ],
        out_specs=pl.BlockSpec((rows, cols), lambda j: (0, 0)),
        out_shape=jax.ShapeDtypeStruct((rows, cols), jnp.float32),
        scratch_shapes=[pltpu.VMEM((256, block), jnp.bfloat16)],
        compiler_params=pltpu.CompilerParams(dimension_semantics=("arbitrary",),
                                             vmem_limit_bytes=48 * 1024 * 1024),
        cost_estimate=pl.CostEstimate(flops=rows * cols, transcendentals=0, bytes_accessed=4 * rows * cols),
    )(pay, flux)


def swap_edges(last, leading, axis):
    peers = lax.axis_size(axis)
    me = lax.axis_index(axis)
    target = lax.broadcasted_iota(jnp.int32, (peers, 1), 0)
    blocks = jnp.where(
        target == (me + 1) % peers,
        last[None],
        jnp.where(target == (me + peers - 1) % peers, leading[None], jnp.zeros_like(last)[None]),
    )
    got = lax.all_to_all(blocks, axis, 0, 0, tiled=True)
    below = lax.dynamic_index_in_dim(got, (me + peers - 1) % peers, 0, keepdims=False)
    above = lax.dynamic_index_in_dim(got, (me + 1) % peers, 0, keepdims=False)
    return below, above


def shift_pair(last, leading, axis):
    peers = lax.axis_size(axis)
    up = [(i, (i + 1) % peers) for i in range(peers)]
    down = [(j, i) for i, j in up]
    return lax.ppermute(last, axis, up), lax.ppermute(leading, axis, down)


def exchange(shard, axis, dim, low, high):
    peers = lax.axis_size(axis)
    length = shard.shape[dim]
    up = [(i, (i + 1) % peers) for i in range(peers)]
    down = [(j, i) for i, j in up]
    last = lax.slice_in_dim(shard, length - low, length, axis=dim)
    leading = lax.slice_in_dim(shard, 0, high, axis=dim)
    before = lax.ppermute(last, axis, up)
    after = lax.ppermute(leading, axis, down)
    return before, after


def local(state, start, eddy, solid, facet_wall, facet_dist, facet_area, facet_owner, facet_cell):
    levels = state.shape[1]
    cells_x = state.shape[2]
    cells_y = state.shape[3]
    width = 3
    edge = 128

    def x_rows(lo, hi):
        rows = jnp.transpose(state[:, :, lo:hi], (1, 0, 2, 3)).reshape(levels, -1, cells_y)
        return jnp.concatenate([rows, eddy[:, lo:hi][:, -1:] if lo else eddy[:, 0:1]], axis=1)

    x_last, x_first = x_rows(cells_x - width, cells_x), x_rows(0, width)
    x_low, x_high = shift_pair(x_last, x_first, "gx")

    facet_count = facet_cell.shape[0]
    owners_gx = lax.axis_size("gx")
    capacity = 2 * facet_count // owners_gx
    slots = owners_gx * capacity
    owner_gx = facet_owner[:, 0]
    owner_hot = (owner_gx[:, None] == jnp.arange(owners_gx, dtype=jnp.int32)[None, :]).astype(
        jnp.bfloat16
    )
    positions = jnp.arange(facet_count, dtype=jnp.int32)
    earlier = (positions[:, None] > positions[None, :]).astype(jnp.bfloat16)
    before = jnp.dot(earlier, owner_hot, preferred_element_type=jnp.float32)
    owner_float = owner_hot.astype(jnp.float32)
    slot_rank = jnp.sum(before * owner_float, axis=1)
    rank_hot = (slot_rank[:, None] == jnp.arange(capacity, dtype=jnp.float32)[None, :]).astype(
        jnp.float32
    )
    payload = jnp.concatenate(
        [facet_wall, facet_dist[None], facet_area[None], facet_cell[None].astype(jnp.float32)],
        axis=0,
    )
    spread = payload[:, None, :] * owner_float.T[None]
    outgoing = jnp.einsum("cof,fk->cok", spread, rank_hot, precision=exact)
    filled = jnp.dot(owner_float.T, rank_hot, precision=exact)
    unit_dist = (jnp.arange(7, dtype=jnp.int32) == 4).astype(jnp.float32)[:, None, None]
    outgoing = outgoing + unit_dist * (1.0 - filled)[None]
    outgoing = jnp.concatenate([outgoing, jnp.zeros((1, owners_gx, capacity), jnp.float32)], axis=0)
    outgoing = jnp.transpose(outgoing, (1, 0, 2)).reshape(owners_gx, -1)
    y_state, y_eddy = state, eddy

    def y_cols(lo, hi, one):
        return jnp.concatenate([y_state[..., lo:hi].reshape(-1), y_eddy[..., one:one + 1].reshape(-1)])

    def y_tile(flat, lanes, one):
        fields_part = flat[: 4 * levels * cells_x * width].reshape(4, levels, cells_x, width)
        eddy_part = flat[4 * levels * cells_x * width:].reshape(1, levels, cells_x, 1)
        pad_f = ((0, 0), (0, 0), (0, 0), (lanes, edge - width - lanes))
        pad_e = ((0, 0), (0, 0), (0, 0), (one, edge - 1 - one))
        return jnp.concatenate([jnp.pad(fields_part, pad_f), jnp.pad(eddy_part, pad_e)], axis=0)

    y_low, y_high = swap_edges(
        y_cols(cells_y - width, cells_y, cells_y - 1), y_cols(0, width, 0), "gy"
    )
    y_low = y_tile(y_low, edge - width, edge - 1)
    y_high = y_tile(y_high, 0, 0)
    x_low, x_high, y_low, y_high, outgoing = lax.optimization_barrier(
        (x_low, x_high, y_low, y_high, outgoing)
    )
    received = lax.all_to_all(outgoing, "gx", 0, 0, tiled=True)
    tend = stencil(state, eddy, x_low, x_high, y_low, y_high)
    tend, received = lax.optimization_barrier((tend, received))
    pay = jnp.transpose(received.reshape(owners_gx, 8, capacity), (1, 0, 2)).reshape(8, slots)
    flux_slots = owner_gather(state.reshape(4 * levels * cells_x, cells_y), pay)
    wall_flux = jnp.transpose(flux_slots.reshape(4, owners_gx, capacity), (1, 0, 2)).reshape(owners_gx, -1)
    wall_flux, pay, flux_slots = lax.optimization_barrier((wall_flux, pay, flux_slots))
    forcing = owner_scatter(pay, flux_slots, 4 * levels * cells_x, cells_y).reshape(state.shape)
    returned = lax.all_to_all(wall_flux, "gx", 0, 0, tiled=True)
    change = (tend - forcing) * (1.0 - solid.astype(jnp.float32))
    new_state = start + dt_step * change
    new_state, returned = lax.optimization_barrier((new_state, returned))
    returned = jnp.transpose(returned.reshape(owners_gx, 4, capacity), (1, 0, 2))
    through = jnp.einsum("cok,fk->cof", returned, rank_hot, precision=exact)
    facet_flux = jnp.sum(through * owner_float.T[None], axis=1)
    return (new_state, facet_flux)


def solution(mesh):
    in_specs = (
        P(None, None, "gx", "gy"),
        P(None, None, "gx", "gy"),
        P(None, "gx", "gy"),
        P(None, "gx", "gy"),
        P(None, ("gx", "gy")),
        P(("gx", "gy")),
        P(("gx", "gy")),
        P(("gx", "gy"), None),
        P(("gx", "gy")),
    )
    out_specs = (P(None, None, "gx", "gy"), P(None, ("gx", "gy")))
    return jax.shard_map(local, mesh=mesh, in_specs=in_specs, out_specs=out_specs, check_vma=False)
```

```python
import math

import jax
import jax.numpy as jnp
from jax import lax
from jax.experimental import pallas as pl
from jax.experimental.pallas import tpu as pltpu
from jax.sharding import PartitionSpec as P

dt_step = 0.2
exact = lax.Precision.HIGHEST


def _upwind(s, c):
    forward = (((((-2.0 * s(-3) + 15.0 * s(-2)) - 60.0 * s(-1)) + 20.0 * s(0)) + 30.0 * s(1)) - 3.0 * s(2))
    backward = (((((3.0 * s(-2) - 30.0 * s(-1)) - 20.0 * s(0)) + 60.0 * s(1)) - 15.0 * s(2)) + 2.0 * s(3))
    return jnp.where(c > 0, forward, backward) / 60.0


def _x_shifter(f, lo_rows, hi_rows):
    rows = f.shape[0]
    row = lax.broadcasted_iota(jnp.int32, f.shape, 0)
    width = len(lo_rows)
    lo_b = [jnp.broadcast_to(r, f.shape) for r in lo_rows]
    hi_b = [jnp.broadcast_to(r, f.shape) for r in hi_rows]
    cache = {0: f}

    def s(k):
        if k in cache:
            return cache[k]
        if k > 0:
            r = pltpu.roll(f, rows - k, 0)
            patch = hi_b[k - 1]
            for i in range(k - 2, -1, -1):
                patch = jnp.where(row == rows - k + i, hi_b[i], patch)
            out = jnp.where(row < rows - k, r, patch)
        else:
            m = -k
            r = pltpu.roll(f, m, 0)
            patch = lo_b[width - 1]
            for i in range(m - 1):
                patch = jnp.where(row == i, lo_b[width - m + i], patch)
            out = jnp.where(row >= m, r, patch)
        cache[k] = out
        return out
    return s


def _y_shifter(f, lo, hi):
    cols = f.shape[1]
    edge = lo.shape[1]
    lane = lax.broadcasted_iota(jnp.int32, lo.shape, 1)
    cache = {0: f}

    def s(k):
        if k in cache:
            return cache[k]
        if k > 0:
            r = pltpu.roll(f, cols - k, 1)
            patch = pltpu.roll(hi, edge - k, 1)
            last = jnp.where(lane >= edge - k, patch, r[:, cols - edge:])
            out = jnp.concatenate([r[:, :cols - edge], last], axis=1)
        else:
            m = -k
            r = pltpu.roll(f, m, 1)
            patch = pltpu.roll(lo, m, 1)
            first = jnp.where(lane < m, patch, r[:, :edge])
            out = jnp.concatenate([first, r[:, edge:]], axis=1)
        cache[k] = out
        return out
    return s


def stencil_kernel(sc_ref, sd_ref, su_ref, ec_ref, ed_ref, eu_ref, xl_ref, xh_ref, yl_ref, yh_ref, out_ref):
    level = pl.program_id(0)
    levels = pl.num_programs(0)
    fields = sc_ref.shape[0]
    width = (xl_ref.shape[1] - 1) // fields
    e = ec_ref[0]
    ed = ed_ref[0]
    eu = eu_ref[0]
    up_w = jnp.where(level < levels - 1, 1.0, 0.0)
    down_w = jnp.where(level > 0, 1.0, 0.0)
    eddy_up = (0.5 * (e + eu)) * up_w
    eddy_down = (0.5 * (ed + e)) * down_w
    ex = _x_shifter(e, [xl_ref[0, pl.ds(fields * width, 1), :]], [xh_ref[0, pl.ds(fields * width, 1), :]])
    ey = _y_shifter(e, yl_ref[fields, 0], yh_ref[fields, 0])
    east = 0.5 * (e + ex(1))
    west = 0.5 * (ex(-1) + e)
    north = 0.5 * (e + ey(1))
    south = 0.5 * (ey(-1) + e)
    u = sc_ref[0, 0]
    v = sc_ref[1, 0]
    w = sc_ref[2, 0]
    for f in range(fields):
        fv = sc_ref[f, 0]
        lower = sd_ref[f, 0]
        upper = su_ref[f, 0]
        sx = _x_shifter(fv, [xl_ref[0, pl.ds(f * width + i, 1), :] for i in range(width)],
                        [xh_ref[0, pl.ds(f * width + i, 1), :] for i in range(width)])
        sy = _y_shifter(fv, yl_ref[f, 0], yh_ref[f, 0])
        derx = _upwind(sx, u)
        dery = _upwind(sy, v)
        derz = (upper - lower) * 0.5
        zdiffuse = eddy_up * (upper - fv) - eddy_down * (fv - lower)
        advect = (u * derx + v * dery) + w * derz
        diff_x = east * (sx(1) - fv) - west * (fv - sx(-1))
        diff_y = north * (sy(1) - fv) - south * (fv - sy(-1))
        diffuse = (diff_x + diff_y) + zdiffuse
        out_ref[f, 0] = diffuse - advect


def stencil(state, eddy, xl, xh, yl, yh):
    fields, levels, cx, cy = state.shape
    w = xl.shape[1]
    nf = yl.shape[0]
    edge = yl.shape[3]
    below = lambda l: jnp.maximum(l - 1, 0)
    above = lambda l: jnp.minimum(l + 1, levels - 1)
    return pl.pallas_call(
        stencil_kernel,
        grid=(levels,),
        in_specs=[
            pl.BlockSpec((fields, 1, cx, cy), lambda l: (0, l, 0, 0)),
            pl.BlockSpec((fields, 1, cx, cy), lambda l: (0, below(l), 0, 0)),
            pl.BlockSpec((fields, 1, cx, cy), lambda l: (0, above(l), 0, 0)),
            pl.BlockSpec((1, cx, cy), lambda l: (l, 0, 0)),
            pl.BlockSpec((1, cx, cy), lambda l: (below(l), 0, 0)),
            pl.BlockSpec((1, cx, cy), lambda l: (above(l), 0, 0)),
            pl.BlockSpec((1, w, cy), lambda l: (l, 0, 0)),
            pl.BlockSpec((1, w, cy), lambda l: (l, 0, 0)),
            pl.BlockSpec((nf, 1, cx, edge), lambda l: (0, l, 0, 0)),
            pl.BlockSpec((nf, 1, cx, edge), lambda l: (0, l, 0, 0)),
        ],
        out_specs=pl.BlockSpec((fields, 1, cx, cy), lambda l: (0, l, 0, 0)),
        out_shape=jax.ShapeDtypeStruct((fields, levels, cx, cy), jnp.float32),
        compiler_params=pltpu.CompilerParams(dimension_semantics=("arbitrary",)),
        cost_estimate=pl.CostEstimate(flops=200 * fields * levels * cx * cy, transcendentals=0,
                                      bytes_accessed=4 * (4 * nf + fields) * levels * cx * cy),
    )(state, state, state, eddy, eddy, eddy, xl, xh, yl, yh)


def _pieces(x, n):
    out = []
    rest = x
    for _ in range(n):
        p = rest.astype(jnp.bfloat16)
        out.append(p)
        rest = rest - p.astype(jnp.float32)
    return out


def _one_hot(cell, cols, iota):
    sub = iota.shape[0]
    col = cell % cols
    hi = col // sub
    lo = (col % sub).astype(jnp.float32)
    hots = []
    for a in range(cols // sub):
        sel = jnp.where(hi == a, lo, -1.0).astype(jnp.bfloat16)
        hots.append(jnp.where(iota == sel, jnp.bfloat16(1), jnp.bfloat16(0)))
    return jnp.concatenate(hots, axis=0)


def gather_kernel(x_ref, pay_ref, flux_ref, pieces_ref, iota_ref):
    rows, cols = x_ref.shape
    fields = 4
    per_field = rows // fields
    block = pay_ref.shape[1]

    @pl.when(pl.program_id(0) == 0)
    def _():
        parts = _pieces(x_ref[...], 2)
        for i, p in enumerate(parts):
            pieces_ref[i * rows:(i + 1) * rows, :] = p
        iota_ref[...] = lax.broadcasted_iota(jnp.int32, iota_ref.shape, 0).astype(jnp.bfloat16)

    pay = pay_ref[...]
    cell = (pay[6:7] + 0.5).astype(jnp.int32)
    row = cell // cols
    hot = _one_hot(cell, cols, iota_ref[...])
    picked = jnp.dot(pieces_ref[...], hot, preferred_element_type=jnp.float32)
    value = picked[0:rows] + picked[rows:2 * rows]
    pick_row = lax.broadcasted_iota(jnp.int32, (per_field, block), 0) == row
    gathered = jnp.concatenate(
        [jnp.sum(jnp.where(pick_row, value[f * per_field:(f + 1) * per_field], 0.0), axis=0, keepdims=True)
         for f in range(fields)], axis=0)
    flux_ref[...] = pay[5:6] * (gathered - pay[0:4]) / pay[4:5]


def scatter_kernel(pay_ref, flux_ref, forcing_ref, iota_ref):
    rows, cols = forcing_ref.shape
    fields = 4
    per_field = rows // fields
    block = pay_ref.shape[1]

    @pl.when(pl.program_id(0) == 0)
    def _():
        forcing_ref[...] = jnp.zeros_like(forcing_ref)
        iota_ref[...] = lax.broadcasted_iota(jnp.int32, iota_ref.shape, 0).astype(jnp.bfloat16)

    pay = pay_ref[...]
    cell = (pay[6:7] + 0.5).astype(jnp.int32)
    row = cell // cols
    hot = _one_hot(cell, cols, iota_ref[...])
    flux = flux_ref[...]
    pick_row = lax.broadcasted_iota(jnp.int32, (per_field, block), 0) == row
    spread = jnp.concatenate(
        [jnp.where(pick_row, flux[f:f + 1], 0.0) for f in range(fields)], axis=0)
    w = jnp.concatenate(_pieces(spread, 2), axis=0)
    added = lax.dot_general(w, hot, (((1,), (1,)), ((), ())), preferred_element_type=jnp.float32)
    forcing_ref[...] += added[0:rows] + added[rows:2 * rows]


def owner_gather(x, pay, block=1024):
    rows, cols = x.shape
    slots = pay.shape[1]
    return pl.pallas_call(
        gather_kernel,
        grid=(slots // block,),
        in_specs=[
            pl.BlockSpec((rows, cols), lambda j: (0, 0)),
            pl.BlockSpec((8, block), lambda j: (0, j)),
        ],
        out_specs=pl.BlockSpec((4, block), lambda j: (0, j)),
        out_shape=jax.ShapeDtypeStruct((4, slots), jnp.float32),
        scratch_shapes=[pltpu.VMEM((2 * rows, cols), jnp.bfloat16),
                        pltpu.VMEM((256, block), jnp.bfloat16)],
        compiler_params=pltpu.CompilerParams(dimension_semantics=("arbitrary",),
                                             vmem_limit_bytes=48 * 1024 * 1024),
        cost_estimate=pl.CostEstimate(flops=2 * (2 * rows) * cols * slots, transcendentals=0,
                                      bytes_accessed=4 * (rows * cols + 12 * slots)),
    )(x, pay)


def owner_scatter(pay, flux, rows, cols, block=1024):
    slots = pay.shape[1]
    return pl.pallas_call(
        scatter_kernel,
        grid=(slots // block,),
        in_specs=[
            pl.BlockSpec((8, block), lambda j: (0, j)),
            pl.BlockSpec((4, block), lambda j: (0, j)),
        ],
        out_specs=pl.BlockSpec((rows, cols), lambda j: (0, 0)),
        out_shape=jax.ShapeDtypeStruct((rows, cols), jnp.float32),
        scratch_shapes=[pltpu.VMEM((256, block), jnp.bfloat16)],
        compiler_params=pltpu.CompilerParams(dimension_semantics=("arbitrary",),
                                             vmem_limit_bytes=48 * 1024 * 1024),
        cost_estimate=pl.CostEstimate(flops=rows * cols, transcendentals=0, bytes_accessed=4 * rows * cols),
    )(pay, flux)


def shift_pair(last, leading, axis):
    peers = lax.axis_size(axis)
    up = [(i, (i + 1) % peers) for i in range(peers)]
    down = [(j, i) for i, j in up]
    return lax.ppermute(last, axis, up), lax.ppermute(leading, axis, down)


def exchange(shard, axis, dim, low, high):
    peers = lax.axis_size(axis)
    length = shard.shape[dim]
    up = [(i, (i + 1) % peers) for i in range(peers)]
    down = [(j, i) for i, j in up]
    last = lax.slice_in_dim(shard, length - low, length, axis=dim)
    leading = lax.slice_in_dim(shard, 0, high, axis=dim)
    before = lax.ppermute(last, axis, up)
    after = lax.ppermute(leading, axis, down)
    return before, after


def local(state, start, eddy, solid, facet_wall, facet_dist, facet_area, facet_owner, facet_cell):
    levels = state.shape[1]
    cells_x = state.shape[2]
    cells_y = state.shape[3]
    width = 3
    edge = 128

    def x_rows(lo, hi):
        rows = jnp.transpose(state[:, :, lo:hi], (1, 0, 2, 3)).reshape(levels, -1, cells_y)
        return jnp.concatenate([rows, eddy[:, lo:hi][:, -1:] if lo else eddy[:, 0:1]], axis=1)

    x_last, x_first = x_rows(cells_x - width, cells_x), x_rows(0, width)
    x_low, x_high = shift_pair(x_last, x_first, "gx")

    def y_cols(lo, hi):
        return jnp.concatenate([state[..., lo:hi], eddy[None, ..., lo:hi]], axis=0)

    y_low, y_high = shift_pair(y_cols(cells_y - edge, cells_y), y_cols(0, edge), "gy")

    facet_count = facet_cell.shape[0]
    owners_gx = lax.axis_size("gx")
    capacity = 2 * facet_count // owners_gx
    slots = owners_gx * capacity
    owner_gx = facet_owner[:, 0]
    owner_hot = (owner_gx[:, None] == jnp.arange(owners_gx, dtype=jnp.int32)[None, :]).astype(
        jnp.bfloat16
    )
    positions = jnp.arange(facet_count, dtype=jnp.int32)
    earlier = (positions[:, None] > positions[None, :]).astype(jnp.bfloat16)
    before = jnp.dot(earlier, owner_hot, preferred_element_type=jnp.float32)
    owner_float = owner_hot.astype(jnp.float32)
    slot_rank = jnp.sum(before * owner_float, axis=1)
    rank_hot = (slot_rank[:, None] == jnp.arange(capacity, dtype=jnp.float32)[None, :]).astype(
        jnp.float32
    )
    payload = jnp.concatenate(
        [facet_wall, facet_dist[None], facet_area[None], facet_cell[None].astype(jnp.float32)],
        axis=0,
    )
    spread = payload[:, None, :] * owner_float.T[None]
    outgoing = jnp.einsum("cof,fk->cok", spread, rank_hot, precision=exact)
    filled = jnp.dot(owner_float.T, rank_hot, precision=exact)
    unit_dist = (jnp.arange(7, dtype=jnp.int32) == 4).astype(jnp.float32)[:, None, None]
    outgoing = outgoing + unit_dist * (1.0 - filled)[None]
    outgoing = jnp.concatenate([outgoing, jnp.zeros((1, owners_gx, capacity), jnp.float32)], axis=0)
    outgoing = jnp.transpose(outgoing, (1, 0, 2)).reshape(owners_gx, -1)
    x_low, x_high, y_low, y_high, outgoing = lax.optimization_barrier(
        (x_low, x_high, y_low, y_high, outgoing)
    )
    received = lax.all_to_all(outgoing, "gx", 0, 0, tiled=True)
    tend = stencil(state, eddy, x_low, x_high, y_low, y_high)
    tend, received = lax.optimization_barrier((tend, received))
    pay = jnp.transpose(received.reshape(owners_gx, 8, capacity), (1, 0, 2)).reshape(8, slots)
    flux_slots = owner_gather(state.reshape(4 * levels * cells_x, cells_y), pay)
    wall_flux = jnp.transpose(flux_slots.reshape(4, owners_gx, capacity), (1, 0, 2)).reshape(owners_gx, -1)
    wall_flux, pay, flux_slots = lax.optimization_barrier((wall_flux, pay, flux_slots))
    forcing = owner_scatter(pay, flux_slots, 4 * levels * cells_x, cells_y).reshape(state.shape)
    returned = lax.all_to_all(wall_flux, "gx", 0, 0, tiled=True)
    change = (tend - forcing) * (1.0 - solid.astype(jnp.float32))
    new_state = start + dt_step * change
    new_state, returned = lax.optimization_barrier((new_state, returned))
    returned = jnp.transpose(returned.reshape(owners_gx, 4, capacity), (1, 0, 2))
    pieces = []
    rest = returned
    for _ in range(3):
        piece = lax.reduce_precision(rest, exponent_bits=8, mantissa_bits=7)
        rest = rest - piece
        pieces.append(piece.astype(jnp.bfloat16))
    rank_bf16 = rank_hot.astype(jnp.bfloat16)
    through = jnp.einsum(
        "cok,fk->cof",
        jnp.concatenate(pieces, axis=2),
        jnp.concatenate([rank_bf16] * 3, axis=1),
        preferred_element_type=jnp.float32,
    )
    facet_flux = jnp.sum(through * owner_float.T[None], axis=1)
    return (new_state, facet_flux)


def solution(mesh):
    in_specs = (
        P(None, None, "gx", "gy"),
        P(None, None, "gx", "gy"),
        P(None, "gx", "gy"),
        P(None, "gx", "gy"),
        P(None, ("gx", "gy")),
        P(("gx", "gy")),
        P(("gx", "gy")),
        P(("gx", "gy"), None),
        P(("gx", "gy")),
    )
    out_specs = (P(None, None, "gx", "gy"), P(None, ("gx", "gy")))
    return jax.shard_map(local, mesh=mesh, in_specs=in_specs, out_specs=out_specs, check_vma=False)
```

```python
import math

import jax
import jax.numpy as jnp
from jax import lax
from jax.experimental import pallas as pl
from jax.experimental.pallas import tpu as pltpu
from jax.sharding import PartitionSpec as P

dt_step = 0.2
exact = lax.Precision.HIGHEST


def _upwind(s, c):
    forward = (((((-2.0 * s(-3) + 15.0 * s(-2)) - 60.0 * s(-1)) + 20.0 * s(0)) + 30.0 * s(1)) - 3.0 * s(2))
    backward = (((((3.0 * s(-2) - 30.0 * s(-1)) - 20.0 * s(0)) + 60.0 * s(1)) - 15.0 * s(2)) + 2.0 * s(3))
    return jnp.where(c > 0, forward, backward) / 60.0


def _x_shifter(f, lo_rows, hi_rows):
    rows = f.shape[0]
    row = lax.broadcasted_iota(jnp.int32, f.shape, 0)
    width = len(lo_rows)
    lo_b = [jnp.broadcast_to(r, f.shape) for r in lo_rows]
    hi_b = [jnp.broadcast_to(r, f.shape) for r in hi_rows]
    cache = {0: f}

    def s(k):
        if k in cache:
            return cache[k]
        if k > 0:
            r = pltpu.roll(f, rows - k, 0)
            patch = hi_b[k - 1]
            for i in range(k - 2, -1, -1):
                patch = jnp.where(row == rows - k + i, hi_b[i], patch)
            out = jnp.where(row < rows - k, r, patch)
        else:
            m = -k
            r = pltpu.roll(f, m, 0)
            patch = lo_b[width - 1]
            for i in range(m - 1):
                patch = jnp.where(row == i, lo_b[width - m + i], patch)
            out = jnp.where(row >= m, r, patch)
        cache[k] = out
        return out
    return s


def _y_shifter(f, lo, hi):
    cols = f.shape[1]
    edge = lo.shape[1]
    lane = lax.broadcasted_iota(jnp.int32, lo.shape, 1)
    cache = {0: f}

    def s(k):
        if k in cache:
            return cache[k]
        if k > 0:
            r = pltpu.roll(f, cols - k, 1)
            patch = pltpu.roll(hi, edge - k, 1)
            last = jnp.where(lane >= edge - k, patch, r[:, cols - edge:])
            out = jnp.concatenate([r[:, :cols - edge], last], axis=1)
        else:
            m = -k
            r = pltpu.roll(f, m, 1)
            patch = pltpu.roll(lo, m, 1)
            first = jnp.where(lane < m, patch, r[:, :edge])
            out = jnp.concatenate([first, r[:, edge:]], axis=1)
        cache[k] = out
        return out
    return s


def stencil_kernel(sc_ref, sd_ref, su_ref, ec_ref, ed_ref, eu_ref, xl_ref, xh_ref, yl_ref, yh_ref, out_ref):
    level = pl.program_id(0)
    levels = pl.num_programs(0)
    fields = sc_ref.shape[0]
    width = (xl_ref.shape[1] - 1) // fields
    e = ec_ref[0]
    ed = ed_ref[0]
    eu = eu_ref[0]
    up_w = jnp.where(level < levels - 1, 1.0, 0.0)
    down_w = jnp.where(level > 0, 1.0, 0.0)
    eddy_up = (0.5 * (e + eu)) * up_w
    eddy_down = (0.5 * (ed + e)) * down_w
    ex = _x_shifter(e, [xl_ref[0, pl.ds(fields * width, 1), :]], [xh_ref[0, pl.ds(fields * width, 1), :]])
    ey = _y_shifter(e, yl_ref[fields, 0], yh_ref[fields, 0])
    east = 0.5 * (e + ex(1))
    west = 0.5 * (ex(-1) + e)
    north = 0.5 * (e + ey(1))
    south = 0.5 * (ey(-1) + e)
    u = sc_ref[0, 0]
    v = sc_ref[1, 0]
    w = sc_ref[2, 0]
    for f in range(fields):
        fv = sc_ref[f, 0]
        lower = sd_ref[f, 0]
        upper = su_ref[f, 0]
        sx = _x_shifter(fv, [xl_ref[0, pl.ds(f * width + i, 1), :] for i in range(width)],
                        [xh_ref[0, pl.ds(f * width + i, 1), :] for i in range(width)])
        sy = _y_shifter(fv, yl_ref[f, 0], yh_ref[f, 0])
        derx = _upwind(sx, u)
        dery = _upwind(sy, v)
        derz = (upper - lower) * 0.5
        zdiffuse = eddy_up * (upper - fv) - eddy_down * (fv - lower)
        advect = (u * derx + v * dery) + w * derz
        diff_x = east * (sx(1) - fv) - west * (fv - sx(-1))
        diff_y = north * (sy(1) - fv) - south * (fv - sy(-1))
        diffuse = (diff_x + diff_y) + zdiffuse
        out_ref[f, 0] = diffuse - advect


def stencil(state, eddy, xl, xh, yl, yh):
    fields, levels, cx, cy = state.shape
    w = xl.shape[1]
    nf = yl.shape[0]
    edge = yl.shape[3]
    below = lambda l: jnp.maximum(l - 1, 0)
    above = lambda l: jnp.minimum(l + 1, levels - 1)
    return pl.pallas_call(
        stencil_kernel,
        grid=(levels,),
        in_specs=[
            pl.BlockSpec((fields, 1, cx, cy), lambda l: (0, l, 0, 0)),
            pl.BlockSpec((fields, 1, cx, cy), lambda l: (0, below(l), 0, 0)),
            pl.BlockSpec((fields, 1, cx, cy), lambda l: (0, above(l), 0, 0)),
            pl.BlockSpec((1, cx, cy), lambda l: (l, 0, 0)),
            pl.BlockSpec((1, cx, cy), lambda l: (below(l), 0, 0)),
            pl.BlockSpec((1, cx, cy), lambda l: (above(l), 0, 0)),
            pl.BlockSpec((1, w, cy), lambda l: (l, 0, 0)),
            pl.BlockSpec((1, w, cy), lambda l: (l, 0, 0)),
            pl.BlockSpec((nf, 1, cx, edge), lambda l: (0, l, 0, 0)),
            pl.BlockSpec((nf, 1, cx, edge), lambda l: (0, l, 0, 0)),
        ],
        out_specs=pl.BlockSpec((fields, 1, cx, cy), lambda l: (0, l, 0, 0)),
        out_shape=jax.ShapeDtypeStruct((fields, levels, cx, cy), jnp.float32),
        compiler_params=pltpu.CompilerParams(dimension_semantics=("arbitrary",)),
        cost_estimate=pl.CostEstimate(flops=200 * fields * levels * cx * cy, transcendentals=0,
                                      bytes_accessed=4 * (4 * nf + fields) * levels * cx * cy),
    )(state, state, state, eddy, eddy, eddy, xl, xh, yl, yh)


def _pieces(x, n):
    out = []
    rest = x
    for _ in range(n):
        p = rest.astype(jnp.bfloat16)
        out.append(p)
        rest = rest - p.astype(jnp.float32)
    return out


def _one_hot(cell, cols, iota):
    sub = iota.shape[0]
    col = cell % cols
    hi = col // sub
    lo = (col % sub).astype(jnp.float32)
    hots = []
    for a in range(cols // sub):
        sel = jnp.where(hi == a, lo, -1.0).astype(jnp.bfloat16)
        hots.append(jnp.where(iota == sel, jnp.bfloat16(1), jnp.bfloat16(0)))
    return jnp.concatenate(hots, axis=0)


def gather_kernel(x_ref, pay_ref, flux_ref, pieces_ref, iota_ref):
    rows, cols = x_ref.shape
    fields = 4
    per_field = rows // fields
    block = pay_ref.shape[1]

    @pl.when(pl.program_id(0) == 0)
    def _():
        parts = _pieces(x_ref[...], 2)
        for i, p in enumerate(parts):
            pieces_ref[i * rows:(i + 1) * rows, :] = p
        iota_ref[...] = lax.broadcasted_iota(jnp.int32, iota_ref.shape, 0).astype(jnp.bfloat16)

    pay = pay_ref[...]
    cell = (pay[6:7] + 0.5).astype(jnp.int32)
    row = cell // cols
    hot = _one_hot(cell, cols, iota_ref[...])
    picked = jnp.dot(pieces_ref[...], hot, preferred_element_type=jnp.float32)
    value = picked[0:rows] + picked[rows:2 * rows]
    pick_row = lax.broadcasted_iota(jnp.int32, (per_field, block), 0) == row
    gathered = jnp.concatenate(
        [jnp.sum(jnp.where(pick_row, value[f * per_field:(f + 1) * per_field], 0.0), axis=0, keepdims=True)
         for f in range(fields)], axis=0)
    flux_ref[...] = pay[5:6] * (gathered - pay[0:4]) / pay[4:5]


def scatter_kernel(pay_ref, flux_ref, forcing_ref, iota_ref):
    rows, cols = forcing_ref.shape
    fields = 4
    per_field = rows // fields
    block = pay_ref.shape[1]

    @pl.when(pl.program_id(0) == 0)
    def _():
        forcing_ref[...] = jnp.zeros_like(forcing_ref)
        iota_ref[...] = lax.broadcasted_iota(jnp.int32, iota_ref.shape, 0).astype(jnp.bfloat16)

    pay = pay_ref[...]
    cell = (pay[6:7] + 0.5).astype(jnp.int32)
    row = cell // cols
    hot = _one_hot(cell, cols, iota_ref[...])
    flux = flux_ref[...]
    pick_row = lax.broadcasted_iota(jnp.int32, (per_field, block), 0) == row
    spread = jnp.concatenate(
        [jnp.where(pick_row, flux[f:f + 1], 0.0) for f in range(fields)], axis=0)
    w = jnp.concatenate(_pieces(spread, 2), axis=0)
    added = lax.dot_general(w, hot, (((1,), (1,)), ((), ())), preferred_element_type=jnp.float32)
    forcing_ref[...] += added[0:rows] + added[rows:2 * rows]


def owner_gather(x, pay, block=1024):
    rows, cols = x.shape
    slots = pay.shape[1]
    return pl.pallas_call(
        gather_kernel,
        grid=(slots // block,),
        in_specs=[
            pl.BlockSpec((rows, cols), lambda j: (0, 0)),
            pl.BlockSpec((8, block), lambda j: (0, j)),
        ],
        out_specs=pl.BlockSpec((4, block), lambda j: (0, j)),
        out_shape=jax.ShapeDtypeStruct((4, slots), jnp.float32),
        scratch_shapes=[pltpu.VMEM((2 * rows, cols), jnp.bfloat16),
                        pltpu.VMEM((256, block), jnp.bfloat16)],
        compiler_params=pltpu.CompilerParams(dimension_semantics=("arbitrary",),
                                             vmem_limit_bytes=48 * 1024 * 1024),
        cost_estimate=pl.CostEstimate(flops=2 * (2 * rows) * cols * slots, transcendentals=0,
                                      bytes_accessed=4 * (rows * cols + 12 * slots)),
    )(x, pay)


def owner_scatter(pay, flux, rows, cols, block=1024):
    slots = pay.shape[1]
    return pl.pallas_call(
        scatter_kernel,
        grid=(slots // block,),
        in_specs=[
            pl.BlockSpec((8, block), lambda j: (0, j)),
            pl.BlockSpec((4, block), lambda j: (0, j)),
        ],
        out_specs=pl.BlockSpec((rows, cols), lambda j: (0, 0)),
        out_shape=jax.ShapeDtypeStruct((rows, cols), jnp.float32),
        scratch_shapes=[pltpu.VMEM((256, block), jnp.bfloat16)],
        compiler_params=pltpu.CompilerParams(dimension_semantics=("arbitrary",),
                                             vmem_limit_bytes=48 * 1024 * 1024),
        cost_estimate=pl.CostEstimate(flops=rows * cols, transcendentals=0, bytes_accessed=4 * rows * cols),
    )(pay, flux)


def shift_pair(last, leading, axis):
    peers = lax.axis_size(axis)
    up = [(i, (i + 1) % peers) for i in range(peers)]
    down = [(j, i) for i, j in up]
    return lax.ppermute(last, axis, up), lax.ppermute(leading, axis, down)


def exchange(shard, axis, dim, low, high):
    peers = lax.axis_size(axis)
    length = shard.shape[dim]
    up = [(i, (i + 1) % peers) for i in range(peers)]
    down = [(j, i) for i, j in up]
    last = lax.slice_in_dim(shard, length - low, length, axis=dim)
    leading = lax.slice_in_dim(shard, 0, high, axis=dim)
    before = lax.ppermute(last, axis, up)
    after = lax.ppermute(leading, axis, down)
    return before, after


def local(state, start, eddy, solid, facet_wall, facet_dist, facet_area, facet_owner, facet_cell):
    levels = state.shape[1]
    cells_x = state.shape[2]
    cells_y = state.shape[3]
    width = 3
    edge = 128

    def x_rows(lo, hi):
        rows = jnp.transpose(state[:, :, lo:hi], (1, 0, 2, 3)).reshape(levels, -1, cells_y)
        return jnp.concatenate([rows, eddy[:, lo:hi][:, -1:] if lo else eddy[:, 0:1]], axis=1)

    x_last, x_first = x_rows(cells_x - width, cells_x), x_rows(0, width)
    x_low, x_high = shift_pair(x_last, x_first, "gx")
    _, _, y_state, y_eddy = lax.optimization_barrier((x_last, x_first, state, eddy))

    def y_cols(lo, hi, one):
        return jnp.concatenate([y_state[..., lo:hi].reshape(-1), y_eddy[..., one:one + 1].reshape(-1)])

    def y_tile(flat, lanes, one):
        fields_part = flat[: 4 * levels * cells_x * width].reshape(4, levels, cells_x, width)
        eddy_part = flat[4 * levels * cells_x * width:].reshape(1, levels, cells_x, 1)
        pad_f = ((0, 0), (0, 0), (0, 0), (lanes, edge - width - lanes))
        pad_e = ((0, 0), (0, 0), (0, 0), (one, edge - 1 - one))
        return jnp.concatenate([jnp.pad(fields_part, pad_f), jnp.pad(eddy_part, pad_e)], axis=0)

    y_last, y_first = y_cols(cells_y - width, cells_y, cells_y - 1), y_cols(0, width, 0)
    y_low, y_high = shift_pair(y_last, y_first, "gy")
    _, _, facet_wall, facet_dist, facet_area, facet_owner, facet_cell = lax.optimization_barrier(
        (y_last, y_first, facet_wall, facet_dist, facet_area, facet_owner, facet_cell)
    )
    y_low = y_tile(y_low, edge - width, edge - 1)
    y_high = y_tile(y_high, 0, 0)

    facet_count = facet_cell.shape[0]
    owners_gx = lax.axis_size("gx")
    capacity = 2 * facet_count // owners_gx
    slots = owners_gx * capacity
    owner_gx = facet_owner[:, 0]
    owner_hot = (owner_gx[:, None] == jnp.arange(owners_gx, dtype=jnp.int32)[None, :]).astype(
        jnp.bfloat16
    )
    positions = jnp.arange(facet_count, dtype=jnp.int32)
    earlier = (positions[:, None] > positions[None, :]).astype(jnp.bfloat16)
    before = jnp.dot(earlier, owner_hot, preferred_element_type=jnp.float32)
    owner_float = owner_hot.astype(jnp.float32)
    slot_rank = jnp.sum(before * owner_float, axis=1)
    rank_hot = (slot_rank[:, None] == jnp.arange(capacity, dtype=jnp.float32)[None, :]).astype(
        jnp.float32
    )
    payload = jnp.concatenate(
        [facet_wall, facet_dist[None], facet_area[None], facet_cell[None].astype(jnp.float32)],
        axis=0,
    )
    spread = payload[:, None, :] * owner_float.T[None]
    outgoing = jnp.einsum("cof,fk->cok", spread, rank_hot, precision=exact)
    filled = jnp.dot(owner_float.T, rank_hot, precision=exact)
    unit_dist = (jnp.arange(7, dtype=jnp.int32) == 4).astype(jnp.float32)[:, None, None]
    outgoing = outgoing + unit_dist * (1.0 - filled)[None]
    outgoing = jnp.concatenate([outgoing, jnp.zeros((1, owners_gx, capacity), jnp.float32)], axis=0)
    outgoing = jnp.transpose(outgoing, (1, 0, 2)).reshape(owners_gx, -1)
    x_low, x_high, y_low, y_high, outgoing = lax.optimization_barrier(
        (x_low, x_high, y_low, y_high, outgoing)
    )
    received = lax.all_to_all(outgoing, "gx", 0, 0, tiled=True)
    tend = stencil(state, eddy, x_low, x_high, y_low, y_high)
    tend, received = lax.optimization_barrier((tend, received))
    pay = jnp.transpose(received.reshape(owners_gx, 8, capacity), (1, 0, 2)).reshape(8, slots)
    flux_slots = owner_gather(state.reshape(4 * levels * cells_x, cells_y), pay)
    wall_flux = jnp.transpose(flux_slots.reshape(4, owners_gx, capacity), (1, 0, 2)).reshape(owners_gx, -1)
    wall_flux, pay, flux_slots = lax.optimization_barrier((wall_flux, pay, flux_slots))
    forcing = owner_scatter(pay, flux_slots, 4 * levels * cells_x, cells_y).reshape(state.shape)
    returned = lax.all_to_all(wall_flux, "gx", 0, 0, tiled=True)
    change = (tend - forcing) * (1.0 - solid.astype(jnp.float32))
    new_state = start + dt_step * change
    new_state, returned = lax.optimization_barrier((new_state, returned))
    returned = jnp.transpose(returned.reshape(owners_gx, 4, capacity), (1, 0, 2))
    through = jnp.einsum("cok,fk->cof", returned, rank_hot, precision=exact)
    facet_flux = jnp.sum(through * owner_float.T[None], axis=1)
    return (new_state, facet_flux)


def solution(mesh):
    in_specs = (
        P(None, None, "gx", "gy"),
        P(None, None, "gx", "gy"),
        P(None, "gx", "gy"),
        P(None, "gx", "gy"),
        P(None, ("gx", "gy")),
        P(("gx", "gy")),
        P(("gx", "gy")),
        P(("gx", "gy"), None),
        P(("gx", "gy")),
    )
    out_specs = (P(None, None, "gx", "gy"), P(None, ("gx", "gy")))
    return jax.shard_map(local, mesh=mesh, in_specs=in_specs, out_specs=out_specs, check_vma=False)
```

```python
import math

import jax
import jax.numpy as jnp
from jax import lax
from jax.experimental import pallas as pl
from jax.experimental.pallas import tpu as pltpu
from jax.sharding import PartitionSpec as P

dt_step = 0.2
exact = lax.Precision.HIGHEST


def _upwind(s, c):
    forward = (((((-2.0 * s(-3) + 15.0 * s(-2)) - 60.0 * s(-1)) + 20.0 * s(0)) + 30.0 * s(1)) - 3.0 * s(2))
    backward = (((((3.0 * s(-2) - 30.0 * s(-1)) - 20.0 * s(0)) + 60.0 * s(1)) - 15.0 * s(2)) + 2.0 * s(3))
    return jnp.where(c > 0, forward, backward) / 60.0


def _x_shifter(f, lo_rows, hi_rows):
    rows = f.shape[0]
    row = lax.broadcasted_iota(jnp.int32, f.shape, 0)
    width = len(lo_rows)
    lo_b = [jnp.broadcast_to(r, f.shape) for r in lo_rows]
    hi_b = [jnp.broadcast_to(r, f.shape) for r in hi_rows]
    cache = {0: f}

    def s(k):
        if k in cache:
            return cache[k]
        if k > 0:
            r = pltpu.roll(f, rows - k, 0)
            patch = hi_b[k - 1]
            for i in range(k - 2, -1, -1):
                patch = jnp.where(row == rows - k + i, hi_b[i], patch)
            out = jnp.where(row < rows - k, r, patch)
        else:
            m = -k
            r = pltpu.roll(f, m, 0)
            patch = lo_b[width - 1]
            for i in range(m - 1):
                patch = jnp.where(row == i, lo_b[width - m + i], patch)
            out = jnp.where(row >= m, r, patch)
        cache[k] = out
        return out
    return s


def _y_shifter(f, lo, hi):
    cols = f.shape[1]
    edge = lo.shape[1]
    lane = lax.broadcasted_iota(jnp.int32, lo.shape, 1)
    cache = {0: f}

    def s(k):
        if k in cache:
            return cache[k]
        if k > 0:
            r = pltpu.roll(f, cols - k, 1)
            patch = pltpu.roll(hi, edge - k, 1)
            last = jnp.where(lane >= edge - k, patch, r[:, cols - edge:])
            out = jnp.concatenate([r[:, :cols - edge], last], axis=1)
        else:
            m = -k
            r = pltpu.roll(f, m, 1)
            patch = pltpu.roll(lo, m, 1)
            first = jnp.where(lane < m, patch, r[:, :edge])
            out = jnp.concatenate([first, r[:, edge:]], axis=1)
        cache[k] = out
        return out
    return s


def stencil_kernel(sc_ref, sd_ref, su_ref, ec_ref, ed_ref, eu_ref, xl_ref, xh_ref, yl_ref, yh_ref, out_ref):
    level = pl.program_id(0)
    levels = pl.num_programs(0)
    fields = sc_ref.shape[0]
    width = (xl_ref.shape[1] - 1) // fields
    e = ec_ref[0]
    ed = ed_ref[0]
    eu = eu_ref[0]
    up_w = jnp.where(level < levels - 1, 1.0, 0.0)
    down_w = jnp.where(level > 0, 1.0, 0.0)
    eddy_up = (0.5 * (e + eu)) * up_w
    eddy_down = (0.5 * (ed + e)) * down_w
    ex = _x_shifter(e, [xl_ref[0, pl.ds(fields * width, 1), :]], [xh_ref[0, pl.ds(fields * width, 1), :]])
    ey = _y_shifter(e, yl_ref[fields, 0], yh_ref[fields, 0])
    east = 0.5 * (e + ex(1))
    west = 0.5 * (ex(-1) + e)
    north = 0.5 * (e + ey(1))
    south = 0.5 * (ey(-1) + e)
    u = sc_ref[0, 0]
    v = sc_ref[1, 0]
    w = sc_ref[2, 0]
    for f in range(fields):
        fv = sc_ref[f, 0]
        lower = sd_ref[f, 0]
        upper = su_ref[f, 0]
        sx = _x_shifter(fv, [xl_ref[0, pl.ds(f * width + i, 1), :] for i in range(width)],
                        [xh_ref[0, pl.ds(f * width + i, 1), :] for i in range(width)])
        sy = _y_shifter(fv, yl_ref[f, 0], yh_ref[f, 0])
        derx = _upwind(sx, u)
        dery = _upwind(sy, v)
        derz = (upper - lower) * 0.5
        zdiffuse = eddy_up * (upper - fv) - eddy_down * (fv - lower)
        advect = (u * derx + v * dery) + w * derz
        diff_x = east * (sx(1) - fv) - west * (fv - sx(-1))
        diff_y = north * (sy(1) - fv) - south * (fv - sy(-1))
        diffuse = (diff_x + diff_y) + zdiffuse
        out_ref[f, 0] = diffuse - advect


def stencil(state, eddy, xl, xh, yl, yh):
    fields, levels, cx, cy = state.shape
    w = xl.shape[1]
    nf = yl.shape[0]
    edge = yl.shape[3]
    below = lambda l: jnp.maximum(l - 1, 0)
    above = lambda l: jnp.minimum(l + 1, levels - 1)
    return pl.pallas_call(
        stencil_kernel,
        grid=(levels,),
        in_specs=[
            pl.BlockSpec((fields, 1, cx, cy), lambda l: (0, l, 0, 0)),
            pl.BlockSpec((fields, 1, cx, cy), lambda l: (0, below(l), 0, 0)),
            pl.BlockSpec((fields, 1, cx, cy), lambda l: (0, above(l), 0, 0)),
            pl.BlockSpec((1, cx, cy), lambda l: (l, 0, 0)),
            pl.BlockSpec((1, cx, cy), lambda l: (below(l), 0, 0)),
            pl.BlockSpec((1, cx, cy), lambda l: (above(l), 0, 0)),
            pl.BlockSpec((1, w, cy), lambda l: (l, 0, 0)),
            pl.BlockSpec((1, w, cy), lambda l: (l, 0, 0)),
            pl.BlockSpec((nf, 1, cx, edge), lambda l: (0, l, 0, 0)),
            pl.BlockSpec((nf, 1, cx, edge), lambda l: (0, l, 0, 0)),
        ],
        out_specs=pl.BlockSpec((fields, 1, cx, cy), lambda l: (0, l, 0, 0)),
        out_shape=jax.ShapeDtypeStruct((fields, levels, cx, cy), jnp.float32),
        compiler_params=pltpu.CompilerParams(dimension_semantics=("arbitrary",)),
        cost_estimate=pl.CostEstimate(flops=200 * fields * levels * cx * cy, transcendentals=0,
                                      bytes_accessed=4 * (4 * nf + fields) * levels * cx * cy),
    )(state, state, state, eddy, eddy, eddy, xl, xh, yl, yh)


def _pieces(x, n):
    out = []
    rest = x
    for _ in range(n):
        p = rest.astype(jnp.bfloat16)
        out.append(p)
        rest = rest - p.astype(jnp.float32)
    return out


def _one_hot(cell, cols, iota):
    sub = iota.shape[0]
    col = cell % cols
    hi = col // sub
    lo = (col % sub).astype(jnp.float32)
    hots = []
    for a in range(cols // sub):
        sel = jnp.where(hi == a, lo, -1.0).astype(jnp.bfloat16)
        hots.append(jnp.where(iota == sel, jnp.bfloat16(1), jnp.bfloat16(0)))
    return jnp.concatenate(hots, axis=0)


def gather_kernel(x_ref, pay_ref, flux_ref, pieces_ref, iota_ref):
    rows, cols = x_ref.shape
    fields = 4
    per_field = rows // fields
    block = pay_ref.shape[1]

    @pl.when(pl.program_id(0) == 0)
    def _():
        parts = _pieces(x_ref[...], 2)
        for i, p in enumerate(parts):
            pieces_ref[i * rows:(i + 1) * rows, :] = p
        iota_ref[...] = lax.broadcasted_iota(jnp.int32, iota_ref.shape, 0).astype(jnp.bfloat16)

    pay = pay_ref[...]
    cell = (pay[6:7] + 0.5).astype(jnp.int32)
    row = cell // cols
    hot = _one_hot(cell, cols, iota_ref[...])
    picked = jnp.dot(pieces_ref[...], hot, preferred_element_type=jnp.float32)
    value = picked[0:rows] + picked[rows:2 * rows]
    pick_row = lax.broadcasted_iota(jnp.int32, (per_field, block), 0) == row
    gathered = jnp.concatenate(
        [jnp.sum(jnp.where(pick_row, value[f * per_field:(f + 1) * per_field], 0.0), axis=0, keepdims=True)
         for f in range(fields)], axis=0)
    flux_ref[...] = pay[5:6] * (gathered - pay[0:4]) / pay[4:5]


def scatter_kernel(pay_ref, flux_ref, forcing_ref, iota_ref):
    rows, cols = forcing_ref.shape
    fields = 4
    per_field = rows // fields
    block = pay_ref.shape[1]

    @pl.when(pl.program_id(0) == 0)
    def _():
        forcing_ref[...] = jnp.zeros_like(forcing_ref)
        iota_ref[...] = lax.broadcasted_iota(jnp.int32, iota_ref.shape, 0).astype(jnp.bfloat16)

    pay = pay_ref[...]
    cell = (pay[6:7] + 0.5).astype(jnp.int32)
    row = cell // cols
    hot = _one_hot(cell, cols, iota_ref[...])
    flux = flux_ref[...]
    pick_row = lax.broadcasted_iota(jnp.int32, (per_field, block), 0) == row
    spread = jnp.concatenate(
        [jnp.where(pick_row, flux[f:f + 1], 0.0) for f in range(fields)], axis=0)
    w = jnp.concatenate(_pieces(spread, 2), axis=0)
    added = lax.dot_general(w, hot, (((1,), (1,)), ((), ())), preferred_element_type=jnp.float32)
    forcing_ref[...] += added[0:rows] + added[rows:2 * rows]


def owner_gather(x, pay, block=1024):
    rows, cols = x.shape
    slots = pay.shape[1]
    return pl.pallas_call(
        gather_kernel,
        grid=(slots // block,),
        in_specs=[
            pl.BlockSpec((rows, cols), lambda j: (0, 0)),
            pl.BlockSpec((8, block), lambda j: (0, j)),
        ],
        out_specs=pl.BlockSpec((4, block), lambda j: (0, j)),
        out_shape=jax.ShapeDtypeStruct((4, slots), jnp.float32),
        scratch_shapes=[pltpu.VMEM((2 * rows, cols), jnp.bfloat16),
                        pltpu.VMEM((256, block), jnp.bfloat16)],
        compiler_params=pltpu.CompilerParams(dimension_semantics=("arbitrary",),
                                             vmem_limit_bytes=48 * 1024 * 1024),
        cost_estimate=pl.CostEstimate(flops=2 * (2 * rows) * cols * slots, transcendentals=0,
                                      bytes_accessed=4 * (rows * cols + 12 * slots)),
    )(x, pay)


def owner_scatter(pay, flux, rows, cols, block=1024):
    slots = pay.shape[1]
    return pl.pallas_call(
        scatter_kernel,
        grid=(slots // block,),
        in_specs=[
            pl.BlockSpec((8, block), lambda j: (0, j)),
            pl.BlockSpec((4, block), lambda j: (0, j)),
        ],
        out_specs=pl.BlockSpec((rows, cols), lambda j: (0, 0)),
        out_shape=jax.ShapeDtypeStruct((rows, cols), jnp.float32),
        scratch_shapes=[pltpu.VMEM((256, block), jnp.bfloat16)],
        compiler_params=pltpu.CompilerParams(dimension_semantics=("arbitrary",),
                                             vmem_limit_bytes=48 * 1024 * 1024),
        cost_estimate=pl.CostEstimate(flops=rows * cols, transcendentals=0, bytes_accessed=4 * rows * cols),
    )(pay, flux)


def shift_pair(last, leading, axis):
    peers = lax.axis_size(axis)
    up = [(i, (i + 1) % peers) for i in range(peers)]
    down = [(j, i) for i, j in up]
    return lax.ppermute(last, axis, up), lax.ppermute(leading, axis, down)


def exchange(shard, axis, dim, low, high):
    peers = lax.axis_size(axis)
    length = shard.shape[dim]
    up = [(i, (i + 1) % peers) for i in range(peers)]
    down = [(j, i) for i, j in up]
    last = lax.slice_in_dim(shard, length - low, length, axis=dim)
    leading = lax.slice_in_dim(shard, 0, high, axis=dim)
    before = lax.ppermute(last, axis, up)
    after = lax.ppermute(leading, axis, down)
    return before, after


def local(state, start, eddy, solid, facet_wall, facet_dist, facet_area, facet_owner, facet_cell):
    levels = state.shape[1]
    cells_x = state.shape[2]
    cells_y = state.shape[3]
    width = 3
    edge = 128

    def x_rows(lo, hi):
        rows = jnp.transpose(state[:, :, lo:hi], (1, 0, 2, 3)).reshape(levels, -1, cells_y)
        return jnp.concatenate([rows, eddy[:, lo:hi][:, -1:] if lo else eddy[:, 0:1]], axis=1)

    x_last, x_first = x_rows(cells_x - width, cells_x), x_rows(0, width)
    x_low, x_high = shift_pair(x_last, x_first, "gx")
    _, _, y_state, y_eddy = lax.optimization_barrier((x_last, x_first, state, eddy))

    def y_cols(lo, hi):
        return jnp.concatenate([y_state[..., lo:hi], y_eddy[None, ..., lo:hi]], axis=0)

    y_last, y_first = y_cols(cells_y - edge, cells_y), y_cols(0, edge)
    y_low, y_high = shift_pair(y_last, y_first, "gy")
    _, _, facet_wall, facet_dist, facet_area, facet_owner, facet_cell = lax.optimization_barrier(
        (y_last, y_first, facet_wall, facet_dist, facet_area, facet_owner, facet_cell)
    )

    facet_count = facet_cell.shape[0]
    owners_gx = lax.axis_size("gx")
    capacity = 2 * facet_count // owners_gx
    slots = owners_gx * capacity
    owner_gx = facet_owner[:, 0]
    owner_hot = (owner_gx[:, None] == jnp.arange(owners_gx, dtype=jnp.int32)[None, :]).astype(
        jnp.bfloat16
    )
    positions = jnp.arange(facet_count, dtype=jnp.int32)
    earlier = (positions[:, None] > positions[None, :]).astype(jnp.bfloat16)
    before = jnp.dot(earlier, owner_hot, preferred_element_type=jnp.float32)
    owner_float = owner_hot.astype(jnp.float32)
    slot_rank = jnp.sum(before * owner_float, axis=1)
    rank_hot = (slot_rank[:, None] == jnp.arange(capacity, dtype=jnp.float32)[None, :]).astype(
        jnp.float32
    )
    payload = jnp.concatenate(
        [facet_wall, facet_dist[None], facet_area[None], facet_cell[None].astype(jnp.float32)],
        axis=0,
    )
    spread = payload[:, None, :] * owner_float.T[None]
    outgoing = jnp.einsum("cof,fk->cok", spread, rank_hot, precision=exact)
    filled = jnp.dot(owner_float.T, rank_hot, precision=exact)
    unit_dist = (jnp.arange(7, dtype=jnp.int32) == 4).astype(jnp.float32)[:, None, None]
    outgoing = outgoing + unit_dist * (1.0 - filled)[None]
    outgoing = jnp.concatenate([outgoing, jnp.zeros((1, owners_gx, capacity), jnp.float32)], axis=0)
    outgoing = jnp.transpose(outgoing, (1, 0, 2)).reshape(owners_gx, -1)
    x_low, x_high, y_low, y_high, outgoing = lax.optimization_barrier(
        (x_low, x_high, y_low, y_high, outgoing)
    )
    received = lax.all_to_all(outgoing, "gx", 0, 0, tiled=True)
    tend = stencil(state, eddy, x_low, x_high, y_low, y_high)
    tend, received = lax.optimization_barrier((tend, received))
    pay = jnp.transpose(received.reshape(owners_gx, 8, capacity), (1, 0, 2)).reshape(8, slots)
    flux_slots = owner_gather(state.reshape(4 * levels * cells_x, cells_y), pay)
    wall_flux = jnp.transpose(flux_slots.reshape(4, owners_gx, capacity), (1, 0, 2)).reshape(owners_gx, -1)
    wall_flux, pay, flux_slots = lax.optimization_barrier((wall_flux, pay, flux_slots))
    forcing = owner_scatter(pay, flux_slots, 4 * levels * cells_x, cells_y).reshape(state.shape)
    returned = lax.all_to_all(wall_flux, "gx", 0, 0, tiled=True)
    change = (tend - forcing) * (1.0 - solid.astype(jnp.float32))
    new_state = start + dt_step * change
    new_state, returned = lax.optimization_barrier((new_state, returned))
    returned = jnp.transpose(returned.reshape(owners_gx, 4, capacity), (1, 0, 2))
    through = jnp.einsum("cok,fk->cof", returned, rank_hot, precision=exact)
    facet_flux = jnp.sum(through * owner_float.T[None], axis=1)
    return (new_state, facet_flux)


def solution(mesh):
    in_specs = (
        P(None, None, "gx", "gy"),
        P(None, None, "gx", "gy"),
        P(None, "gx", "gy"),
        P(None, "gx", "gy"),
        P(None, ("gx", "gy")),
        P(("gx", "gy")),
        P(("gx", "gy")),
        P(("gx", "gy"), None),
        P(("gx", "gy")),
    )
    out_specs = (P(None, None, "gx", "gy"), P(None, ("gx", "gy")))
    return jax.shard_map(local, mesh=mesh, in_specs=in_specs, out_specs=out_specs, check_vma=False)
```

```python
import math

import jax
import jax.numpy as jnp
from jax import lax
from jax.experimental import pallas as pl
from jax.experimental.pallas import tpu as pltpu
from jax.sharding import PartitionSpec as P

dt_step = 0.2
exact = lax.Precision.HIGHEST


def _upwind(s, c):
    forward = (((((-2.0 * s(-3) + 15.0 * s(-2)) - 60.0 * s(-1)) + 20.0 * s(0)) + 30.0 * s(1)) - 3.0 * s(2))
    backward = (((((3.0 * s(-2) - 30.0 * s(-1)) - 20.0 * s(0)) + 60.0 * s(1)) - 15.0 * s(2)) + 2.0 * s(3))
    return jnp.where(c > 0, forward, backward) / 60.0


def _x_shifter(f, lo_rows, hi_rows):
    rows = f.shape[0]
    row = lax.broadcasted_iota(jnp.int32, f.shape, 0)
    width = len(lo_rows)
    lo_b = [jnp.broadcast_to(r, f.shape) for r in lo_rows]
    hi_b = [jnp.broadcast_to(r, f.shape) for r in hi_rows]
    cache = {0: f}

    def s(k):
        if k in cache:
            return cache[k]
        if k > 0:
            r = pltpu.roll(f, rows - k, 0)
            patch = hi_b[k - 1]
            for i in range(k - 2, -1, -1):
                patch = jnp.where(row == rows - k + i, hi_b[i], patch)
            out = jnp.where(row < rows - k, r, patch)
        else:
            m = -k
            r = pltpu.roll(f, m, 0)
            patch = lo_b[width - 1]
            for i in range(m - 1):
                patch = jnp.where(row == i, lo_b[width - m + i], patch)
            out = jnp.where(row >= m, r, patch)
        cache[k] = out
        return out
    return s


def _y_shifter(f, lo, hi):
    cols = f.shape[1]
    edge = lo.shape[1]
    lane = lax.broadcasted_iota(jnp.int32, lo.shape, 1)
    cache = {0: f}

    def s(k):
        if k in cache:
            return cache[k]
        if k > 0:
            r = pltpu.roll(f, cols - k, 1)
            patch = pltpu.roll(hi, edge - k, 1)
            last = jnp.where(lane >= edge - k, patch, r[:, cols - edge:])
            out = jnp.concatenate([r[:, :cols - edge], last], axis=1)
        else:
            m = -k
            r = pltpu.roll(f, m, 1)
            patch = pltpu.roll(lo, m, 1)
            first = jnp.where(lane < m, patch, r[:, :edge])
            out = jnp.concatenate([first, r[:, edge:]], axis=1)
        cache[k] = out
        return out
    return s


def stencil_kernel(sc_ref, sd_ref, su_ref, ec_ref, ed_ref, eu_ref, xl_ref, xh_ref, yl_ref, yh_ref, out_ref):
    level = pl.program_id(0)
    levels = pl.num_programs(0)
    fields = sc_ref.shape[0]
    width = (xl_ref.shape[1] - 1) // fields
    e = ec_ref[0]
    ed = ed_ref[0]
    eu = eu_ref[0]
    up_w = jnp.where(level < levels - 1, 1.0, 0.0)
    down_w = jnp.where(level > 0, 1.0, 0.0)
    eddy_up = (0.5 * (e + eu)) * up_w
    eddy_down = (0.5 * (ed + e)) * down_w
    ex = _x_shifter(e, [xl_ref[0, pl.ds(fields * width, 1), :]], [xh_ref[0, pl.ds(fields * width, 1), :]])
    ey = _y_shifter(e, yl_ref[fields, 0], yh_ref[fields, 0])
    east = 0.5 * (e + ex(1))
    west = 0.5 * (ex(-1) + e)
    north = 0.5 * (e + ey(1))
    south = 0.5 * (ey(-1) + e)
    u = sc_ref[0, 0]
    v = sc_ref[1, 0]
    w = sc_ref[2, 0]
    for f in range(fields):
        fv = sc_ref[f, 0]
        lower = sd_ref[f, 0]
        upper = su_ref[f, 0]
        sx = _x_shifter(fv, [xl_ref[0, pl.ds(f * width + i, 1), :] for i in range(width)],
                        [xh_ref[0, pl.ds(f * width + i, 1), :] for i in range(width)])
        sy = _y_shifter(fv, yl_ref[f, 0], yh_ref[f, 0])
        derx = _upwind(sx, u)
        dery = _upwind(sy, v)
        derz = (upper - lower) * 0.5
        zdiffuse = eddy_up * (upper - fv) - eddy_down * (fv - lower)
        advect = (u * derx + v * dery) + w * derz
        diff_x = east * (sx(1) - fv) - west * (fv - sx(-1))
        diff_y = north * (sy(1) - fv) - south * (fv - sy(-1))
        diffuse = (diff_x + diff_y) + zdiffuse
        out_ref[f, 0] = diffuse - advect


def stencil(state, eddy, xl, xh, yl, yh):
    fields, levels, cx, cy = state.shape
    w = xl.shape[1]
    nf = yl.shape[0]
    edge = yl.shape[3]
    below = lambda l: jnp.maximum(l - 1, 0)
    above = lambda l: jnp.minimum(l + 1, levels - 1)
    return pl.pallas_call(
        stencil_kernel,
        grid=(levels,),
        in_specs=[
            pl.BlockSpec((fields, 1, cx, cy), lambda l: (0, l, 0, 0)),
            pl.BlockSpec((fields, 1, cx, cy), lambda l: (0, below(l), 0, 0)),
            pl.BlockSpec((fields, 1, cx, cy), lambda l: (0, above(l), 0, 0)),
            pl.BlockSpec((1, cx, cy), lambda l: (l, 0, 0)),
            pl.BlockSpec((1, cx, cy), lambda l: (below(l), 0, 0)),
            pl.BlockSpec((1, cx, cy), lambda l: (above(l), 0, 0)),
            pl.BlockSpec((1, w, cy), lambda l: (l, 0, 0)),
            pl.BlockSpec((1, w, cy), lambda l: (l, 0, 0)),
            pl.BlockSpec((nf, 1, cx, edge), lambda l: (0, l, 0, 0)),
            pl.BlockSpec((nf, 1, cx, edge), lambda l: (0, l, 0, 0)),
        ],
        out_specs=pl.BlockSpec((fields, 1, cx, cy), lambda l: (0, l, 0, 0)),
        out_shape=jax.ShapeDtypeStruct((fields, levels, cx, cy), jnp.float32),
        compiler_params=pltpu.CompilerParams(dimension_semantics=("arbitrary",)),
        cost_estimate=pl.CostEstimate(flops=200 * fields * levels * cx * cy, transcendentals=0,
                                      bytes_accessed=4 * (4 * nf + fields) * levels * cx * cy),
    )(state, state, state, eddy, eddy, eddy, xl, xh, yl, yh)


def _pieces(x, n):
    out = []
    rest = x
    for _ in range(n):
        p = rest.astype(jnp.bfloat16)
        out.append(p)
        rest = rest - p.astype(jnp.float32)
    return out


def _one_hot(cell, cols, iota):
    sub = iota.shape[0]
    col = cell % cols
    hi = col // sub
    lo = (col % sub).astype(jnp.float32)
    hots = []
    for a in range(cols // sub):
        sel = jnp.where(hi == a, lo, -1.0).astype(jnp.bfloat16)
        hots.append(jnp.where(iota == sel, jnp.bfloat16(1), jnp.bfloat16(0)))
    return jnp.concatenate(hots, axis=0)


def gather_kernel(x_ref, pay_ref, flux_ref, iota_ref):
    rows, cols = x_ref.shape
    fields = 4
    per_field = rows // fields
    block = pay_ref.shape[1]

    rows = rows // 2
    per_field = rows // fields

    @pl.when(pl.program_id(0) == 0)
    def _():
        iota_ref[...] = lax.broadcasted_iota(jnp.int32, iota_ref.shape, 0).astype(jnp.bfloat16)

    pay = pay_ref[...]
    cell = (pay[6:7] + 0.5).astype(jnp.int32)
    row = cell // cols
    hot = _one_hot(cell, cols, iota_ref[...])
    picked = jnp.dot(x_ref[...], hot, preferred_element_type=jnp.float32)
    value = picked[0:rows] + picked[rows:2 * rows]
    pick_row = lax.broadcasted_iota(jnp.int32, (per_field, block), 0) == row
    gathered = jnp.concatenate(
        [jnp.sum(jnp.where(pick_row, value[f * per_field:(f + 1) * per_field], 0.0), axis=0, keepdims=True)
         for f in range(fields)], axis=0)
    flux_ref[...] = pay[5:6] * (gathered - pay[0:4]) / pay[4:5]


def scatter_kernel(pay_ref, flux_ref, forcing_ref, iota_ref):
    rows, cols = forcing_ref.shape
    fields = 4
    per_field = rows // fields
    block = pay_ref.shape[1]

    @pl.when(pl.program_id(0) == 0)
    def _():
        forcing_ref[...] = jnp.zeros_like(forcing_ref)
        iota_ref[...] = lax.broadcasted_iota(jnp.int32, iota_ref.shape, 0).astype(jnp.bfloat16)

    pay = pay_ref[...]
    cell = (pay[6:7] + 0.5).astype(jnp.int32)
    row = cell // cols
    hot = _one_hot(cell, cols, iota_ref[...])
    flux = flux_ref[...]
    pick_row = lax.broadcasted_iota(jnp.int32, (per_field, block), 0) == row
    spread = jnp.concatenate(
        [jnp.where(pick_row, flux[f:f + 1], 0.0) for f in range(fields)], axis=0)
    w = jnp.concatenate(_pieces(spread, 2), axis=0)
    added = lax.dot_general(w, hot, (((1,), (1,)), ((), ())), preferred_element_type=jnp.float32)
    forcing_ref[...] += added[0:rows] + added[rows:2 * rows]


def owner_gather(x, pay, block=1024):
    rows, cols = x.shape
    slots = pay.shape[1]
    return pl.pallas_call(
        gather_kernel,
        grid=(slots // block,),
        in_specs=[
            pl.BlockSpec((rows, cols), lambda j: (0, 0)),
            pl.BlockSpec((8, block), lambda j: (0, j)),
        ],
        out_specs=pl.BlockSpec((4, block), lambda j: (0, j)),
        out_shape=jax.ShapeDtypeStruct((4, slots), jnp.float32),
        scratch_shapes=[pltpu.VMEM((256, block), jnp.bfloat16)],
        compiler_params=pltpu.CompilerParams(dimension_semantics=("arbitrary",),
                                             vmem_limit_bytes=48 * 1024 * 1024),
        cost_estimate=pl.CostEstimate(flops=2 * rows * cols * slots, transcendentals=0,
                                      bytes_accessed=2 * rows * cols + 48 * slots),
    )(x, pay)


def split_kernel(x_ref, out_ref):
    rows = x_ref.shape[0]
    parts = _pieces(x_ref[...], 2)
    for i, p in enumerate(parts):
        out_ref[i * rows:(i + 1) * rows, :] = p


def split_pieces(x):
    rows, cols = x.shape
    return pl.pallas_call(
        split_kernel,
        out_shape=jax.ShapeDtypeStruct((2 * rows, cols), jnp.bfloat16),
        cost_estimate=pl.CostEstimate(flops=4 * rows * cols, transcendentals=0, bytes_accessed=8 * rows * cols),
    )(x)


def owner_scatter(pay, flux, rows, cols, block=1024):
    slots = pay.shape[1]
    return pl.pallas_call(
        scatter_kernel,
        grid=(slots // block,),
        in_specs=[
            pl.BlockSpec((8, block), lambda j: (0, j)),
            pl.BlockSpec((4, block), lambda j: (0, j)),
        ],
        out_specs=pl.BlockSpec((rows, cols), lambda j: (0, 0)),
        out_shape=jax.ShapeDtypeStruct((rows, cols), jnp.float32),
        scratch_shapes=[pltpu.VMEM((256, block), jnp.bfloat16)],
        compiler_params=pltpu.CompilerParams(dimension_semantics=("arbitrary",),
                                             vmem_limit_bytes=48 * 1024 * 1024),
        cost_estimate=pl.CostEstimate(flops=rows * cols, transcendentals=0, bytes_accessed=4 * rows * cols),
    )(pay, flux)


def shift_pair(last, leading, axis):
    peers = lax.axis_size(axis)
    up = [(i, (i + 1) % peers) for i in range(peers)]
    down = [(j, i) for i, j in up]
    return lax.ppermute(last, axis, up), lax.ppermute(leading, axis, down)


def exchange(shard, axis, dim, low, high):
    peers = lax.axis_size(axis)
    length = shard.shape[dim]
    up = [(i, (i + 1) % peers) for i in range(peers)]
    down = [(j, i) for i, j in up]
    last = lax.slice_in_dim(shard, length - low, length, axis=dim)
    leading = lax.slice_in_dim(shard, 0, high, axis=dim)
    before = lax.ppermute(last, axis, up)
    after = lax.ppermute(leading, axis, down)
    return before, after


def local(state, start, eddy, solid, facet_wall, facet_dist, facet_area, facet_owner, facet_cell):
    levels = state.shape[1]
    cells_x = state.shape[2]
    cells_y = state.shape[3]
    width = 3
    edge = 128

    def x_rows(lo, hi):
        rows = jnp.transpose(state[:, :, lo:hi], (1, 0, 2, 3)).reshape(levels, -1, cells_y)
        return jnp.concatenate([rows, eddy[:, lo:hi][:, -1:] if lo else eddy[:, 0:1]], axis=1)

    x_last, x_first = x_rows(cells_x - width, cells_x), x_rows(0, width)
    x_low, x_high = shift_pair(x_last, x_first, "gx")
    _, _, y_state, y_eddy = lax.optimization_barrier((x_last, x_first, state, eddy))

    def y_cols(lo, hi, one):
        return jnp.concatenate([y_state[..., lo:hi].reshape(-1), y_eddy[..., one:one + 1].reshape(-1)])

    def y_tile(flat, lanes, one):
        fields_part = flat[: 4 * levels * cells_x * width].reshape(4, levels, cells_x, width)
        eddy_part = flat[4 * levels * cells_x * width:].reshape(1, levels, cells_x, 1)
        pad_f = ((0, 0), (0, 0), (0, 0), (lanes, edge - width - lanes))
        pad_e = ((0, 0), (0, 0), (0, 0), (one, edge - 1 - one))
        return jnp.concatenate([jnp.pad(fields_part, pad_f), jnp.pad(eddy_part, pad_e)], axis=0)

    y_last, y_first = y_cols(cells_y - width, cells_y, cells_y - 1), y_cols(0, width, 0)
    y_low, y_high = shift_pair(y_last, y_first, "gy")
    _, _, facet_wall, facet_dist, facet_area, facet_owner, facet_cell = lax.optimization_barrier(
        (y_last, y_first, facet_wall, facet_dist, facet_area, facet_owner, facet_cell)
    )
    y_low = y_tile(y_low, edge - width, edge - 1)
    y_high = y_tile(y_high, 0, 0)

    facet_count = facet_cell.shape[0]
    owners_gx = lax.axis_size("gx")
    capacity = 2 * facet_count // owners_gx
    slots = owners_gx * capacity
    owner_gx = facet_owner[:, 0]
    owner_hot = (owner_gx[:, None] == jnp.arange(owners_gx, dtype=jnp.int32)[None, :]).astype(
        jnp.bfloat16
    )
    positions = jnp.arange(facet_count, dtype=jnp.int32)
    earlier = (positions[:, None] > positions[None, :]).astype(jnp.bfloat16)
    before = jnp.dot(earlier, owner_hot, preferred_element_type=jnp.float32)
    owner_float = owner_hot.astype(jnp.float32)
    slot_rank = jnp.sum(before * owner_float, axis=1)
    rank_hot = (slot_rank[:, None] == jnp.arange(capacity, dtype=jnp.float32)[None, :]).astype(
        jnp.float32
    )
    payload = jnp.concatenate(
        [facet_wall, facet_dist[None], facet_area[None], facet_cell[None].astype(jnp.float32)],
        axis=0,
    )
    spread = payload[:, None, :] * owner_float.T[None]
    outgoing = jnp.einsum("cof,fk->cok", spread, rank_hot, precision=exact)
    filled = jnp.dot(owner_float.T, rank_hot, precision=exact)
    unit_dist = (jnp.arange(7, dtype=jnp.int32) == 4).astype(jnp.float32)[:, None, None]
    outgoing = outgoing + unit_dist * (1.0 - filled)[None]
    outgoing = jnp.concatenate([outgoing, jnp.zeros((1, owners_gx, capacity), jnp.float32)], axis=0)
    outgoing = jnp.transpose(outgoing, (1, 0, 2)).reshape(owners_gx, -1)
    x_low, x_high, y_low, y_high, outgoing = lax.optimization_barrier(
        (x_low, x_high, y_low, y_high, outgoing)
    )
    received = lax.all_to_all(outgoing, "gx", 0, 0, tiled=True)
    tend = stencil(state, eddy, x_low, x_high, y_low, y_high)
    state_pieces = split_pieces(state.reshape(4 * levels * cells_x, cells_y))
    tend, state_pieces, received = lax.optimization_barrier((tend, state_pieces, received))
    pay = jnp.transpose(received.reshape(owners_gx, 8, capacity), (1, 0, 2)).reshape(8, slots)
    flux_slots = owner_gather(state_pieces, pay)
    wall_flux = jnp.transpose(flux_slots.reshape(4, owners_gx, capacity), (1, 0, 2)).reshape(owners_gx, -1)
    wall_flux, pay, flux_slots = lax.optimization_barrier((wall_flux, pay, flux_slots))
    forcing = owner_scatter(pay, flux_slots, 4 * levels * cells_x, cells_y).reshape(state.shape)
    returned = lax.all_to_all(wall_flux, "gx", 0, 0, tiled=True)
    change = (tend - forcing) * (1.0 - solid.astype(jnp.float32))
    new_state = start + dt_step * change
    new_state, returned = lax.optimization_barrier((new_state, returned))
    returned = jnp.transpose(returned.reshape(owners_gx, 4, capacity), (1, 0, 2))
    through = jnp.einsum("cok,fk->cof", returned, rank_hot, precision=exact)
    facet_flux = jnp.sum(through * owner_float.T[None], axis=1)
    return (new_state, facet_flux)


def solution(mesh):
    in_specs = (
        P(None, None, "gx", "gy"),
        P(None, None, "gx", "gy"),
        P(None, "gx", "gy"),
        P(None, "gx", "gy"),
        P(None, ("gx", "gy")),
        P(("gx", "gy")),
        P(("gx", "gy")),
        P(("gx", "gy"), None),
        P(("gx", "gy")),
    )
    out_specs = (P(None, None, "gx", "gy"), P(None, ("gx", "gy")))
    return jax.shard_map(local, mesh=mesh, in_specs=in_specs, out_specs=out_specs, check_vma=False)
```

```python
import math

import jax
import jax.numpy as jnp
from jax import lax
from jax.experimental import pallas as pl
from jax.experimental.pallas import tpu as pltpu
from jax.sharding import PartitionSpec as P

dt_step = 0.2
exact = lax.Precision.HIGHEST


def _upwind(s, c):
    forward = (((((-2.0 * s(-3) + 15.0 * s(-2)) - 60.0 * s(-1)) + 20.0 * s(0)) + 30.0 * s(1)) - 3.0 * s(2))
    backward = (((((3.0 * s(-2) - 30.0 * s(-1)) - 20.0 * s(0)) + 60.0 * s(1)) - 15.0 * s(2)) + 2.0 * s(3))
    return jnp.where(c > 0, forward, backward) / 60.0


def _x_shifter(f, lo_rows, hi_rows):
    rows = f.shape[0]
    row = lax.broadcasted_iota(jnp.int32, f.shape, 0)
    width = len(lo_rows)
    lo_b = [jnp.broadcast_to(r, f.shape) for r in lo_rows]
    hi_b = [jnp.broadcast_to(r, f.shape) for r in hi_rows]
    cache = {0: f}

    def s(k):
        if k in cache:
            return cache[k]
        if k > 0:
            r = pltpu.roll(f, rows - k, 0)
            patch = hi_b[k - 1]
            for i in range(k - 2, -1, -1):
                patch = jnp.where(row == rows - k + i, hi_b[i], patch)
            out = jnp.where(row < rows - k, r, patch)
        else:
            m = -k
            r = pltpu.roll(f, m, 0)
            patch = lo_b[width - 1]
            for i in range(m - 1):
                patch = jnp.where(row == i, lo_b[width - m + i], patch)
            out = jnp.where(row >= m, r, patch)
        cache[k] = out
        return out
    return s


def _y_shifter(f, lo, hi):
    cols = f.shape[1]
    edge = lo.shape[1]
    lane = lax.broadcasted_iota(jnp.int32, lo.shape, 1)
    cache = {0: f}

    def s(k):
        if k in cache:
            return cache[k]
        if k > 0:
            r = pltpu.roll(f, cols - k, 1)
            patch = pltpu.roll(hi, edge - k, 1)
            last = jnp.where(lane >= edge - k, patch, r[:, cols - edge:])
            out = jnp.concatenate([r[:, :cols - edge], last], axis=1)
        else:
            m = -k
            r = pltpu.roll(f, m, 1)
            patch = pltpu.roll(lo, m, 1)
            first = jnp.where(lane < m, patch, r[:, :edge])
            out = jnp.concatenate([first, r[:, edge:]], axis=1)
        cache[k] = out
        return out
    return s


def stencil_kernel(sc_ref, sd_ref, su_ref, ec_ref, ed_ref, eu_ref, xl_ref, xh_ref, yl_ref, yh_ref, out_ref):
    level = pl.program_id(0)
    levels = pl.num_programs(0)
    fields = sc_ref.shape[0]
    width = (xl_ref.shape[1] - 1) // fields
    e = ec_ref[0]
    ed = ed_ref[0]
    eu = eu_ref[0]
    up_w = jnp.where(level < levels - 1, 1.0, 0.0)
    down_w = jnp.where(level > 0, 1.0, 0.0)
    eddy_up = (0.5 * (e + eu)) * up_w
    eddy_down = (0.5 * (ed + e)) * down_w
    ex = _x_shifter(e, [xl_ref[0, pl.ds(fields * width, 1), :]], [xh_ref[0, pl.ds(fields * width, 1), :]])
    ey = _y_shifter(e, yl_ref[fields, 0], yh_ref[fields, 0])
    east = 0.5 * (e + ex(1))
    west = 0.5 * (ex(-1) + e)
    north = 0.5 * (e + ey(1))
    south = 0.5 * (ey(-1) + e)
    u = sc_ref[0, 0]
    v = sc_ref[1, 0]
    w = sc_ref[2, 0]
    for f in range(fields):
        fv = sc_ref[f, 0]
        lower = sd_ref[f, 0]
        upper = su_ref[f, 0]
        sx = _x_shifter(fv, [xl_ref[0, pl.ds(f * width + i, 1), :] for i in range(width)],
                        [xh_ref[0, pl.ds(f * width + i, 1), :] for i in range(width)])
        sy = _y_shifter(fv, yl_ref[f, 0], yh_ref[f, 0])
        derx = _upwind(sx, u)
        dery = _upwind(sy, v)
        derz = (upper - lower) * 0.5
        zdiffuse = eddy_up * (upper - fv) - eddy_down * (fv - lower)
        advect = (u * derx + v * dery) + w * derz
        diff_x = east * (sx(1) - fv) - west * (fv - sx(-1))
        diff_y = north * (sy(1) - fv) - south * (fv - sy(-1))
        diffuse = (diff_x + diff_y) + zdiffuse
        out_ref[f, 0] = diffuse - advect


def stencil(state, eddy, xl, xh, yl, yh):
    fields, levels, cx, cy = state.shape
    w = xl.shape[1]
    nf = yl.shape[0]
    edge = yl.shape[3]
    below = lambda l: jnp.maximum(l - 1, 0)
    above = lambda l: jnp.minimum(l + 1, levels - 1)
    return pl.pallas_call(
        stencil_kernel,
        grid=(levels,),
        in_specs=[
            pl.BlockSpec((fields, 1, cx, cy), lambda l: (0, l, 0, 0)),
            pl.BlockSpec((fields, 1, cx, cy), lambda l: (0, below(l), 0, 0)),
            pl.BlockSpec((fields, 1, cx, cy), lambda l: (0, above(l), 0, 0)),
            pl.BlockSpec((1, cx, cy), lambda l: (l, 0, 0)),
            pl.BlockSpec((1, cx, cy), lambda l: (below(l), 0, 0)),
            pl.BlockSpec((1, cx, cy), lambda l: (above(l), 0, 0)),
            pl.BlockSpec((1, w, cy), lambda l: (l, 0, 0)),
            pl.BlockSpec((1, w, cy), lambda l: (l, 0, 0)),
            pl.BlockSpec((nf, 1, cx, edge), lambda l: (0, l, 0, 0)),
            pl.BlockSpec((nf, 1, cx, edge), lambda l: (0, l, 0, 0)),
        ],
        out_specs=pl.BlockSpec((fields, 1, cx, cy), lambda l: (0, l, 0, 0)),
        out_shape=jax.ShapeDtypeStruct((fields, levels, cx, cy), jnp.float32),
        compiler_params=pltpu.CompilerParams(dimension_semantics=("arbitrary",)),
        cost_estimate=pl.CostEstimate(flops=200 * fields * levels * cx * cy, transcendentals=0,
                                      bytes_accessed=4 * (4 * nf + fields) * levels * cx * cy),
    )(state, state, state, eddy, eddy, eddy, xl, xh, yl, yh)


def _pieces(x, n):
    out = []
    rest = x
    for _ in range(n):
        p = rest.astype(jnp.bfloat16)
        out.append(p)
        rest = rest - p.astype(jnp.float32)
    return out


def _one_hot(cell, cols, iota):
    sub = iota.shape[0]
    col = cell % cols
    hi = col // sub
    lo = (col % sub).astype(jnp.float32)
    hots = []
    for a in range(cols // sub):
        sel = jnp.where(hi == a, lo, -1.0).astype(jnp.bfloat16)
        hots.append(jnp.where(iota == sel, jnp.bfloat16(1), jnp.bfloat16(0)))
    return jnp.concatenate(hots, axis=0)


def gather_kernel(x_ref, pay_ref, flux_ref, iota_ref):
    rows, cols = x_ref.shape
    fields = 4
    per_field = rows // fields
    block = pay_ref.shape[1]

    rows = rows // 2
    per_field = rows // fields

    @pl.when(pl.program_id(0) == 0)
    def _():
        iota_ref[...] = lax.broadcasted_iota(jnp.int32, iota_ref.shape, 0).astype(jnp.bfloat16)

    pay = pay_ref[...]
    cell = (pay[6:7] + 0.5).astype(jnp.int32)
    row = cell // cols
    hot = _one_hot(cell, cols, iota_ref[...])
    picked = jnp.dot(x_ref[...], hot, preferred_element_type=jnp.float32)
    value = picked[0:rows] + picked[rows:2 * rows]
    pick_row = lax.broadcasted_iota(jnp.int32, (per_field, block), 0) == row
    gathered = jnp.concatenate(
        [jnp.sum(jnp.where(pick_row, value[f * per_field:(f + 1) * per_field], 0.0), axis=0, keepdims=True)
         for f in range(fields)], axis=0)
    flux_ref[...] = pay[5:6] * (gathered - pay[0:4]) / pay[4:5]


def scatter_kernel(pay_ref, flux_ref, forcing_ref, iota_ref):
    rows, cols = forcing_ref.shape
    fields = 4
    per_field = rows // fields
    block = pay_ref.shape[1]

    @pl.when(pl.program_id(0) == 0)
    def _():
        forcing_ref[...] = jnp.zeros_like(forcing_ref)
        iota_ref[...] = lax.broadcasted_iota(jnp.int32, iota_ref.shape, 0).astype(jnp.bfloat16)

    pay = pay_ref[...]
    cell = (pay[6:7] + 0.5).astype(jnp.int32)
    row = cell // cols
    hot = _one_hot(cell, cols, iota_ref[...])
    flux = flux_ref[...]
    pick_row = lax.broadcasted_iota(jnp.int32, (per_field, block), 0) == row
    spread = jnp.concatenate(
        [jnp.where(pick_row, flux[f:f + 1], 0.0) for f in range(fields)], axis=0)
    w = jnp.concatenate(_pieces(spread, 2), axis=0)
    added = lax.dot_general(w, hot, (((1,), (1,)), ((), ())), preferred_element_type=jnp.float32)
    forcing_ref[...] += added[0:rows] + added[rows:2 * rows]


def owner_gather(x, pay, block=2048):
    rows, cols = x.shape
    slots = pay.shape[1]
    return pl.pallas_call(
        gather_kernel,
        grid=(slots // block,),
        in_specs=[
            pl.BlockSpec((rows, cols), lambda j: (0, 0)),
            pl.BlockSpec((8, block), lambda j: (0, j)),
        ],
        out_specs=pl.BlockSpec((4, block), lambda j: (0, j)),
        out_shape=jax.ShapeDtypeStruct((4, slots), jnp.float32),
        scratch_shapes=[pltpu.VMEM((256, block), jnp.bfloat16)],
        compiler_params=pltpu.CompilerParams(dimension_semantics=("arbitrary",),
                                             vmem_limit_bytes=48 * 1024 * 1024),
        cost_estimate=pl.CostEstimate(flops=2 * rows * cols * slots, transcendentals=0,
                                      bytes_accessed=2 * rows * cols + 48 * slots),
    )(x, pay)


def split_kernel(x_ref, out_ref):
    rows = x_ref.shape[0]
    parts = _pieces(x_ref[...], 2)
    for i, p in enumerate(parts):
        out_ref[i * rows:(i + 1) * rows, :] = p


def split_pieces(x):
    rows, cols = x.shape
    return pl.pallas_call(
        split_kernel,
        out_shape=jax.ShapeDtypeStruct((2 * rows, cols), jnp.bfloat16),
        cost_estimate=pl.CostEstimate(flops=4 * rows * cols, transcendentals=0, bytes_accessed=8 * rows * cols),
    )(x)


def owner_scatter(pay, flux, rows, cols, block=1024):
    slots = pay.shape[1]
    return pl.pallas_call(
        scatter_kernel,
        grid=(slots // block,),
        in_specs=[
            pl.BlockSpec((8, block), lambda j: (0, j)),
            pl.BlockSpec((4, block), lambda j: (0, j)),
        ],
        out_specs=pl.BlockSpec((rows, cols), lambda j: (0, 0)),
        out_shape=jax.ShapeDtypeStruct((rows, cols), jnp.float32),
        scratch_shapes=[pltpu.VMEM((256, block), jnp.bfloat16)],
        compiler_params=pltpu.CompilerParams(dimension_semantics=("arbitrary",),
                                             vmem_limit_bytes=48 * 1024 * 1024),
        cost_estimate=pl.CostEstimate(flops=rows * cols, transcendentals=0, bytes_accessed=4 * rows * cols),
    )(pay, flux)


def shift_pair(last, leading, axis):
    peers = lax.axis_size(axis)
    up = [(i, (i + 1) % peers) for i in range(peers)]
    down = [(j, i) for i, j in up]
    return lax.ppermute(last, axis, up), lax.ppermute(leading, axis, down)


def exchange(shard, axis, dim, low, high):
    peers = lax.axis_size(axis)
    length = shard.shape[dim]
    up = [(i, (i + 1) % peers) for i in range(peers)]
    down = [(j, i) for i, j in up]
    last = lax.slice_in_dim(shard, length - low, length, axis=dim)
    leading = lax.slice_in_dim(shard, 0, high, axis=dim)
    before = lax.ppermute(last, axis, up)
    after = lax.ppermute(leading, axis, down)
    return before, after


def local(state, start, eddy, solid, facet_wall, facet_dist, facet_area, facet_owner, facet_cell):
    levels = state.shape[1]
    cells_x = state.shape[2]
    cells_y = state.shape[3]
    width = 3
    edge = 128

    def x_rows(lo, hi):
        rows = jnp.transpose(state[:, :, lo:hi], (1, 0, 2, 3)).reshape(levels, -1, cells_y)
        return jnp.concatenate([rows, eddy[:, lo:hi][:, -1:] if lo else eddy[:, 0:1]], axis=1)

    x_last, x_first = x_rows(cells_x - width, cells_x), x_rows(0, width)
    x_low, x_high = shift_pair(x_last, x_first, "gx")
    _, _, y_state, y_eddy = lax.optimization_barrier((x_last, x_first, state, eddy))

    def y_cols(lo, hi, one):
        return jnp.concatenate([y_state[..., lo:hi].reshape(-1), y_eddy[..., one:one + 1].reshape(-1)])

    def y_tile(flat, lanes, one):
        fields_part = flat[: 4 * levels * cells_x * width].reshape(4, levels, cells_x, width)
        eddy_part = flat[4 * levels * cells_x * width:].reshape(1, levels, cells_x, 1)
        pad_f = ((0, 0), (0, 0), (0, 0), (lanes, edge - width - lanes))
        pad_e = ((0, 0), (0, 0), (0, 0), (one, edge - 1 - one))
        return jnp.concatenate([jnp.pad(fields_part, pad_f), jnp.pad(eddy_part, pad_e)], axis=0)

    y_last, y_first = y_cols(cells_y - width, cells_y, cells_y - 1), y_cols(0, width, 0)
    y_low, y_high = shift_pair(y_last, y_first, "gy")
    _, _, facet_wall, facet_dist, facet_area, facet_owner, facet_cell = lax.optimization_barrier(
        (y_last, y_first, facet_wall, facet_dist, facet_area, facet_owner, facet_cell)
    )
    y_low = y_tile(y_low, edge - width, edge - 1)
    y_high = y_tile(y_high, 0, 0)

    facet_count = facet_cell.shape[0]
    owners_gx = lax.axis_size("gx")
    capacity = 2 * facet_count // owners_gx
    slots = owners_gx * capacity
    owner_gx = facet_owner[:, 0]
    owner_hot = (owner_gx[:, None] == jnp.arange(owners_gx, dtype=jnp.int32)[None, :]).astype(
        jnp.bfloat16
    )
    positions = jnp.arange(facet_count, dtype=jnp.int32)
    earlier = (positions[:, None] > positions[None, :]).astype(jnp.bfloat16)
    before = jnp.dot(earlier, owner_hot, preferred_element_type=jnp.float32)
    owner_float = owner_hot.astype(jnp.float32)
    slot_rank = jnp.sum(before * owner_float, axis=1)
    rank_hot = (slot_rank[:, None] == jnp.arange(capacity, dtype=jnp.float32)[None, :]).astype(
        jnp.float32
    )
    payload = jnp.concatenate(
        [facet_wall, facet_dist[None], facet_area[None], facet_cell[None].astype(jnp.float32)],
        axis=0,
    )
    spread = payload[:, None, :] * owner_float.T[None]
    outgoing = jnp.einsum("cof,fk->cok", spread, rank_hot, precision=exact)
    filled = jnp.dot(owner_float.T, rank_hot, precision=exact)
    unit_dist = (jnp.arange(7, dtype=jnp.int32) == 4).astype(jnp.float32)[:, None, None]
    outgoing = outgoing + unit_dist * (1.0 - filled)[None]
    outgoing = jnp.concatenate([outgoing, jnp.zeros((1, owners_gx, capacity), jnp.float32)], axis=0)
    outgoing = jnp.transpose(outgoing, (1, 0, 2)).reshape(owners_gx, -1)
    x_low, x_high, y_low, y_high, outgoing = lax.optimization_barrier(
        (x_low, x_high, y_low, y_high, outgoing)
    )
    received = lax.all_to_all(outgoing, "gx", 0, 0, tiled=True)
    tend = stencil(state, eddy, x_low, x_high, y_low, y_high)
    state_pieces = split_pieces(state.reshape(4 * levels * cells_x, cells_y))
    tend, state_pieces, received = lax.optimization_barrier((tend, state_pieces, received))
    pay = jnp.transpose(received.reshape(owners_gx, 8, capacity), (1, 0, 2)).reshape(8, slots)
    flux_slots = owner_gather(state_pieces, pay)
    wall_flux = jnp.transpose(flux_slots.reshape(4, owners_gx, capacity), (1, 0, 2)).reshape(owners_gx, -1)
    wall_flux, pay, flux_slots = lax.optimization_barrier((wall_flux, pay, flux_slots))
    forcing = owner_scatter(pay, flux_slots, 4 * levels * cells_x, cells_y).reshape(state.shape)
    returned = lax.all_to_all(wall_flux, "gx", 0, 0, tiled=True)
    change = (tend - forcing) * (1.0 - solid.astype(jnp.float32))
    new_state = start + dt_step * change
    new_state, returned = lax.optimization_barrier((new_state, returned))
    returned = jnp.transpose(returned.reshape(owners_gx, 4, capacity), (1, 0, 2))
    through = jnp.einsum("cok,fk->cof", returned, rank_hot, precision=exact)
    facet_flux = jnp.sum(through * owner_float.T[None], axis=1)
    return (new_state, facet_flux)


def solution(mesh):
    in_specs = (
        P(None, None, "gx", "gy"),
        P(None, None, "gx", "gy"),
        P(None, "gx", "gy"),
        P(None, "gx", "gy"),
        P(None, ("gx", "gy")),
        P(("gx", "gy")),
        P(("gx", "gy")),
        P(("gx", "gy"), None),
        P(("gx", "gy")),
    )
    out_specs = (P(None, None, "gx", "gy"), P(None, ("gx", "gy")))
    return jax.shard_map(local, mesh=mesh, in_specs=in_specs, out_specs=out_specs, check_vma=False)
```

```python
import math

import jax
import jax.numpy as jnp
from jax import lax
from jax.experimental import pallas as pl
from jax.experimental.pallas import tpu as pltpu
from jax.sharding import PartitionSpec as P

dt_step = 0.2
exact = lax.Precision.HIGHEST


def _upwind(s, c):
    forward = (((((-2.0 * s(-3) + 15.0 * s(-2)) - 60.0 * s(-1)) + 20.0 * s(0)) + 30.0 * s(1)) - 3.0 * s(2))
    backward = (((((3.0 * s(-2) - 30.0 * s(-1)) - 20.0 * s(0)) + 60.0 * s(1)) - 15.0 * s(2)) + 2.0 * s(3))
    return jnp.where(c > 0, forward, backward) / 60.0


def _x_shifter(f, lo_rows, hi_rows):
    rows = f.shape[0]
    row = lax.broadcasted_iota(jnp.int32, f.shape, 0)
    width = len(lo_rows)
    lo_b = [jnp.broadcast_to(r, f.shape) for r in lo_rows]
    hi_b = [jnp.broadcast_to(r, f.shape) for r in hi_rows]
    cache = {0: f}

    def s(k):
        if k in cache:
            return cache[k]
        if k > 0:
            r = pltpu.roll(f, rows - k, 0)
            patch = hi_b[k - 1]
            for i in range(k - 2, -1, -1):
                patch = jnp.where(row == rows - k + i, hi_b[i], patch)
            out = jnp.where(row < rows - k, r, patch)
        else:
            m = -k
            r = pltpu.roll(f, m, 0)
            patch = lo_b[width - 1]
            for i in range(m - 1):
                patch = jnp.where(row == i, lo_b[width - m + i], patch)
            out = jnp.where(row >= m, r, patch)
        cache[k] = out
        return out
    return s


def _y_shifter(f, lo, hi):
    cols = f.shape[1]
    edge = lo.shape[1]
    lane = lax.broadcasted_iota(jnp.int32, lo.shape, 1)
    cache = {0: f}

    def s(k):
        if k in cache:
            return cache[k]
        if k > 0:
            r = pltpu.roll(f, cols - k, 1)
            patch = pltpu.roll(hi, edge - k, 1)
            last = jnp.where(lane >= edge - k, patch, r[:, cols - edge:])
            out = jnp.concatenate([r[:, :cols - edge], last], axis=1)
        else:
            m = -k
            r = pltpu.roll(f, m, 1)
            patch = pltpu.roll(lo, m, 1)
            first = jnp.where(lane < m, patch, r[:, :edge])
            out = jnp.concatenate([first, r[:, edge:]], axis=1)
        cache[k] = out
        return out
    return s


def stencil_kernel(sc_ref, sd_ref, su_ref, ec_ref, ed_ref, eu_ref, xl_ref, xh_ref, yl_ref, yh_ref, out_ref):
    level = pl.program_id(0)
    levels = pl.num_programs(0)
    fields = sc_ref.shape[0]
    width = (xl_ref.shape[1] - 1) // fields
    e = ec_ref[0]
    ed = ed_ref[0]
    eu = eu_ref[0]
    up_w = jnp.where(level < levels - 1, 1.0, 0.0)
    down_w = jnp.where(level > 0, 1.0, 0.0)
    eddy_up = (0.5 * (e + eu)) * up_w
    eddy_down = (0.5 * (ed + e)) * down_w
    ex = _x_shifter(e, [xl_ref[0, pl.ds(fields * width, 1), :]], [xh_ref[0, pl.ds(fields * width, 1), :]])
    ey = _y_shifter(e, yl_ref[fields, 0], yh_ref[fields, 0])
    east = 0.5 * (e + ex(1))
    west = 0.5 * (ex(-1) + e)
    north = 0.5 * (e + ey(1))
    south = 0.5 * (ey(-1) + e)
    u = sc_ref[0, 0]
    v = sc_ref[1, 0]
    w = sc_ref[2, 0]
    for f in range(fields):
        fv = sc_ref[f, 0]
        lower = sd_ref[f, 0]
        upper = su_ref[f, 0]
        sx = _x_shifter(fv, [xl_ref[0, pl.ds(f * width + i, 1), :] for i in range(width)],
                        [xh_ref[0, pl.ds(f * width + i, 1), :] for i in range(width)])
        sy = _y_shifter(fv, yl_ref[f, 0], yh_ref[f, 0])
        derx = _upwind(sx, u)
        dery = _upwind(sy, v)
        derz = (upper - lower) * 0.5
        zdiffuse = eddy_up * (upper - fv) - eddy_down * (fv - lower)
        advect = (u * derx + v * dery) + w * derz
        diff_x = east * (sx(1) - fv) - west * (fv - sx(-1))
        diff_y = north * (sy(1) - fv) - south * (fv - sy(-1))
        diffuse = (diff_x + diff_y) + zdiffuse
        out_ref[f, 0] = diffuse - advect


def stencil(state, eddy, xl, xh, yl, yh):
    fields, levels, cx, cy = state.shape
    w = xl.shape[1]
    nf = yl.shape[0]
    edge = yl.shape[3]
    below = lambda l: jnp.maximum(l - 1, 0)
    above = lambda l: jnp.minimum(l + 1, levels - 1)
    return pl.pallas_call(
        stencil_kernel,
        grid=(levels,),
        in_specs=[
            pl.BlockSpec((fields, 1, cx, cy), lambda l: (0, l, 0, 0)),
            pl.BlockSpec((fields, 1, cx, cy), lambda l: (0, below(l), 0, 0)),
            pl.BlockSpec((fields, 1, cx, cy), lambda l: (0, above(l), 0, 0)),
            pl.BlockSpec((1, cx, cy), lambda l: (l, 0, 0)),
            pl.BlockSpec((1, cx, cy), lambda l: (below(l), 0, 0)),
            pl.BlockSpec((1, cx, cy), lambda l: (above(l), 0, 0)),
            pl.BlockSpec((1, w, cy), lambda l: (l, 0, 0)),
            pl.BlockSpec((1, w, cy), lambda l: (l, 0, 0)),
            pl.BlockSpec((nf, 1, cx, edge), lambda l: (0, l, 0, 0)),
            pl.BlockSpec((nf, 1, cx, edge), lambda l: (0, l, 0, 0)),
        ],
        out_specs=pl.BlockSpec((fields, 1, cx, cy), lambda l: (0, l, 0, 0)),
        out_shape=jax.ShapeDtypeStruct((fields, levels, cx, cy), jnp.float32),
        compiler_params=pltpu.CompilerParams(dimension_semantics=("arbitrary",)),
        cost_estimate=pl.CostEstimate(flops=200 * fields * levels * cx * cy, transcendentals=0,
                                      bytes_accessed=4 * (4 * nf + fields) * levels * cx * cy),
    )(state, state, state, eddy, eddy, eddy, xl, xh, yl, yh)


def _pieces(x, n):
    out = []
    rest = x
    for _ in range(n):
        p = rest.astype(jnp.bfloat16)
        out.append(p)
        rest = rest - p.astype(jnp.float32)
    return out


def _one_hot(cell, cols, iota):
    sub = iota.shape[0]
    col = cell % cols
    hi = col // sub
    lo = (col % sub).astype(jnp.float32)
    hots = []
    for a in range(cols // sub):
        sel = jnp.where(hi == a, lo, -1.0).astype(jnp.bfloat16)
        hots.append(jnp.where(iota == sel, jnp.bfloat16(1), jnp.bfloat16(0)))
    return jnp.concatenate(hots, axis=0)


def gather_kernel(x_ref, pay_ref, flux_ref, iota_ref):
    rows, cols = x_ref.shape
    fields = 4
    per_field = rows // fields
    block = pay_ref.shape[1]

    rows = rows // 2
    per_field = rows // fields

    @pl.when(pl.program_id(0) == 0)
    def _():
        iota_ref[...] = lax.broadcasted_iota(jnp.int32, iota_ref.shape, 0).astype(jnp.bfloat16)

    pay = pay_ref[...]
    cell = (pay[6:7] + 0.5).astype(jnp.int32)
    row = cell // cols
    hot = _one_hot(cell, cols, iota_ref[...])
    picked = jnp.dot(x_ref[...], hot, preferred_element_type=jnp.float32)
    value = picked[0:rows] + picked[rows:2 * rows]
    pick_row = lax.broadcasted_iota(jnp.int32, (per_field, block), 0) == row
    gathered = jnp.concatenate(
        [jnp.sum(jnp.where(pick_row, value[f * per_field:(f + 1) * per_field], 0.0), axis=0, keepdims=True)
         for f in range(fields)], axis=0)
    flux_ref[...] = pay[5:6] * (gathered - pay[0:4]) / pay[4:5]


def scatter_kernel(pay_ref, flux_ref, forcing_ref, iota_ref):
    rows, cols = forcing_ref.shape
    fields = 4
    per_field = rows // fields
    block = pay_ref.shape[1]

    @pl.when(pl.program_id(0) == 0)
    def _():
        forcing_ref[...] = jnp.zeros_like(forcing_ref)
        iota_ref[...] = lax.broadcasted_iota(jnp.int32, iota_ref.shape, 0).astype(jnp.bfloat16)

    pay = pay_ref[...]
    cell = (pay[6:7] + 0.5).astype(jnp.int32)
    row = cell // cols
    hot = _one_hot(cell, cols, iota_ref[...])
    flux = flux_ref[...]
    pick_row = lax.broadcasted_iota(jnp.int32, (per_field, block), 0) == row
    spread = jnp.concatenate(
        [jnp.where(pick_row, flux[f:f + 1], 0.0) for f in range(fields)], axis=0)
    w = jnp.concatenate(_pieces(spread, 2), axis=0)
    added = lax.dot_general(w, hot, (((1,), (1,)), ((), ())), preferred_element_type=jnp.float32)
    forcing_ref[...] += added[0:rows] + added[rows:2 * rows]


def owner_gather(x, pay, block=4096):
    rows, cols = x.shape
    slots = pay.shape[1]
    return pl.pallas_call(
        gather_kernel,
        grid=(slots // block,),
        in_specs=[
            pl.BlockSpec((rows, cols), lambda j: (0, 0)),
            pl.BlockSpec((8, block), lambda j: (0, j)),
        ],
        out_specs=pl.BlockSpec((4, block), lambda j: (0, j)),
        out_shape=jax.ShapeDtypeStruct((4, slots), jnp.float32),
        scratch_shapes=[pltpu.VMEM((256, block), jnp.bfloat16)],
        compiler_params=pltpu.CompilerParams(dimension_semantics=("arbitrary",),
                                             vmem_limit_bytes=48 * 1024 * 1024),
        cost_estimate=pl.CostEstimate(flops=2 * rows * cols * slots, transcendentals=0,
                                      bytes_accessed=2 * rows * cols + 48 * slots),
    )(x, pay)


def split_kernel(x_ref, out_ref):
    rows = x_ref.shape[0]
    parts = _pieces(x_ref[...], 2)
    for i, p in enumerate(parts):
        out_ref[i * rows:(i + 1) * rows, :] = p


def split_pieces(x):
    rows, cols = x.shape
    return pl.pallas_call(
        split_kernel,
        out_shape=jax.ShapeDtypeStruct((2 * rows, cols), jnp.bfloat16),
        cost_estimate=pl.CostEstimate(flops=4 * rows * cols, transcendentals=0, bytes_accessed=8 * rows * cols),
    )(x)


def owner_scatter(pay, flux, rows, cols, block=1024):
    slots = pay.shape[1]
    return pl.pallas_call(
        scatter_kernel,
        grid=(slots // block,),
        in_specs=[
            pl.BlockSpec((8, block), lambda j: (0, j)),
            pl.BlockSpec((4, block), lambda j: (0, j)),
        ],
        out_specs=pl.BlockSpec((rows, cols), lambda j: (0, 0)),
        out_shape=jax.ShapeDtypeStruct((rows, cols), jnp.float32),
        scratch_shapes=[pltpu.VMEM((256, block), jnp.bfloat16)],
        compiler_params=pltpu.CompilerParams(dimension_semantics=("arbitrary",),
                                             vmem_limit_bytes=48 * 1024 * 1024),
        cost_estimate=pl.CostEstimate(flops=rows * cols, transcendentals=0, bytes_accessed=4 * rows * cols),
    )(pay, flux)


def shift_pair(last, leading, axis):
    peers = lax.axis_size(axis)
    up = [(i, (i + 1) % peers) for i in range(peers)]
    down = [(j, i) for i, j in up]
    return lax.ppermute(last, axis, up), lax.ppermute(leading, axis, down)


def exchange(shard, axis, dim, low, high):
    peers = lax.axis_size(axis)
    length = shard.shape[dim]
    up = [(i, (i + 1) % peers) for i in range(peers)]
    down = [(j, i) for i, j in up]
    last = lax.slice_in_dim(shard, length - low, length, axis=dim)
    leading = lax.slice_in_dim(shard, 0, high, axis=dim)
    before = lax.ppermute(last, axis, up)
    after = lax.ppermute(leading, axis, down)
    return before, after


def local(state, start, eddy, solid, facet_wall, facet_dist, facet_area, facet_owner, facet_cell):
    levels = state.shape[1]
    cells_x = state.shape[2]
    cells_y = state.shape[3]
    width = 3
    edge = 128

    def x_rows(lo, hi):
        rows = jnp.transpose(state[:, :, lo:hi], (1, 0, 2, 3)).reshape(levels, -1, cells_y)
        return jnp.concatenate([rows, eddy[:, lo:hi][:, -1:] if lo else eddy[:, 0:1]], axis=1)

    x_last, x_first = x_rows(cells_x - width, cells_x), x_rows(0, width)
    x_low, x_high = shift_pair(x_last, x_first, "gx")
    _, _, y_state, y_eddy = lax.optimization_barrier((x_last, x_first, state, eddy))

    def y_cols(lo, hi, one):
        return jnp.concatenate([y_state[..., lo:hi].reshape(-1), y_eddy[..., one:one + 1].reshape(-1)])

    def y_tile(flat, lanes, one):
        fields_part = flat[: 4 * levels * cells_x * width].reshape(4, levels, cells_x, width)
        eddy_part = flat[4 * levels * cells_x * width:].reshape(1, levels, cells_x, 1)
        pad_f = ((0, 0), (0, 0), (0, 0), (lanes, edge - width - lanes))
        pad_e = ((0, 0), (0, 0), (0, 0), (one, edge - 1 - one))
        return jnp.concatenate([jnp.pad(fields_part, pad_f), jnp.pad(eddy_part, pad_e)], axis=0)

    y_last, y_first = y_cols(cells_y - width, cells_y, cells_y - 1), y_cols(0, width, 0)
    y_low, y_high = shift_pair(y_last, y_first, "gy")
    _, _, facet_wall, facet_dist, facet_area, facet_owner, facet_cell = lax.optimization_barrier(
        (y_last, y_first, facet_wall, facet_dist, facet_area, facet_owner, facet_cell)
    )
    y_low = y_tile(y_low, edge - width, edge - 1)
    y_high = y_tile(y_high, 0, 0)

    facet_count = facet_cell.shape[0]
    owners_gx = lax.axis_size("gx")
    capacity = 2 * facet_count // owners_gx
    slots = owners_gx * capacity
    owner_gx = facet_owner[:, 0]
    owner_hot = (owner_gx[:, None] == jnp.arange(owners_gx, dtype=jnp.int32)[None, :]).astype(
        jnp.bfloat16
    )
    positions = jnp.arange(facet_count, dtype=jnp.int32)
    earlier = (positions[:, None] > positions[None, :]).astype(jnp.bfloat16)
    before = jnp.dot(earlier, owner_hot, preferred_element_type=jnp.float32)
    owner_float = owner_hot.astype(jnp.float32)
    slot_rank = jnp.sum(before * owner_float, axis=1)
    rank_hot = (slot_rank[:, None] == jnp.arange(capacity, dtype=jnp.float32)[None, :]).astype(
        jnp.float32
    )
    payload = jnp.concatenate(
        [facet_wall, facet_dist[None], facet_area[None], facet_cell[None].astype(jnp.float32)],
        axis=0,
    )
    spread = payload[:, None, :] * owner_float.T[None]
    outgoing = jnp.einsum("cof,fk->cok", spread, rank_hot, precision=exact)
    filled = jnp.dot(owner_float.T, rank_hot, precision=exact)
    unit_dist = (jnp.arange(7, dtype=jnp.int32) == 4).astype(jnp.float32)[:, None, None]
    outgoing = outgoing + unit_dist * (1.0 - filled)[None]
    outgoing = jnp.concatenate([outgoing, jnp.zeros((1, owners_gx, capacity), jnp.float32)], axis=0)
    outgoing = jnp.transpose(outgoing, (1, 0, 2)).reshape(owners_gx, -1)
    x_low, x_high, y_low, y_high, outgoing = lax.optimization_barrier(
        (x_low, x_high, y_low, y_high, outgoing)
    )
    received = lax.all_to_all(outgoing, "gx", 0, 0, tiled=True)
    tend = stencil(state, eddy, x_low, x_high, y_low, y_high)
    state_pieces = split_pieces(state.reshape(4 * levels * cells_x, cells_y))
    tend, state_pieces, received = lax.optimization_barrier((tend, state_pieces, received))
    pay = jnp.transpose(received.reshape(owners_gx, 8, capacity), (1, 0, 2)).reshape(8, slots)
    flux_slots = owner_gather(state_pieces, pay)
    wall_flux = jnp.transpose(flux_slots.reshape(4, owners_gx, capacity), (1, 0, 2)).reshape(owners_gx, -1)
    wall_flux, pay, flux_slots = lax.optimization_barrier((wall_flux, pay, flux_slots))
    forcing = owner_scatter(pay, flux_slots, 4 * levels * cells_x, cells_y).reshape(state.shape)
    returned = lax.all_to_all(wall_flux, "gx", 0, 0, tiled=True)
    change = (tend - forcing) * (1.0 - solid.astype(jnp.float32))
    new_state = start + dt_step * change
    new_state, returned = lax.optimization_barrier((new_state, returned))
    returned = jnp.transpose(returned.reshape(owners_gx, 4, capacity), (1, 0, 2))
    through = jnp.einsum("cok,fk->cof", returned, rank_hot, precision=exact)
    facet_flux = jnp.sum(through * owner_float.T[None], axis=1)
    return (new_state, facet_flux)


def solution(mesh):
    in_specs = (
        P(None, None, "gx", "gy"),
        P(None, None, "gx", "gy"),
        P(None, "gx", "gy"),
        P(None, "gx", "gy"),
        P(None, ("gx", "gy")),
        P(("gx", "gy")),
        P(("gx", "gy")),
        P(("gx", "gy"), None),
        P(("gx", "gy")),
    )
    out_specs = (P(None, None, "gx", "gy"), P(None, ("gx", "gy")))
    return jax.shard_map(local, mesh=mesh, in_specs=in_specs, out_specs=out_specs, check_vma=False)
```
